128 devices in a mesh: group: 16 (over z, y), expert: 8 (over x, core).
Axes of the slice: x: 4, y: 4, z: 4, core: 2. Of those that a mesh axis runs over, the one named last changes fastest.
Arguments:
- tokens: bfloat16 [8192, 2048], P(('group', 'expert')), may hold values from -6 to 6
- attention_gain: float32 [2048], replicated, may hold values from 0.1 to 1.9
- query_weight: bfloat16 [2048, 2048], P(None, 'expert')
- key_weight: bfloat16 [2048, 2048], P(None, 'expert')
- value_weight: bfloat16 [2048, 2048], P(None, 'expert'), may hold values from -0.125 to 0.125
- query_gain: float32 [2048], P('expert'), may hold values from 0.1 to 1.9
- key_gain: float32 [2048], P('expert'), may hold values from 0.1 to 1.9
- out_weight: bfloat16 [2048, 2048], P('expert'), may hold values from -0.125 to 0.125
- key_pages: bfloat16 [1024, 128, 2048], P('group', None, 'expert'), may hold values from -720 to 720
- value_pages: bfloat16 [1024, 128, 2048], P('group', None, 'expert'), may hold values from -6 to 6
- page_table: int32 [16, 8, 12], P('group'), may hold values from 0 to 63
- far_table: int32 [16, 12], P('group'), may hold values from 0 to 63
- cached_lengths: int32 [16, 8], P('group'), may hold values from 1 to 1536, 6144 in all within a row
- far_lengths: int32 [16], replicated, may hold values from 1 to 1536, 12288 in all
- visible_from: int32 [16, 8], P('group'), may hold values from 0 to 255
- feedforward_gain: float32 [2048], replicated, may hold values from 0.1 to 1.9
- routes: int32 [8192, 8], P(('group', 'expert')), may hold values from 0 to 63, all different within a row; in each aligned block of 64 rows (0 to 63, 64 to 127, ...) at most 12 rows name the same one
- route_weights: float32 [8192, 8], P(('group', 'expert')), may hold values from 0.05 to 0.5
- gate_weight: bfloat16 [2048, 65536], P(None, ('group', 'expert')), may hold values from -0.125 to 0.125
- up_weight: bfloat16 [2048, 65536], P(None, ('group', 'expert')), may hold values from -0.125 to 0.125
- down_weight: bfloat16 [65536, 2048], P(('group', 'expert')), may hold values from -0.1875 to 0.1875
Outputs:
- layer_out: bfloat16 [8192, 2048], P(('group', 'expert'))
The draws below stay inside these ranges and needn't reach their ends.
Inputs may be any that keep to these rules, and one draw needn't show every extreme that they name: `routes`: each row names 8 different experts; in each aligned block of 64 rows (the rows of one device) no expert is named by more than 12 rows, a bound that some block reaches. `cached_lengths`: in each group the 8 lengths sum to 6144 and the largest is 1536. `far_lengths`: the lengths sum to 12288 and the largest is 1536. `page_table`: pages may repeat within a request and across requests. `far_table`: pages may repeat.
All inputs are finite; a program needn't handle non-finite values.
Results may differ from the reference program's by a relative error of at most 0.015.
The reference program's roundings to bfloat16 on the way count: a program that leaves them out, or rounds other values in their place, can miss the bound.
Values may be sent and summed in bfloat16 or wider, within the bound.
No kernel may reach another device: no remote copies, remote signals or barrier semaphores. Data moves between devices by JAX's collectives and lax.ppermute only.
A program may use at most 128 MiB of HBM per device.

```python
import math
import jax
import jax.numpy as jnp
import numpy as np
from jax import lax

D = 2048
HEADS = 16
HD = 128
EXPERTS = 64
FF = 1024
TOP = 8
PAGE = 128
REQ = 8
SPAN = 64
MAXP = 12
POOL = 64
TOKENS = 8192
TOK_DEV = 64
CAP = 12
N_GROUP = 16
DEVICES = 128


def rising_columns(key):
    base = jnp.clip(jax.random.normal(key, (D, HEADS * HD), jnp.float32), -6.0, 6.0) / math.sqrt(D)
    head_index = (jnp.arange(HEADS * HD) // HD).astype(jnp.float32)
    ramp = 1.0 + 0.8 * head_index / max(HEADS - 1, 1)
    return base * ramp[None, :]


def draw_query_weight(key, part):
    return rising_columns(jax.random.fold_in(key, 11)).astype(jnp.bfloat16)


def draw_key_weight(key, part):
    return rising_columns(jax.random.fold_in(key, 12)).astype(jnp.bfloat16)


def draw_key_pages(key, part):
    shape = (N_GROUP * POOL, PAGE, HEADS * HD)
    base = jnp.clip(jax.random.normal(jax.random.fold_in(key, 21), shape, jnp.float32), -6.0, 6.0)
    return base.astype(jnp.bfloat16)


def with_ends(array, own_key, least, top_value):
    longest = array.shape.index(max(array.shape))
    spots = []
    for shift in (0, 1):
        where = [jax.random.randint(jax.random.fold_in(own_key, axis), (), 0, length) for axis, length in enumerate(array.shape)]
        where[longest] = (where[longest] + shift) % array.shape[longest]
        spots.append(tuple(where))
    return array.at[spots[0]].set(least).at[spots[1]].set(top_value)


def steps_of(rng, shape, cuts, low, largest):
    loudness = 1.0
    for axis_at, blocks in cuts:
        heights = jax.random.uniform(jax.random.fold_in(jax.random.fold_in(rng, 6), axis_at), (blocks,), jnp.float32, low / len(cuts), largest / len(cuts))
        loudness = loudness * jnp.repeat(jnp.exp(heights), shape[axis_at] // blocks).reshape((-1,) + (1,) * (len(shape) - 1 - axis_at))
    return loudness


def profile(amount, total, reach, slope):
    weights = [(1 << 20) // math.isqrt(rank ** slope) + 1 for rank in range(2, amount + 1)]
    spare, holding = total - reach - (amount - 1), [1] * (amount - 1)
    while spare > 0:
        movable = [i for i in range(amount - 1) if holding[i] < reach]
        whole, budget = sum([weights[i] for i in movable]), spare
        for i in movable:
            extra = min(reach - holding[i], max(1, budget * weights[i] // whole), spare)
            holding[i] = holding[i] + extra
            spare = spare - extra
    return np.array([reach] + holding)


def ragged_sizes(key, amount, total, reach, skew):
    if amount == 2:
        one = jax.random.randint(key, (), max(1, total - reach), min(reach, total - 1) + 1)
        return jnp.stack([one, total - one])
    tallies = jnp.asarray(profile(amount, total, reach, skew), jnp.int32)
    couples = (amount - 1) // 2
    source_of, sink = tallies[1:1 + 2 * couples:2], tallies[2:2 + 2 * couples:2]
    margin = jnp.minimum(source_of - 1, reach - sink)
    moved = jax.random.randint(jax.random.fold_in(key, 1), (couples,), 0, 1 << 20) % (margin + 1)
    tallies = tallies.at[1:1 + 2 * couples:2].set(source_of - moved).at[2:2 + 2 * couples:2].set(sink + moved)
    return tallies[jax.random.permutation(jax.random.fold_in(key, 2), amount)]


def deal_out(own_key, own, number, rows, amount, top, reach, lean):
    ranking = jax.random.permutation(own_key, amount)
    heavy_load, usual = portions_of(amount, rows * top, reach, lean, True), portions_of(amount, rows * top, reach, lean, False)
    places = jnp.arange(amount)

    def named(sizes, offset_by):
        used = int((sizes > 0).sum())
        fixed = max(1, used // 4)
        shifted = fixed + (places - fixed + offset_by * (used - fixed)) % max(1, amount - fixed)
        return jnp.zeros((amount,), jnp.int32).at[ranking[jnp.where(places < fixed, places, shifted)]].set(jnp.asarray(sizes, jnp.int32))

    sizes = jnp.where(number % 4 == 0, named(heavy_load, number // 4), named(usual, number - number // 4 - 1))
    mixed = jax.random.permutation(jax.random.fold_in(own, 3), amount)
    donor, sink = mixed[0:amount // 2 * 2:2], mixed[1:amount // 2 * 2:2]
    room = jnp.minimum(sizes[donor] - 1, reach - sizes[sink]) // 2
    room = jnp.where((donor == ranking[0]) | (sink == ranking[0]) | (sizes[sink] == 0), 0, jnp.maximum(room, 0))
    shifted = jax.random.randint(jax.random.fold_in(own, 4), (amount // 2,), 0, 1 << 20) % (room + 1)
    sizes = sizes.at[donor].add(-shifted).at[sink].add(shifted)
    items = jnp.searchsorted(jnp.cumsum(sizes), jnp.arange(rows * top), side="right").astype(jnp.int32)
    table = items.reshape(top, rows).T
    table = table[jax.random.permutation(jax.random.fold_in(own, 1), rows)]
    offset_by = jax.random.randint(jax.random.fold_in(own, 2), (rows, 1), 0, top)
    return jnp.take_along_axis(table, (jnp.arange(top)[None, :] + offset_by) % top, axis=1)


def portions_of(amount, total, most, slope, full):
    loads = [(1 << 20) // math.isqrt(rank ** slope) + 1 for rank in range(1, amount + 1)]
    largest = most if full else min(most, max(-(-total // amount), total * loads[0] // sum(loads)))
    least = 1 if total - largest >= amount - 1 else 0
    counts, rest = [largest] + [least] * (amount - 1), total - largest - least * (amount - 1)
    while rest > 0:
        movable = [i for i in range(1, amount) if counts[i] < largest] or [i for i in range(1, amount) if counts[i] < most]
        mass, budget = sum([loads[i] for i in movable]), rest
        for i in movable:
            more = min(most - counts[i], max(1, budget * loads[i] // mass), rest)
            counts[i] = counts[i] + more
            rest = rest - more
    return np.array(counts)


def bell_draw(key, extent, spread, limit, cuts=(), held_as=jnp.bfloat16):
    gain = steps_of(key, extent, cuts, -0.22, 0.18) if cuts else 1.0
    entries = jax.random.normal(key, extent, jnp.float32) * spread * gain
    return jnp.minimum(jnp.maximum(entries, -limit), limit).astype(held_as)


def setup_inputs(seed: int = 0) -> dict:
    seeds = jax.random.split(jax.random.key(seed), 22)
    tokens = bell_draw(seeds[0], (TOKENS, D), 1.0, 6.0, ((0, 128),))
    attention_gain = jnp.clip(1.0 + 0.18 * jax.random.normal(seeds[1], (D,), jnp.float32), 0.1, 1.9)
    query_weight = draw_query_weight(jax.random.fold_in(seeds[21], 71), 0)
    key_weight = draw_key_weight(jax.random.fold_in(seeds[21], 71), 0)
    value_weight = bell_draw(seeds[4], (D, HEADS * HD), D ** -0.5, 0.125, ((1, 8),))
    query_gain = jnp.clip(1.0 + 0.18 * jax.random.normal(seeds[5], (HEADS * HD,), jnp.float32), 0.1, 1.9)
    key_gain = jnp.clip(1.0 + 0.18 * jax.random.normal(seeds[6], (HEADS * HD,), jnp.float32), 0.1, 1.9)
    out_weight = bell_draw(seeds[7], (HEADS * HD, D), (HEADS * HD) ** -0.5, 0.125, ((0, 8),))
    key_pages = draw_key_pages(jax.random.fold_in(seeds[21], 71), 0)
    value_pages = bell_draw(seeds[9], (N_GROUP * POOL, PAGE, HEADS * HD), 1.0, 6.0, ((0, 16), (2, 8)))
    page_table = with_ends(jax.random.randint(seeds[10], (N_GROUP, REQ, MAXP), 0, POOL), jax.random.fold_in(seeds[10], 1), 0, POOL - 1).astype(jnp.int32)
    far_table = with_ends(jax.random.randint(seeds[11], (N_GROUP, MAXP), 0, POOL), jax.random.fold_in(seeds[11], 1), 0, POOL - 1).astype(jnp.int32)
    cached_lengths = jax.vmap(lambda own: ragged_sizes(own, REQ, REQ * MAXP * PAGE // 2, MAXP * PAGE, 2))(jax.random.split(seeds[12], N_GROUP)).reshape((N_GROUP, REQ)).astype(jnp.int32)
    far_lengths = ragged_sizes(seeds[13], N_GROUP, N_GROUP * MAXP * PAGE // 2, MAXP * PAGE, 2).astype(jnp.int32)
    visible_from = with_ends(jax.random.randint(seeds[14], (N_GROUP, REQ), 0, 2 * PAGE), jax.random.fold_in(seeds[14], 1), 0, (2 * PAGE) - 1).astype(jnp.int32)
    feedforward_gain = jnp.clip(1.0 + 0.18 * jax.random.normal(seeds[15], (D,), jnp.float32), 0.1, 1.9)
    routes_keys = jax.random.split(jax.random.fold_in(seeds[16], 1), TOKENS // TOK_DEV)
    routes_turns = jax.random.permutation(jax.random.fold_in(seeds[16], 3), TOKENS // TOK_DEV)
    routes = jax.vmap(lambda own, number: deal_out(jax.random.fold_in(seeds[16], 2), own, number, TOK_DEV, EXPERTS, TOP, CAP, 2))(routes_keys, routes_turns).reshape((TOKENS, TOP))
    route_weights = jnp.clip(jnp.exp(math.log(0.5) - 2.3025851 * jax.random.uniform(seeds[17], (TOKENS, TOP), jnp.float32) ** steps_of(seeds[17], (TOKENS, TOP), ((0, 128),), -0.2, 0.2)), 0.05, 0.5)
    gate_weight = bell_draw(seeds[18], (D, EXPERTS * FF), D ** -0.5, 0.125, ((1, 128),))
    up_weight = bell_draw(seeds[19], (D, EXPERTS * FF), D ** -0.5, 0.125, ((1, 128),))
    down_weight = bell_draw(seeds[20], (EXPERTS * FF, D), FF ** -0.5, 0.1875, ((0, 128),))
    return dict(tokens=tokens, attention_gain=attention_gain, query_weight=query_weight, key_weight=key_weight, value_weight=value_weight, query_gain=query_gain, key_gain=key_gain, out_weight=out_weight, key_pages=key_pages, value_pages=value_pages, page_table=page_table, far_table=far_table, cached_lengths=cached_lengths, far_lengths=far_lengths, visible_from=visible_from, feedforward_gain=feedforward_gain, routes=routes, route_weights=route_weights, gate_weight=gate_weight, up_weight=up_weight, down_weight=down_weight)


EPSILON = 1e-05
MASKED = -1e+30

def rms_norm(values, norm_gain):
    return values * lax.rsqrt(lax.optimization_barrier(jnp.mean(values * values, axis=-1, keepdims=True)) + EPSILON) * norm_gain

def rotate(values, position):
    half_width = values.shape[-1] // 2
    inverse_freq = 10000.0 ** (-2.0 * jnp.arange(half_width, dtype=jnp.float32) / values.shape[-1])
    angles = position[:, None] * inverse_freq[None, :]
    cosine = jnp.cos(angles)[:, None, :]
    sine_part = jnp.sin(angles)[:, None, :]
    first_part = values[..., :half_width]
    second = values[..., half_width:]
    return jnp.concatenate([first_part * cosine - second * sine_part, second * cosine + first_part * sine_part], axis=-1)

def attend(queries, key_rows, value_rows, allowed):
    scores = jnp.einsum('chd,lhd->hcl', queries.astype(jnp.float32), key_rows.astype(jnp.float32)) / math.sqrt(HD)
    scores = jnp.where(allowed[None], scores, MASKED)
    row_max = lax.optimization_barrier(jnp.max(scores, axis=-1, keepdims=True))
    raised = jnp.where(allowed[None], jnp.exp(scores - row_max), 0.0)
    weights = (raised / lax.optimization_barrier(jnp.sum(raised, axis=-1, keepdims=True))).astype(jnp.bfloat16)
    context = jnp.einsum('hcl,lhd->chd', weights.astype(jnp.float32), value_rows.astype(jnp.float32))
    return context.astype(jnp.bfloat16)

def reference(tokens, attention_gain, query_weight, key_weight, value_weight, query_gain, key_gain, out_weight, key_pages, value_pages, page_table, far_table, cached_lengths, far_lengths, visible_from, feedforward_gain, routes, route_weights, gate_weight, up_weight, down_weight):
    as_float = tokens.astype(jnp.float32)
    normed = rms_norm(as_float, attention_gain).astype(jnp.bfloat16)
    query_raw = rms_norm(jnp.dot(normed, query_weight, preferred_element_type=jnp.float32), query_gain)
    key_raw = rms_norm(jnp.dot(normed, key_weight, preferred_element_type=jnp.float32), key_gain)
    new_values = jnp.dot(normed, value_weight, preferred_element_type=jnp.float32).astype(jnp.bfloat16).reshape(TOKENS, HEADS, HD)
    first_flag = (jnp.arange(REQ, dtype=jnp.int32) == 0).astype(jnp.int32)
    offsets = cached_lengths + far_lengths[:, None] * first_flag[None, :]
    position = (offsets[:, :, None] + jnp.arange(SPAN, dtype=jnp.int32)[None, None, :]).reshape(TOKENS).astype(jnp.float32)
    queries = rotate(query_raw.reshape(TOKENS, HEADS, HD), position).astype(jnp.bfloat16)
    new_keys = rotate(key_raw.reshape(TOKENS, HEADS, HD), position).astype(jnp.bfloat16)
    key_grid = key_pages.reshape(N_GROUP, POOL, PAGE, HEADS, HD)
    value_grid = value_pages.reshape(N_GROUP, POOL, PAGE, HEADS, HD)
    cache_slots = MAXP * PAGE
    cache_pos = jnp.arange(cache_slots, dtype=jnp.int32)
    causal = jnp.arange(SPAN)[:, None] >= jnp.arange(SPAN)[None, :]
    group_rows = REQ * SPAN

    def one_group(group_id):
        group_q = lax.dynamic_slice_in_dim(queries, group_id * group_rows, group_rows).reshape(REQ, SPAN, HEADS, HD)
        group_k = lax.dynamic_slice_in_dim(new_keys, group_id * group_rows, group_rows).reshape(REQ, SPAN, HEADS, HD)
        group_v = lax.dynamic_slice_in_dim(new_values, group_id * group_rows, group_rows).reshape(REQ, SPAN, HEADS, HD)
        own_keys = key_grid[group_id][page_table[group_id]].reshape(REQ, cache_slots, HEADS, HD)
        own_values = value_grid[group_id][page_table[group_id]].reshape(REQ, cache_slots, HEADS, HD)

        def own_allowed(request):
            visible = (cache_pos < cached_lengths[group_id, request]) & (cache_pos >= visible_from[group_id, request])
            return jnp.concatenate([jnp.broadcast_to(visible[None], (SPAN, cache_slots)), causal], axis=1)

        def one_request(request):
            key_rows = jnp.concatenate([own_keys[request], group_k[request]], axis=0)
            value_rows = jnp.concatenate([own_values[request], group_v[request]], axis=0)
            return attend(group_q[request], key_rows, value_rows, own_allowed(request))
        outputs = lax.map(one_request, jnp.arange(1, REQ, dtype=jnp.int32))
        partner = jnp.bitwise_xor(group_id, 1)
        far_keys = key_grid[partner][far_table[partner]].reshape(cache_slots, HEADS, HD)
        far_values = value_grid[partner][far_table[partner]].reshape(cache_slots, HEADS, HD)
        far_visible = jnp.broadcast_to((cache_pos < far_lengths[group_id])[None], (SPAN, cache_slots))
        allowed = jnp.concatenate([own_allowed(0), far_visible], axis=1)
        key_rows = jnp.concatenate([own_keys[0], group_k[0], far_keys], axis=0)
        value_rows = jnp.concatenate([own_values[0], group_v[0], far_values], axis=0)
        first_out = attend(group_q[0], key_rows, value_rows, allowed)
        return jnp.concatenate([first_out[None], outputs], axis=0).reshape(group_rows, HEADS * HD)
    context = lax.map(one_group, jnp.arange(N_GROUP, dtype=jnp.int32)).reshape(TOKENS, HEADS * HD)
    residual = (as_float + jnp.dot(context, out_weight, preferred_element_type=jnp.float32)).astype(jnp.bfloat16)
    moe_in = rms_norm(residual.astype(jnp.float32), feedforward_gain).astype(jnp.bfloat16)
    flat_routes = routes.reshape(DEVICES, TOK_DEV * TOP)
    onehot = (flat_routes[:, :, None] == jnp.arange(EXPERTS, dtype=jnp.int32)[None, None, :]).astype(jnp.int32)
    earlier = jnp.cumsum(onehot, axis=1) - onehot
    slot_index = lax.optimization_barrier(jnp.sum(earlier * onehot, axis=2))
    block_id = jnp.arange(DEVICES, dtype=jnp.int32)[:, None]
    flat_index = ((block_id * EXPERTS + flat_routes) * CAP + slot_index).reshape(-1)
    token_ids = jnp.repeat(jnp.arange(TOKENS, dtype=jnp.int32), TOP)
    table = jnp.full((DEVICES * EXPERTS * CAP,), TOKENS, dtype=jnp.int32).at[flat_index].set(token_ids).reshape(DEVICES, EXPERTS, CAP)
    weight_table = jnp.zeros((DEVICES * EXPERTS * CAP,), jnp.float32).at[flat_index].set(route_weights.reshape(-1)).reshape(DEVICES, EXPERTS, CAP)
    padded = jnp.concatenate([moe_in, jnp.zeros((1, D), jnp.bfloat16)], axis=0)

    def expert_step(accum, expert):
        picked = lax.dynamic_index_in_dim(table, expert, axis=1, keepdims=False).reshape(-1)
        scale_rows = lax.dynamic_index_in_dim(weight_table, expert, axis=1, keepdims=False).reshape(-1)
        rows_in = padded[picked]
        begin = expert * FF
        gate_act = jnp.dot(rows_in, lax.dynamic_slice_in_dim(gate_weight, begin, FF, 1), preferred_element_type=jnp.float32)
        up_act = jnp.dot(rows_in, lax.dynamic_slice_in_dim(up_weight, begin, FF, 1), preferred_element_type=jnp.float32)
        hidden = (jax.nn.silu(gate_act) * up_act).astype(jnp.bfloat16)
        expert_out = jnp.dot(hidden, lax.dynamic_slice_in_dim(down_weight, begin, FF, 0), preferred_element_type=jnp.float32).astype(jnp.bfloat16)
        summed = lax.optimization_barrier(expert_out).astype(jnp.float32)
        return (accum.at[picked].add(scale_rows[:, None] * summed), None)
    accum, _ = lax.scan(expert_step, jnp.zeros((TOKENS + 1, D), jnp.float32), jnp.arange(EXPERTS, dtype=jnp.int32))
    return (residual.astype(jnp.float32) + accum[:TOKENS]).astype(jnp.bfloat16)
```

```python
import math

import jax
import jax.numpy as jnp
from jax import lax
from jax.sharding import PartitionSpec as P

D = 2048
HD = 128
EXPERTS = 64
TOP = 8
PAGE = 128
REQ = 8
SPAN = 64
MAXP = 12


EPSILON = 1e-05
MASKED = -1e30
HEAD_AXES = ("x", "core")


def from_partner(value, axis, bit):
    mask = 2**bit
    pairs = [(source, source ^ mask) for source in range(lax.axis_size(axis))]
    return lax.ppermute(value, axis, pairs)


def rms_norm(values, norm_gain):
    return (
        values * lax.rsqrt(jnp.mean(values * values, axis=-1, keepdims=True) + EPSILON) * norm_gain
    )


def rotate(values, position):
    half_width = values.shape[-1] // 2
    inverse_freq = 10000.0 ** (-2.0 * jnp.arange(half_width, dtype=jnp.float32) / values.shape[-1])
    angles = position[:, None] * inverse_freq[None, :]
    cosine = jnp.cos(angles)[:, None, :]
    sine_part = jnp.sin(angles)[:, None, :]
    first_part = values[..., :half_width]
    second = values[..., half_width:]
    return jnp.concatenate(
        [first_part * cosine - second * sine_part, second * cosine + first_part * sine_part],
        axis=-1,
    )


def masked_scores(queries, key_rows, allowed):
    scores = jnp.einsum(
        "chd,lhd->hcl", queries, key_rows, preferred_element_type=jnp.float32
    ) / math.sqrt(queries.shape[-1])
    return jnp.where(allowed[None], scores, MASKED)


def attend(queries, key_rows, value_rows, allowed):
    scores = masked_scores(queries, key_rows, allowed)
    row_max = jnp.max(scores, axis=-1, keepdims=True)
    raised = jnp.where(allowed[None], jnp.exp(scores - row_max), 0.0)
    weights = (raised / jnp.sum(raised, axis=-1, keepdims=True)).astype(jnp.bfloat16)
    return jnp.einsum("hcl,lhd->chd", weights, value_rows, preferred_element_type=jnp.float32)


def body(
    tokens,
    attention_gain,
    query_weight,
    key_weight,
    value_weight,
    query_gain,
    key_gain,
    out_weight,
    key_pages,
    value_pages,
    page_table,
    far_table,
    cached_lengths,
    far_lengths,
    visible_from,
    feedforward_gain,
    routes,
    route_weights,
    gate_weight,
    up_weight,
    down_weight,
):
    n_group = lax.axis_size("group")
    n_expert = lax.axis_size(HEAD_AXES)
    group_id = lax.axis_index("group")
    as_float = tokens.astype(jnp.float32)
    normed = rms_norm(as_float, attention_gain).astype(jnp.bfloat16)
    row_block = lax.all_gather(normed, HEAD_AXES, axis=0, tiled=True)
    joined = jnp.concatenate(
        [
            jnp.dot(row_block, query_weight, preferred_element_type=jnp.float32),
            jnp.dot(row_block, key_weight, preferred_element_type=jnp.float32),
            jnp.dot(row_block, value_weight, preferred_element_type=jnp.float32),
        ],
        axis=1,
    )
    local_width = query_weight.shape[1]
    heads_here = local_width // HD
    query_raw = joined[:, :local_width]
    key_raw = joined[:, local_width : 2 * local_width]
    new_values = (
        joined[:, 2 * local_width :].astype(jnp.bfloat16).reshape(REQ, SPAN, heads_here, HD)
    )
    query_sums, key_sums = lax.psum(
        (jnp.sum(query_raw * query_raw, axis=1), jnp.sum(key_raw * key_raw, axis=1)), HEAD_AXES
    )
    full_width = local_width * n_expert
    query_normed = query_raw * lax.rsqrt(query_sums[:, None] / full_width + EPSILON) * query_gain
    key_normed = key_raw * lax.rsqrt(key_sums[:, None] / full_width + EPSILON) * key_gain
    lengths = cached_lengths[0]
    starts = visible_from[0]
    first_flag = (jnp.arange(REQ, dtype=jnp.int32) == 0).astype(jnp.int32)
    offsets = lengths + far_lengths[group_id] * first_flag
    position = (
        (offsets[:, None] + jnp.arange(SPAN, dtype=jnp.int32)[None, :])
        .reshape(-1)
        .astype(jnp.float32)
    )
    queries = (
        rotate(query_normed.reshape(-1, heads_here, HD), position)
        .astype(jnp.bfloat16)
        .reshape(REQ, SPAN, heads_here, HD)
    )
    new_keys = (
        rotate(key_normed.reshape(-1, heads_here, HD), position)
        .astype(jnp.bfloat16)
        .reshape(REQ, SPAN, heads_here, HD)
    )
    cache_slots = MAXP * PAGE
    own_keys = key_pages[page_table[0]].reshape(REQ, cache_slots, heads_here, HD)
    own_values = value_pages[page_table[0]].reshape(REQ, cache_slots, heads_here, HD)
    cache_pos = jnp.arange(cache_slots, dtype=jnp.int32)
    causal = jnp.arange(SPAN)[:, None] >= jnp.arange(SPAN)[None, :]

    def own_allowed(request):
        visible = (cache_pos < lengths[request]) & (cache_pos >= starts[request])
        return jnp.concatenate(
            [jnp.broadcast_to(visible[None], (SPAN, cache_slots)), causal], axis=1
        )

    def one_request(request):
        key_rows = jnp.concatenate([own_keys[request], new_keys[request]], axis=0)
        value_rows = jnp.concatenate([own_values[request], new_values[request]], axis=0)
        return attend(queries[request], key_rows, value_rows, own_allowed(request)).astype(
            jnp.bfloat16
        )

    other_outs = lax.map(one_request, jnp.arange(1, REQ, dtype=jnp.int32))
    keys_first = jnp.concatenate([own_keys[0], new_keys[0]], axis=0)
    values_first = jnp.concatenate([own_values[0], new_values[0]], axis=0)
    allowed_first = own_allowed(0)
    far_stack = jnp.stack([key_pages[far_table[0]], value_pages[far_table[0]]])
    received = from_partner(far_stack, "group", 0).reshape(2, cache_slots, heads_here, HD)
    far_visible = jnp.broadcast_to((cache_pos < far_lengths[group_id])[None], (SPAN, cache_slots))
    first_out = attend(
        queries[0],
        jnp.concatenate([keys_first, received[0]], axis=0),
        jnp.concatenate([values_first, received[1]], axis=0),
        jnp.concatenate([allowed_first, far_visible], axis=1),
    )
    context = jnp.concatenate([first_out.astype(jnp.bfloat16)[None], other_outs], axis=0).reshape(
        REQ * SPAN, local_width
    )
    attended = lax.psum_scatter(
        jnp.dot(context, out_weight, preferred_element_type=jnp.float32).astype(jnp.bfloat16),
        HEAD_AXES,
        scatter_dimension=0,
        tiled=True,
    ).astype(jnp.float32)
    residual = (as_float + attended).astype(jnp.bfloat16)
    moe_in = rms_norm(residual.astype(jnp.float32), feedforward_gain).astype(jnp.bfloat16)
    row_count = tokens.shape[0]
    n_chip = lax.axis_size(("group", "x"))
    capacity = row_count * TOP * 3 // (2 * EXPERTS)
    slots = EXPERTS * capacity
    flat_routes = routes.reshape(-1)
    onehot = (flat_routes[:, None] == jnp.arange(EXPERTS, dtype=jnp.int32)[None, :]).astype(
        jnp.int32
    )
    earlier = jnp.cumsum(onehot, axis=0) - onehot
    slot_index = jnp.sum(earlier * onehot, axis=1)
    position_of = (flat_routes * capacity + slot_index).reshape(row_count, TOP)
    slot_ids = jnp.arange(slots, dtype=jnp.int32)
    picks = position_of[None, :, :] == slot_ids[:, None, None]
    dispatch = jnp.any(picks, axis=2).astype(jnp.bfloat16)
    buffer = jnp.dot(dispatch, moe_in, preferred_element_type=jnp.float32).astype(jnp.bfloat16)
    incoming = lax.all_to_all(
        buffer.reshape(n_chip, capacity, D), ("group", "x"), split_axis=0, concat_axis=0, tiled=True
    ).reshape(-1, D)
    swap = [(0, 1), (1, 0)]
    partner_rows = lax.ppermute(incoming, "core", swap)
    rows_in = jnp.concatenate([incoming, partner_rows], axis=0)
    gate_act = jnp.dot(rows_in, gate_weight, preferred_element_type=jnp.float32)
    up_act = jnp.dot(rows_in, up_weight, preferred_element_type=jnp.float32)
    hidden = (jax.nn.silu(gate_act) * up_act).astype(jnp.bfloat16)
    down_part = jnp.dot(hidden, down_weight, preferred_element_type=jnp.float32)
    own_count = incoming.shape[0]
    from_partner_half = lax.ppermute(down_part[own_count:], "core", swap)
    expert_rows = (down_part[:own_count] + from_partner_half).astype(jnp.bfloat16)
    returned = lax.all_to_all(
        expert_rows.reshape(n_chip, capacity, D), ("group", "x"), split_axis=0, concat_axis=0, tiled=True
    ).reshape(slots, D)
    combine = jnp.sum(
        jnp.where(picks, route_weights[None, :, :], 0.0), axis=2
    ).T
    moe_out = jnp.dot(
        combine,
        returned.astype(jnp.float32),
        precision=lax.Precision.HIGHEST,
        preferred_element_type=jnp.float32,
    )
    return (residual.astype(jnp.float32) + moe_out).astype(jnp.bfloat16)


def solution(mesh):
    n_group, n_expert = mesh.devices.shape
    chip_mesh = jax.sharding.Mesh(
        mesh.devices.reshape(n_group, n_expert // 2, 2), ("group", "x", "core")
    )
    everyone = ("group", "x", "core")
    return jax.shard_map(
        body,
        mesh=chip_mesh,
        in_specs=(
            P(everyone, None),
            P(),
            P(None, HEAD_AXES),
            P(None, HEAD_AXES),
            P(None, HEAD_AXES),
            P(HEAD_AXES),
            P(HEAD_AXES),
            P(HEAD_AXES, None),
            P("group", None, HEAD_AXES),
            P("group", None, HEAD_AXES),
            P("group", None, None),
            P("group", None),
            P("group", None),
            P(),
            P("group", None),
            P(),
            P(everyone, None),
            P(everyone, None),
            P(None, everyone),
            P(None, everyone),
            P(everyone, None),
        ),
        out_specs=P(everyone, None),
        check_vma=False,
    )
```

```python
import math

import jax
import jax.numpy as jnp
from jax import lax
from jax.sharding import PartitionSpec as P

D = 2048
HD = 128
EXPERTS = 64
TOP = 8
PAGE = 128
REQ = 8
SPAN = 64
MAXP = 12


EPSILON = 1e-05
MASKED = -1e30
HEAD_AXES = ("x", "core")


def from_partner(value, axis, bit):
    mask = 2**bit
    pairs = [(source, source ^ mask) for source in range(lax.axis_size(axis))]
    return lax.ppermute(value, axis, pairs)


def rms_norm(values, norm_gain):
    return (
        values * lax.rsqrt(jnp.mean(values * values, axis=-1, keepdims=True) + EPSILON) * norm_gain
    )


def rotate(values, position):
    half_width = values.shape[-1] // 2
    inverse_freq = 10000.0 ** (-2.0 * jnp.arange(half_width, dtype=jnp.float32) / values.shape[-1])
    angles = position[:, None] * inverse_freq[None, :]
    cosine = jnp.cos(angles)[:, None, :]
    sine_part = jnp.sin(angles)[:, None, :]
    first_part = values[..., :half_width]
    second = values[..., half_width:]
    return jnp.concatenate(
        [first_part * cosine - second * sine_part, second * cosine + first_part * sine_part],
        axis=-1,
    )


def masked_scores(queries, key_rows, allowed):
    scores = jnp.einsum(
        "chd,lhd->hcl", queries, key_rows, preferred_element_type=jnp.float32
    ) / math.sqrt(queries.shape[-1])
    return jnp.where(allowed[None], scores, MASKED)


def attend(queries, key_rows, value_rows, allowed):
    scores = masked_scores(queries, key_rows, allowed)
    row_max = jnp.max(scores, axis=-1, keepdims=True)
    raised = jnp.where(allowed[None], jnp.exp(scores - row_max), 0.0)
    weights = (raised / jnp.sum(raised, axis=-1, keepdims=True)).astype(jnp.bfloat16)
    return jnp.einsum("hcl,lhd->chd", weights, value_rows, preferred_element_type=jnp.float32)


def body(
    tokens,
    attention_gain,
    query_weight,
    key_weight,
    value_weight,
    query_gain,
    key_gain,
    out_weight,
    key_pages,
    value_pages,
    page_table,
    far_table,
    cached_lengths,
    far_lengths,
    visible_from,
    feedforward_gain,
    routes,
    route_weights,
    gate_weight,
    up_weight,
    down_weight,
):
    n_group = lax.axis_size("group")
    n_expert = lax.axis_size(HEAD_AXES)
    group_id = lax.axis_index("group")
    as_float = tokens.astype(jnp.float32)
    normed = rms_norm(as_float, attention_gain).astype(jnp.bfloat16)
    row_block = lax.all_gather(normed, HEAD_AXES, axis=0, tiled=True)
    joined = jnp.concatenate(
        [
            jnp.dot(row_block, query_weight, preferred_element_type=jnp.float32),
            jnp.dot(row_block, key_weight, preferred_element_type=jnp.float32),
            jnp.dot(row_block, value_weight, preferred_element_type=jnp.float32),
        ],
        axis=1,
    )
    local_width = query_weight.shape[1]
    heads_here = local_width // HD
    query_raw = joined[:, :local_width]
    key_raw = joined[:, local_width : 2 * local_width]
    new_values = (
        joined[:, 2 * local_width :].astype(jnp.bfloat16).reshape(REQ, SPAN, heads_here, HD)
    )
    query_sums, key_sums = lax.psum(
        (jnp.sum(query_raw * query_raw, axis=1), jnp.sum(key_raw * key_raw, axis=1)), HEAD_AXES
    )
    full_width = local_width * n_expert
    query_normed = query_raw * lax.rsqrt(query_sums[:, None] / full_width + EPSILON) * query_gain
    key_normed = key_raw * lax.rsqrt(key_sums[:, None] / full_width + EPSILON) * key_gain
    lengths = cached_lengths[0]
    starts = visible_from[0]
    first_flag = (jnp.arange(REQ, dtype=jnp.int32) == 0).astype(jnp.int32)
    offsets = lengths + far_lengths[group_id] * first_flag
    position = (
        (offsets[:, None] + jnp.arange(SPAN, dtype=jnp.int32)[None, :])
        .reshape(-1)
        .astype(jnp.float32)
    )
    queries = (
        rotate(query_normed.reshape(-1, heads_here, HD), position)
        .astype(jnp.bfloat16)
        .reshape(REQ, SPAN, heads_here, HD)
    )
    new_keys = (
        rotate(key_normed.reshape(-1, heads_here, HD), position)
        .astype(jnp.bfloat16)
        .reshape(REQ, SPAN, heads_here, HD)
    )
    cache_slots = MAXP * PAGE
    own_keys = key_pages[page_table[0]].reshape(REQ, cache_slots, heads_here, HD)
    own_values = value_pages[page_table[0]].reshape(REQ, cache_slots, heads_here, HD)
    cache_pos = jnp.arange(cache_slots, dtype=jnp.int32)
    causal = jnp.arange(SPAN)[:, None] >= jnp.arange(SPAN)[None, :]

    def own_allowed(request):
        visible = (cache_pos < lengths[request]) & (cache_pos >= starts[request])
        return jnp.concatenate(
            [jnp.broadcast_to(visible[None], (SPAN, cache_slots)), causal], axis=1
        )

    def one_request(request):
        key_rows = jnp.concatenate([own_keys[request], new_keys[request]], axis=0)
        value_rows = jnp.concatenate([own_values[request], new_values[request]], axis=0)
        return attend(queries[request], key_rows, value_rows, own_allowed(request)).astype(
            jnp.bfloat16
        )

    other_outs = lax.map(one_request, jnp.arange(1, REQ, dtype=jnp.int32))
    keys_first = jnp.concatenate([own_keys[0], new_keys[0]], axis=0)
    values_first = jnp.concatenate([own_values[0], new_values[0]], axis=0)
    allowed_first = own_allowed(0)
    far_stack = jnp.stack([key_pages[far_table[0]], value_pages[far_table[0]]])
    received = from_partner(far_stack, "group", 0).reshape(2, cache_slots, heads_here, HD)
    far_visible = jnp.broadcast_to((cache_pos < far_lengths[group_id])[None], (SPAN, cache_slots))
    first_out = attend(
        queries[0],
        jnp.concatenate([keys_first, received[0]], axis=0),
        jnp.concatenate([values_first, received[1]], axis=0),
        jnp.concatenate([allowed_first, far_visible], axis=1),
    )
    context = jnp.concatenate([first_out.astype(jnp.bfloat16)[None], other_outs], axis=0)
    n_x = lax.axis_size("x")
    by_core = (
        context.reshape(n_x, 2, SPAN, local_width)
        .transpose(1, 0, 2, 3)
        .reshape(REQ * SPAN, local_width)
    )
    projected = jnp.dot(by_core, out_weight, preferred_element_type=jnp.float32)
    core_summed = lax.psum_scatter(projected, "core", scatter_dimension=0, tiled=True)
    attended = lax.psum_scatter(
        core_summed.astype(jnp.bfloat16), "x", scatter_dimension=0, tiled=True
    ).astype(jnp.float32)
    residual = (as_float + attended).astype(jnp.bfloat16)
    moe_in = rms_norm(residual.astype(jnp.float32), feedforward_gain).astype(jnp.bfloat16)
    row_count = tokens.shape[0]
    n_chip = lax.axis_size(("group", "x"))
    capacity = row_count * TOP * 3 // (2 * EXPERTS)
    slots = EXPERTS * capacity
    flat_routes = routes.reshape(-1)
    onehot = (flat_routes[:, None] == jnp.arange(EXPERTS, dtype=jnp.int32)[None, :]).astype(
        jnp.int32
    )
    earlier = jnp.cumsum(onehot, axis=0) - onehot
    slot_index = jnp.sum(earlier * onehot, axis=1)
    position_of = (flat_routes * capacity + slot_index).reshape(row_count, TOP)
    slot_ids = jnp.arange(slots, dtype=jnp.int32).reshape(EXPERTS, capacity)
    picks = position_of[None, None, :, :] == slot_ids[:, :, None, None]
    dispatch = jnp.any(picks, axis=3).astype(jnp.bfloat16)
    buffer = jnp.einsum(
        "est,td->esd", dispatch, moe_in, preferred_element_type=jnp.float32
    ).astype(jnp.bfloat16)
    incoming = lax.all_to_all(buffer, ("group", "x"), split_axis=0, concat_axis=0, tiled=True)
    swap = [(0, 1), (1, 0)]
    partner_rows = lax.ppermute(incoming, "core", swap)

    def expert_half(rows_in):
        gate_act = jnp.einsum("esd,df->esf", rows_in, gate_weight, preferred_element_type=jnp.float32)
        up_act = jnp.einsum("esd,df->esf", rows_in, up_weight, preferred_element_type=jnp.float32)
        hidden = (jax.nn.silu(gate_act) * up_act).astype(jnp.bfloat16)
        return jnp.einsum("esf,fd->esd", hidden, down_weight, preferred_element_type=jnp.float32)

    for_partner = expert_half(partner_rows)
    from_partner_half = lax.ppermute(for_partner, "core", swap)
    own_part = expert_half(incoming)
    expert_rows = (own_part + from_partner_half).astype(jnp.bfloat16)
    returned = lax.all_to_all(expert_rows, ("group", "x"), split_axis=0, concat_axis=0, tiled=True)
    combine = jnp.sum(jnp.where(picks, route_weights[None, None, :, :], 0.0), axis=3)
    moe_out = jnp.einsum(
        "est,esd->td",
        combine,
        returned.astype(jnp.float32),
        precision=lax.Precision.HIGHEST,
        preferred_element_type=jnp.float32,
    )
    return (residual.astype(jnp.float32) + moe_out).astype(jnp.bfloat16)


def solution(mesh):
    n_group, n_expert = mesh.devices.shape
    chip_mesh = jax.sharding.Mesh(
        mesh.devices.reshape(n_group, n_expert // 2, 2), ("group", "x", "core")
    )
    everyone = ("group", "x", "core")
    return jax.shard_map(
        body,
        mesh=chip_mesh,
        in_specs=(
            P(everyone, None),
            P(),
            P(None, HEAD_AXES),
            P(None, HEAD_AXES),
            P(None, HEAD_AXES),
            P(HEAD_AXES),
            P(HEAD_AXES),
            P(HEAD_AXES, None),
            P("group", None, HEAD_AXES),
            P("group", None, HEAD_AXES),
            P("group", None, None),
            P("group", None),
            P("group", None),
            P(),
            P("group", None),
            P(),
            P(everyone, None),
            P(everyone, None),
            P(None, everyone),
            P(None, everyone),
            P(everyone, None),
        ),
        out_specs=P(everyone, None),
        check_vma=False,
    )
```

```python
import math

import jax
import jax.numpy as jnp
from jax import lax
from jax.sharding import PartitionSpec as P

D = 2048
HD = 128
EXPERTS = 64
TOP = 8
PAGE = 128
REQ = 8
SPAN = 64
MAXP = 12


EPSILON = 1e-05
MASKED = -1e30
HEAD_AXES = ("x", "core")


def from_partner(value, axis, bit):
    mask = 2**bit
    pairs = [(source, source ^ mask) for source in range(lax.axis_size(axis))]
    return lax.ppermute(value, axis, pairs)


def rms_norm(values, norm_gain):
    return (
        values * lax.rsqrt(jnp.mean(values * values, axis=-1, keepdims=True) + EPSILON) * norm_gain
    )


def rotate(values, position):
    half_width = values.shape[-1] // 2
    inverse_freq = 10000.0 ** (-2.0 * jnp.arange(half_width, dtype=jnp.float32) / values.shape[-1])
    angles = position[:, None] * inverse_freq[None, :]
    cosine = jnp.cos(angles)[:, None, :]
    sine_part = jnp.sin(angles)[:, None, :]
    first_part = values[..., :half_width]
    second = values[..., half_width:]
    return jnp.concatenate(
        [first_part * cosine - second * sine_part, second * cosine + first_part * sine_part],
        axis=-1,
    )


def masked_scores(queries, key_rows, allowed):
    scores = jnp.einsum(
        "chd,lhd->hcl", queries, key_rows, preferred_element_type=jnp.float32
    ) / math.sqrt(queries.shape[-1])
    return jnp.where(allowed[None], scores, MASKED)


def attend(queries, key_rows, value_rows, allowed):
    scores = masked_scores(queries, key_rows, allowed)
    row_max = jnp.max(scores, axis=-1, keepdims=True)
    raised = jnp.where(allowed[None], jnp.exp(scores - row_max), 0.0)
    weights = (raised / jnp.sum(raised, axis=-1, keepdims=True)).astype(jnp.bfloat16)
    return jnp.einsum("hcl,lhd->chd", weights, value_rows, preferred_element_type=jnp.float32)


def body(
    tokens,
    attention_gain,
    query_weight,
    key_weight,
    value_weight,
    query_gain,
    key_gain,
    out_weight,
    key_pages,
    value_pages,
    page_table,
    far_table,
    cached_lengths,
    far_lengths,
    visible_from,
    feedforward_gain,
    routes,
    route_weights,
    gate_weight,
    up_weight,
    down_weight,
):
    n_group = lax.axis_size("group")
    n_expert = lax.axis_size(HEAD_AXES)
    group_id = lax.axis_index("group")
    as_float = tokens.astype(jnp.float32)
    normed = rms_norm(as_float, attention_gain).astype(jnp.bfloat16)
    row_block = lax.all_gather(normed, HEAD_AXES, axis=0, tiled=True)
    joined = jnp.concatenate(
        [
            jnp.dot(row_block, query_weight, preferred_element_type=jnp.float32),
            jnp.dot(row_block, key_weight, preferred_element_type=jnp.float32),
            jnp.dot(row_block, value_weight, preferred_element_type=jnp.float32),
        ],
        axis=1,
    )
    local_width = query_weight.shape[1]
    heads_here = local_width // HD
    query_raw = joined[:, :local_width]
    key_raw = joined[:, local_width : 2 * local_width]
    new_values = (
        joined[:, 2 * local_width :].astype(jnp.bfloat16).reshape(REQ, SPAN, heads_here, HD)
    )
    query_sums, key_sums = lax.psum(
        (jnp.sum(query_raw * query_raw, axis=1), jnp.sum(key_raw * key_raw, axis=1)), HEAD_AXES
    )
    full_width = local_width * n_expert
    query_normed = query_raw * lax.rsqrt(query_sums[:, None] / full_width + EPSILON) * query_gain
    key_normed = key_raw * lax.rsqrt(key_sums[:, None] / full_width + EPSILON) * key_gain
    lengths = cached_lengths[0]
    starts = visible_from[0]
    first_flag = (jnp.arange(REQ, dtype=jnp.int32) == 0).astype(jnp.int32)
    offsets = lengths + far_lengths[group_id] * first_flag
    position = (
        (offsets[:, None] + jnp.arange(SPAN, dtype=jnp.int32)[None, :])
        .reshape(-1)
        .astype(jnp.float32)
    )
    queries = (
        rotate(query_normed.reshape(-1, heads_here, HD), position)
        .astype(jnp.bfloat16)
        .reshape(REQ, SPAN, heads_here, HD)
    )
    new_keys = (
        rotate(key_normed.reshape(-1, heads_here, HD), position)
        .astype(jnp.bfloat16)
        .reshape(REQ, SPAN, heads_here, HD)
    )
    cache_slots = MAXP * PAGE
    pool_size = key_pages.shape[0]
    page_pick = (
        page_table[0][:, :, None] == jnp.arange(pool_size, dtype=jnp.int32)[None, None, :]
    ).astype(jnp.bfloat16)
    own_keys = jnp.einsum(
        "rpq,qsc->rpsc", page_pick, key_pages, preferred_element_type=jnp.float32
    ).astype(jnp.bfloat16).reshape(REQ, cache_slots, local_width)
    own_values = jnp.einsum(
        "rpq,qsc->rpsc", page_pick, value_pages, preferred_element_type=jnp.float32
    ).astype(jnp.bfloat16).reshape(REQ, cache_slots, local_width)
    far_stack = jnp.stack([key_pages[far_table[0]], value_pages[far_table[0]]])
    received = from_partner(far_stack, "group", 0).reshape(2, cache_slots, local_width)
    cache_pos = jnp.arange(cache_slots, dtype=jnp.int32)
    own_visible = (cache_pos[None, :] < lengths[:, None]) & (cache_pos[None, :] >= starts[:, None])
    far_visible = cache_pos < far_lengths[group_id]
    causal = jnp.arange(SPAN)[:, None] >= jnp.arange(SPAN)[None, :]
    is_first = (jnp.arange(REQ) == 0)[:, None, None]
    new_keys = new_keys.reshape(REQ, SPAN, local_width)
    new_values = new_values.reshape(REQ, SPAN, local_width)
    queries = queries.reshape(REQ, SPAN, local_width)
    scale = math.sqrt(HD)
    head_outs = []
    for head in range(heads_here):
        cols = slice(head * HD, (head + 1) * HD)
        q = queries[:, :, cols]
        s_own = jnp.einsum("rcd,rld->rcl", q, own_keys[:, :, cols], preferred_element_type=jnp.float32) / scale
        s_new = jnp.einsum("rcd,rjd->rcj", q, new_keys[:, :, cols], preferred_element_type=jnp.float32) / scale
        s_far = jnp.einsum("cd,ld->cl", q[0], received[0][:, cols], preferred_element_type=jnp.float32) / scale
        s_own = jnp.where(own_visible[:, None, :], s_own, MASKED)
        s_new = jnp.where(causal[None], s_new, MASKED)
        s_far = jnp.where(far_visible[None, :], s_far, MASKED)
        far_max = jnp.max(s_far, axis=-1, keepdims=True)
        row_max = jnp.maximum(
            jnp.max(s_own, axis=-1, keepdims=True), jnp.max(s_new, axis=-1, keepdims=True)
        )
        row_max = jnp.where(is_first, jnp.maximum(row_max, far_max[None]), row_max)
        p_own = jnp.where(own_visible[:, None, :], jnp.exp(s_own - row_max), 0.0)
        p_new = jnp.where(causal[None], jnp.exp(s_new - row_max), 0.0)
        p_far = jnp.where(far_visible[None, :], jnp.exp(s_far - row_max[0]), 0.0)
        total = jnp.sum(p_own, axis=-1, keepdims=True) + jnp.sum(p_new, axis=-1, keepdims=True)
        total = jnp.where(is_first, total + jnp.sum(p_far, axis=-1, keepdims=True)[None], total)
        w_own = (p_own / total).astype(jnp.bfloat16)
        w_new = (p_new / total).astype(jnp.bfloat16)
        w_far = (p_far / total[0]).astype(jnp.bfloat16)
        ctx = jnp.einsum("rcl,rld->rcd", w_own, own_values[:, :, cols], preferred_element_type=jnp.float32)
        ctx = ctx + jnp.einsum("rcj,rjd->rcd", w_new, new_values[:, :, cols], preferred_element_type=jnp.float32)
        far_ctx = jnp.einsum("cl,ld->cd", w_far, received[1][:, cols], preferred_element_type=jnp.float32)
        ctx = ctx + jnp.where(is_first, far_ctx[None], 0.0)
        head_outs.append(ctx.astype(jnp.bfloat16))
    context = jnp.concatenate(head_outs, axis=-1)
    attended = lax.psum_scatter(
        jnp.dot(context.reshape(REQ * SPAN, local_width), out_weight, preferred_element_type=jnp.float32).astype(jnp.bfloat16),
        HEAD_AXES,
        scatter_dimension=0,
        tiled=True,
    ).astype(jnp.float32)
    residual = (as_float + attended).astype(jnp.bfloat16)
    moe_in = rms_norm(residual.astype(jnp.float32), feedforward_gain).astype(jnp.bfloat16)
    row_count = tokens.shape[0]
    n_chip = lax.axis_size(("group", "x"))
    capacity = row_count * TOP * 3 // (2 * EXPERTS)
    slots = EXPERTS * capacity
    flat_routes = routes.reshape(-1)
    onehot = (flat_routes[:, None] == jnp.arange(EXPERTS, dtype=jnp.int32)[None, :]).astype(
        jnp.int32
    )
    earlier = jnp.cumsum(onehot, axis=0) - onehot
    slot_index = jnp.sum(earlier * onehot, axis=1)
    position_of = (flat_routes * capacity + slot_index).reshape(row_count, TOP)
    slot_ids = jnp.arange(slots, dtype=jnp.int32).reshape(EXPERTS, capacity)
    picks = position_of[None, None, :, :] == slot_ids[:, :, None, None]
    dispatch = jnp.any(picks, axis=3).astype(jnp.bfloat16)
    buffer = jnp.einsum(
        "est,td->esd", dispatch, moe_in, preferred_element_type=jnp.float32
    ).astype(jnp.bfloat16)
    incoming = lax.all_to_all(buffer, ("group", "x"), split_axis=0, concat_axis=0, tiled=True)
    swap = [(0, 1), (1, 0)]
    partner_rows = lax.ppermute(incoming, "core", swap)

    def expert_half(rows_in):
        gate_act = jnp.einsum("esd,df->esf", rows_in, gate_weight, preferred_element_type=jnp.float32)
        up_act = jnp.einsum("esd,df->esf", rows_in, up_weight, preferred_element_type=jnp.float32)
        hidden = (jax.nn.silu(gate_act) * up_act).astype(jnp.bfloat16)
        return jnp.einsum("esf,fd->esd", hidden, down_weight, preferred_element_type=jnp.float32)

    for_partner = expert_half(partner_rows)
    from_partner_half = lax.ppermute(for_partner, "core", swap)
    own_part = expert_half(incoming)
    expert_rows = (own_part + from_partner_half).astype(jnp.bfloat16)
    returned = lax.all_to_all(expert_rows, ("group", "x"), split_axis=0, concat_axis=0, tiled=True)
    combine = jnp.sum(jnp.where(picks, route_weights[None, None, :, :], 0.0), axis=3)
    moe_out = jnp.einsum(
        "est,esd->td",
        combine,
        returned.astype(jnp.float32),
        precision=lax.Precision.HIGHEST,
        preferred_element_type=jnp.float32,
    )
    return (residual.astype(jnp.float32) + moe_out).astype(jnp.bfloat16)


def solution(mesh):
    n_group, n_expert = mesh.devices.shape
    chip_mesh = jax.sharding.Mesh(
        mesh.devices.reshape(n_group, n_expert // 2, 2), ("group", "x", "core")
    )
    everyone = ("group", "x", "core")
    return jax.shard_map(
        body,
        mesh=chip_mesh,
        in_specs=(
            P(everyone, None),
            P(),
            P(None, HEAD_AXES),
            P(None, HEAD_AXES),
            P(None, HEAD_AXES),
            P(HEAD_AXES),
            P(HEAD_AXES),
            P(HEAD_AXES, None),
            P("group", None, HEAD_AXES),
            P("group", None, HEAD_AXES),
            P("group", None, None),
            P("group", None),
            P("group", None),
            P(),
            P("group", None),
            P(),
            P(everyone, None),
            P(everyone, None),
            P(None, everyone),
            P(None, everyone),
            P(everyone, None),
        ),
        out_specs=P(everyone, None),
        check_vma=False,
    )
```

```python
import math

import jax
import jax.numpy as jnp
from jax import lax
from jax.sharding import PartitionSpec as P

D = 2048
HD = 128
EXPERTS = 64
TOP = 8
PAGE = 128
REQ = 8
SPAN = 64
MAXP = 12


EPSILON = 1e-05
MASKED = -1e30
HEAD_AXES = ("x", "core")


def from_partner(value, axis, bit):
    mask = 2**bit
    pairs = [(source, source ^ mask) for source in range(lax.axis_size(axis))]
    return lax.ppermute(value, axis, pairs)


def rms_norm(values, norm_gain):
    return (
        values * lax.rsqrt(jnp.mean(values * values, axis=-1, keepdims=True) + EPSILON) * norm_gain
    )


def rotate(values, position):
    half_width = values.shape[-1] // 2
    inverse_freq = 10000.0 ** (-2.0 * jnp.arange(half_width, dtype=jnp.float32) / values.shape[-1])
    angles = position[:, None] * inverse_freq[None, :]
    cosine = jnp.cos(angles)[:, None, :]
    sine_part = jnp.sin(angles)[:, None, :]
    first_part = values[..., :half_width]
    second = values[..., half_width:]
    return jnp.concatenate(
        [first_part * cosine - second * sine_part, second * cosine + first_part * sine_part],
        axis=-1,
    )


def masked_scores(queries, key_rows, allowed):
    scores = jnp.einsum(
        "chd,lhd->hcl", queries, key_rows, preferred_element_type=jnp.float32
    ) / math.sqrt(queries.shape[-1])
    return jnp.where(allowed[None], scores, MASKED)


def attend(queries, key_rows, value_rows, allowed):
    scores = masked_scores(queries, key_rows, allowed)
    row_max = jnp.max(scores, axis=-1, keepdims=True)
    raised = jnp.where(allowed[None], jnp.exp(scores - row_max), 0.0)
    weights = (raised / jnp.sum(raised, axis=-1, keepdims=True)).astype(jnp.bfloat16)
    return jnp.einsum("hcl,lhd->chd", weights, value_rows, preferred_element_type=jnp.float32)


def body(
    tokens,
    attention_gain,
    query_weight,
    key_weight,
    value_weight,
    query_gain,
    key_gain,
    out_weight,
    key_pages,
    value_pages,
    page_table,
    far_table,
    cached_lengths,
    far_lengths,
    visible_from,
    feedforward_gain,
    routes,
    route_weights,
    gate_weight,
    up_weight,
    down_weight,
):
    n_group = lax.axis_size("group")
    n_expert = lax.axis_size(HEAD_AXES)
    group_id = lax.axis_index("group")
    as_float = tokens.astype(jnp.float32)
    normed = rms_norm(as_float, attention_gain).astype(jnp.bfloat16)
    row_block = lax.all_gather(normed, HEAD_AXES, axis=0, tiled=True)
    row_block, out_weight = lax.optimization_barrier((row_block, out_weight))
    full_out_weight = lax.all_gather(out_weight, HEAD_AXES, axis=0, tiled=True)
    joined = jnp.concatenate(
        [
            jnp.dot(row_block, query_weight, preferred_element_type=jnp.float32),
            jnp.dot(row_block, key_weight, preferred_element_type=jnp.float32),
            jnp.dot(row_block, value_weight, preferred_element_type=jnp.float32),
        ],
        axis=1,
    )
    local_width = query_weight.shape[1]
    heads_here = local_width // HD
    query_raw = joined[:, :local_width]
    key_raw = joined[:, local_width : 2 * local_width]
    new_values = (
        joined[:, 2 * local_width :].astype(jnp.bfloat16).reshape(REQ, SPAN, heads_here, HD)
    )
    query_sums, key_sums = lax.psum(
        (jnp.sum(query_raw * query_raw, axis=1), jnp.sum(key_raw * key_raw, axis=1)), HEAD_AXES
    )
    full_width = local_width * n_expert
    query_normed = query_raw * lax.rsqrt(query_sums[:, None] / full_width + EPSILON) * query_gain
    key_normed = key_raw * lax.rsqrt(key_sums[:, None] / full_width + EPSILON) * key_gain
    lengths = cached_lengths[0]
    starts = visible_from[0]
    first_flag = (jnp.arange(REQ, dtype=jnp.int32) == 0).astype(jnp.int32)
    offsets = lengths + far_lengths[group_id] * first_flag
    position = (
        (offsets[:, None] + jnp.arange(SPAN, dtype=jnp.int32)[None, :])
        .reshape(-1)
        .astype(jnp.float32)
    )
    queries = (
        rotate(query_normed.reshape(-1, heads_here, HD), position)
        .astype(jnp.bfloat16)
        .reshape(REQ, SPAN, heads_here, HD)
    )
    new_keys = (
        rotate(key_normed.reshape(-1, heads_here, HD), position)
        .astype(jnp.bfloat16)
        .reshape(REQ, SPAN, heads_here, HD)
    )
    cache_slots = MAXP * PAGE
    pool_size = key_pages.shape[0]
    page_pick = (
        page_table[0][:, :, None] == jnp.arange(pool_size, dtype=jnp.int32)[None, None, :]
    ).astype(jnp.bfloat16)
    own_keys = jnp.einsum(
        "rpq,qsc->rpsc", page_pick, key_pages, preferred_element_type=jnp.float32
    ).astype(jnp.bfloat16).reshape(REQ, cache_slots, local_width)
    own_values = jnp.einsum(
        "rpq,qsc->rpsc", page_pick, value_pages, preferred_element_type=jnp.float32
    ).astype(jnp.bfloat16).reshape(REQ, cache_slots, local_width)
    far_stack = jnp.stack([key_pages[far_table[0]], value_pages[far_table[0]]])
    received = from_partner(far_stack, "group", 0).reshape(2, cache_slots, local_width)
    cache_pos = jnp.arange(cache_slots, dtype=jnp.int32)
    own_visible = (cache_pos[None, :] < lengths[:, None]) & (cache_pos[None, :] >= starts[:, None])
    far_visible = cache_pos < far_lengths[group_id]
    causal = jnp.arange(SPAN)[:, None] >= jnp.arange(SPAN)[None, :]
    is_first = (jnp.arange(REQ) == 0)[:, None, None]
    new_keys = new_keys.reshape(REQ, SPAN, local_width)
    new_values = new_values.reshape(REQ, SPAN, local_width)
    queries = queries.reshape(REQ, SPAN, local_width)
    scale = math.sqrt(HD)
    head_outs = []
    for head in range(heads_here):
        cols = slice(head * HD, (head + 1) * HD)
        q = queries[:, :, cols]
        s_own = jnp.einsum("rcd,rld->rcl", q, own_keys[:, :, cols], preferred_element_type=jnp.float32) / scale
        s_new = jnp.einsum("rcd,rjd->rcj", q, new_keys[:, :, cols], preferred_element_type=jnp.float32) / scale
        s_far = jnp.einsum("cd,ld->cl", q[0], received[0][:, cols], preferred_element_type=jnp.float32) / scale
        s_own = jnp.where(own_visible[:, None, :], s_own, MASKED)
        s_new = jnp.where(causal[None], s_new, MASKED)
        s_far = jnp.where(far_visible[None, :], s_far, MASKED)
        far_max = jnp.max(s_far, axis=-1, keepdims=True)
        row_max = jnp.maximum(
            jnp.max(s_own, axis=-1, keepdims=True), jnp.max(s_new, axis=-1, keepdims=True)
        )
        row_max = jnp.where(is_first, jnp.maximum(row_max, far_max[None]), row_max)
        p_own = jnp.where(own_visible[:, None, :], jnp.exp(s_own - row_max), 0.0)
        p_new = jnp.where(causal[None], jnp.exp(s_new - row_max), 0.0)
        p_far = jnp.where(far_visible[None, :], jnp.exp(s_far - row_max[0]), 0.0)
        total = jnp.sum(p_own, axis=-1, keepdims=True) + jnp.sum(p_new, axis=-1, keepdims=True)
        total = jnp.where(is_first, total + jnp.sum(p_far, axis=-1, keepdims=True)[None], total)
        w_own = (p_own / total).astype(jnp.bfloat16)
        w_new = (p_new / total).astype(jnp.bfloat16)
        w_far = (p_far / total[0]).astype(jnp.bfloat16)
        ctx = jnp.einsum("rcl,rld->rcd", w_own, own_values[:, :, cols], preferred_element_type=jnp.float32)
        ctx = ctx + jnp.einsum("rcj,rjd->rcd", w_new, new_values[:, :, cols], preferred_element_type=jnp.float32)
        far_ctx = jnp.einsum("cl,ld->cd", w_far, received[1][:, cols], preferred_element_type=jnp.float32)
        ctx = ctx + jnp.where(is_first, far_ctx[None], 0.0)
        head_outs.append(ctx.astype(jnp.bfloat16))
    context = jnp.concatenate(head_outs, axis=-1)
    token_context = lax.all_to_all(
        context, HEAD_AXES, split_axis=0, concat_axis=2, tiled=True
    ).reshape(SPAN, -1)
    attended = jnp.dot(token_context, full_out_weight, preferred_element_type=jnp.float32)
    residual = (as_float + attended).astype(jnp.bfloat16)
    moe_in = rms_norm(residual.astype(jnp.float32), feedforward_gain).astype(jnp.bfloat16)
    row_count = tokens.shape[0]
    n_chip = lax.axis_size(("group", "x"))
    capacity = row_count * TOP * 3 // (2 * EXPERTS)
    slots = EXPERTS * capacity
    flat_routes = routes.reshape(-1)
    onehot = (flat_routes[:, None] == jnp.arange(EXPERTS, dtype=jnp.int32)[None, :]).astype(
        jnp.int32
    )
    earlier = jnp.cumsum(onehot, axis=0) - onehot
    slot_index = jnp.sum(earlier * onehot, axis=1)
    position_of = (flat_routes * capacity + slot_index).reshape(row_count, TOP)
    slot_ids = jnp.arange(slots, dtype=jnp.int32).reshape(EXPERTS, capacity)
    picks = position_of[None, None, :, :] == slot_ids[:, :, None, None]
    dispatch = jnp.any(picks, axis=3).astype(jnp.bfloat16)
    lanes = 128
    bands = D // lanes
    tiled_in = moe_in.reshape(row_count, bands, lanes)
    buffer = jnp.einsum(
        "est,tjl->esjl", dispatch, tiled_in, preferred_element_type=jnp.float32
    ).astype(jnp.bfloat16)

    def exchange(blocks):
        flat = blocks.reshape(n_chip, capacity * bands, lanes)
        moved = lax.all_to_all(flat, ("group", "x"), split_axis=0, concat_axis=0, tiled=True)
        return moved.reshape(n_chip, capacity, bands, lanes)

    incoming = exchange(buffer)
    swap = [(0, 1), (1, 0)]
    partner_rows = lax.ppermute(incoming, "core", swap)
    gate_bands = gate_weight.reshape(bands, lanes, -1)
    up_bands = up_weight.reshape(bands, lanes, -1)
    down_bands = down_weight.reshape(-1, bands, lanes)

    def expert_half(rows_in):
        gate_act = jnp.einsum("esjl,jlf->esf", rows_in, gate_bands, preferred_element_type=jnp.float32)
        up_act = jnp.einsum("esjl,jlf->esf", rows_in, up_bands, preferred_element_type=jnp.float32)
        hidden = (jax.nn.silu(gate_act) * up_act).astype(jnp.bfloat16)
        return jnp.einsum("esf,fjl->esjl", hidden, down_bands, preferred_element_type=jnp.float32)

    for_partner = expert_half(partner_rows)
    from_partner_half = lax.ppermute(for_partner, "core", swap)
    own_part = expert_half(incoming)
    expert_rows = (own_part + from_partner_half).astype(jnp.bfloat16)
    returned = exchange(expert_rows)
    combine = jnp.sum(jnp.where(picks, route_weights[None, None, :, :], 0.0), axis=3)
    moe_out = jnp.einsum(
        "est,esjl->tjl",
        combine,
        returned.astype(jnp.float32),
        precision=lax.Precision.HIGHEST,
        preferred_element_type=jnp.float32,
    ).reshape(row_count, D)
    return (residual.astype(jnp.float32) + moe_out).astype(jnp.bfloat16)


def solution(mesh):
    n_group, n_expert = mesh.devices.shape
    chip_mesh = jax.sharding.Mesh(
        mesh.devices.reshape(n_group, n_expert // 2, 2), ("group", "x", "core")
    )
    everyone = ("group", "x", "core")
    return jax.shard_map(
        body,
        mesh=chip_mesh,
        in_specs=(
            P(everyone, None),
            P(),
            P(None, HEAD_AXES),
            P(None, HEAD_AXES),
            P(None, HEAD_AXES),
            P(HEAD_AXES),
            P(HEAD_AXES),
            P(HEAD_AXES, None),
            P("group", None, HEAD_AXES),
            P("group", None, HEAD_AXES),
            P("group", None, None),
            P("group", None),
            P("group", None),
            P(),
            P("group", None),
            P(),
            P(everyone, None),
            P(everyone, None),
            P(None, everyone),
            P(None, everyone),
            P(everyone, None),
        ),
        out_specs=P(everyone, None),
        check_vma=False,
    )
```

```python
import math

import jax
import jax.numpy as jnp
from jax import lax
from jax.sharding import PartitionSpec as P

D = 2048
HD = 128
EXPERTS = 64
TOP = 8
PAGE = 128
REQ = 8
SPAN = 64
MAXP = 12


EPSILON = 1e-05
MASKED = -1e30
HEAD_AXES = ("x", "core")


def from_partner(value, axis, bit):
    mask = 2**bit
    pairs = [(source, source ^ mask) for source in range(lax.axis_size(axis))]
    return lax.ppermute(value, axis, pairs)


def rms_norm(values, norm_gain):
    return (
        values * lax.rsqrt(jnp.mean(values * values, axis=-1, keepdims=True) + EPSILON) * norm_gain
    )


def rotate(values, position):
    half_width = values.shape[-1] // 2
    inverse_freq = 10000.0 ** (-2.0 * jnp.arange(half_width, dtype=jnp.float32) / values.shape[-1])
    angles = position[:, None] * inverse_freq[None, :]
    cosine = jnp.cos(angles)[:, None, :]
    sine_part = jnp.sin(angles)[:, None, :]
    first_part = values[..., :half_width]
    second = values[..., half_width:]
    return jnp.concatenate(
        [first_part * cosine - second * sine_part, second * cosine + first_part * sine_part],
        axis=-1,
    )


def masked_scores(queries, key_rows, allowed):
    scores = jnp.einsum(
        "chd,lhd->hcl", queries, key_rows, preferred_element_type=jnp.float32
    ) / math.sqrt(queries.shape[-1])
    return jnp.where(allowed[None], scores, MASKED)


def attend(queries, key_rows, value_rows, allowed):
    scores = masked_scores(queries, key_rows, allowed)
    row_max = jnp.max(scores, axis=-1, keepdims=True)
    raised = jnp.where(allowed[None], jnp.exp(scores - row_max), 0.0)
    weights = (raised / jnp.sum(raised, axis=-1, keepdims=True)).astype(jnp.bfloat16)
    return jnp.einsum("hcl,lhd->chd", weights, value_rows, preferred_element_type=jnp.float32)


def body(
    tokens,
    attention_gain,
    query_weight,
    key_weight,
    value_weight,
    query_gain,
    key_gain,
    out_weight,
    key_pages,
    value_pages,
    page_table,
    far_table,
    cached_lengths,
    far_lengths,
    visible_from,
    feedforward_gain,
    routes,
    route_weights,
    gate_weight,
    up_weight,
    down_weight,
):
    n_group = lax.axis_size("group")
    n_expert = lax.axis_size(HEAD_AXES)
    group_id = lax.axis_index("group")
    as_float = tokens.astype(jnp.float32)
    normed = rms_norm(as_float, attention_gain).astype(jnp.bfloat16)
    row_block = lax.all_gather(normed, HEAD_AXES, axis=0, tiled=True)
    swap = [(0, 1), (1, 0)]
    gate_full = jnp.concatenate([gate_weight, lax.ppermute(gate_weight, "core", swap)], axis=1)
    up_full = jnp.concatenate([up_weight, lax.ppermute(up_weight, "core", swap)], axis=1)
    down_full = jnp.concatenate([down_weight, lax.ppermute(down_weight, "core", swap)], axis=0)
    joined = jnp.concatenate(
        [
            jnp.dot(row_block, query_weight, preferred_element_type=jnp.float32),
            jnp.dot(row_block, key_weight, preferred_element_type=jnp.float32),
            jnp.dot(row_block, value_weight, preferred_element_type=jnp.float32),
        ],
        axis=1,
    )
    local_width = query_weight.shape[1]
    heads_here = local_width // HD
    query_raw = joined[:, :local_width]
    key_raw = joined[:, local_width : 2 * local_width]
    new_values = (
        joined[:, 2 * local_width :].astype(jnp.bfloat16).reshape(REQ, SPAN, heads_here, HD)
    )
    query_sums, key_sums = lax.psum(
        (jnp.sum(query_raw * query_raw, axis=1), jnp.sum(key_raw * key_raw, axis=1)), HEAD_AXES
    )
    full_width = local_width * n_expert
    query_normed = query_raw * lax.rsqrt(query_sums[:, None] / full_width + EPSILON) * query_gain
    key_normed = key_raw * lax.rsqrt(key_sums[:, None] / full_width + EPSILON) * key_gain
    lengths = cached_lengths[0]
    starts = visible_from[0]
    first_flag = (jnp.arange(REQ, dtype=jnp.int32) == 0).astype(jnp.int32)
    offsets = lengths + far_lengths[group_id] * first_flag
    position = (
        (offsets[:, None] + jnp.arange(SPAN, dtype=jnp.int32)[None, :])
        .reshape(-1)
        .astype(jnp.float32)
    )
    queries = (
        rotate(query_normed.reshape(-1, heads_here, HD), position)
        .astype(jnp.bfloat16)
        .reshape(REQ, SPAN, heads_here, HD)
    )
    new_keys = (
        rotate(key_normed.reshape(-1, heads_here, HD), position)
        .astype(jnp.bfloat16)
        .reshape(REQ, SPAN, heads_here, HD)
    )
    cache_slots = MAXP * PAGE
    pool_size = key_pages.shape[0]
    page_pick = (
        page_table[0][:, :, None] == jnp.arange(pool_size, dtype=jnp.int32)[None, None, :]
    ).astype(jnp.bfloat16)
    own_keys = jnp.einsum(
        "rpq,qsc->rpsc", page_pick, key_pages, preferred_element_type=jnp.float32
    ).astype(jnp.bfloat16).reshape(REQ, cache_slots, local_width)
    own_values = jnp.einsum(
        "rpq,qsc->rpsc", page_pick, value_pages, preferred_element_type=jnp.float32
    ).astype(jnp.bfloat16).reshape(REQ, cache_slots, local_width)
    own_values, out_weight = lax.optimization_barrier((own_values, out_weight))
    full_out_weight = lax.all_gather(out_weight, HEAD_AXES, axis=0, tiled=True)
    far_stack = jnp.stack([key_pages[far_table[0]], value_pages[far_table[0]]])
    received = from_partner(far_stack, "group", 0).reshape(2, cache_slots, local_width)
    cache_pos = jnp.arange(cache_slots, dtype=jnp.int32)
    own_visible = (cache_pos[None, :] < lengths[:, None]) & (cache_pos[None, :] >= starts[:, None])
    far_visible = cache_pos < far_lengths[group_id]
    causal = jnp.arange(SPAN)[:, None] >= jnp.arange(SPAN)[None, :]
    is_first = (jnp.arange(REQ) == 0)[:, None, None]
    new_keys = new_keys.reshape(REQ, SPAN, local_width)
    new_values = new_values.reshape(REQ, SPAN, local_width)
    queries = queries.reshape(REQ, SPAN, local_width)
    scale = math.sqrt(HD)
    head_outs = []
    for head in range(heads_here):
        cols = slice(head * HD, (head + 1) * HD)
        q = queries[:, :, cols]
        s_own = jnp.einsum("rcd,rld->rcl", q, own_keys[:, :, cols], preferred_element_type=jnp.float32) / scale
        s_new = jnp.einsum("rcd,rjd->rcj", q, new_keys[:, :, cols], preferred_element_type=jnp.float32) / scale
        s_far = jnp.einsum("cd,ld->cl", q[0], received[0][:, cols], preferred_element_type=jnp.float32) / scale
        s_own = jnp.where(own_visible[:, None, :], s_own, MASKED)
        s_new = jnp.where(causal[None], s_new, MASKED)
        s_far = jnp.where(far_visible[None, :], s_far, MASKED)
        far_max = jnp.max(s_far, axis=-1, keepdims=True)
        row_max = jnp.maximum(
            jnp.max(s_own, axis=-1, keepdims=True), jnp.max(s_new, axis=-1, keepdims=True)
        )
        row_max = jnp.where(is_first, jnp.maximum(row_max, far_max[None]), row_max)
        p_own = jnp.where(own_visible[:, None, :], jnp.exp(s_own - row_max), 0.0)
        p_new = jnp.where(causal[None], jnp.exp(s_new - row_max), 0.0)
        p_far = jnp.where(far_visible[None, :], jnp.exp(s_far - row_max[0]), 0.0)
        total = jnp.sum(p_own, axis=-1, keepdims=True) + jnp.sum(p_new, axis=-1, keepdims=True)
        total = jnp.where(is_first, total + jnp.sum(p_far, axis=-1, keepdims=True)[None], total)
        w_own = (p_own / total).astype(jnp.bfloat16)
        w_new = (p_new / total).astype(jnp.bfloat16)
        w_far = (p_far / total[0]).astype(jnp.bfloat16)
        ctx = jnp.einsum("rcl,rld->rcd", w_own, own_values[:, :, cols], preferred_element_type=jnp.float32)
        ctx = ctx + jnp.einsum("rcj,rjd->rcd", w_new, new_values[:, :, cols], preferred_element_type=jnp.float32)
        far_ctx = jnp.einsum("cl,ld->cd", w_far, received[1][:, cols], preferred_element_type=jnp.float32)
        ctx = ctx + jnp.where(is_first, far_ctx[None], 0.0)
        head_outs.append(ctx.astype(jnp.bfloat16))
    context = jnp.concatenate(head_outs, axis=-1)
    token_context = lax.all_to_all(
        context, HEAD_AXES, split_axis=0, concat_axis=2, tiled=True
    ).reshape(SPAN, -1)
    attended = jnp.dot(token_context, full_out_weight, preferred_element_type=jnp.float32)
    residual = (as_float + attended).astype(jnp.bfloat16)
    moe_in = rms_norm(residual.astype(jnp.float32), feedforward_gain).astype(jnp.bfloat16)
    row_count = tokens.shape[0]
    n_chip = lax.axis_size(("group", "x"))
    capacity = row_count * TOP * 3 // (2 * EXPERTS)
    slots = EXPERTS * capacity
    flat_routes = routes.reshape(-1)
    onehot = (flat_routes[:, None] == jnp.arange(EXPERTS, dtype=jnp.int32)[None, :]).astype(
        jnp.int32
    )
    earlier = jnp.cumsum(onehot, axis=0) - onehot
    slot_index = jnp.sum(earlier * onehot, axis=1)
    position_of = (flat_routes * capacity + slot_index).reshape(row_count, TOP)
    slot_ids = jnp.arange(slots, dtype=jnp.int32).reshape(EXPERTS, capacity)
    picks = position_of[None, None, :, :] == slot_ids[:, :, None, None]
    dispatch = jnp.any(picks, axis=3).astype(jnp.bfloat16)
    lanes = 128
    bands = D // lanes
    tiled_in = moe_in.reshape(row_count, bands, lanes)
    buffer = jnp.einsum(
        "est,tjl->esjl", dispatch, tiled_in, preferred_element_type=jnp.float32
    ).astype(jnp.bfloat16)

    def exchange(blocks):
        flat = blocks.reshape(n_chip, capacity * bands, lanes)
        moved = lax.all_to_all(flat, ("group", "x"), split_axis=0, concat_axis=0, tiled=True)
        return moved.reshape(n_chip, capacity, bands, lanes)

    incoming = exchange(buffer)
    gate_act = jnp.einsum("esjl,jlf->esf", incoming, gate_full.reshape(bands, lanes, -1), preferred_element_type=jnp.float32)
    up_act = jnp.einsum("esjl,jlf->esf", incoming, up_full.reshape(bands, lanes, -1), preferred_element_type=jnp.float32)
    hidden = (jax.nn.silu(gate_act) * up_act).astype(jnp.bfloat16)
    expert_rows = jnp.einsum(
        "esf,fjl->esjl", hidden, down_full.reshape(-1, bands, lanes), preferred_element_type=jnp.float32
    ).astype(jnp.bfloat16)
    returned = exchange(expert_rows)
    combine = jnp.sum(jnp.where(picks, route_weights[None, None, :, :], 0.0), axis=3)
    moe_out = jnp.einsum(
        "est,esjl->tjl",
        combine,
        returned.astype(jnp.float32),
        precision=lax.Precision.HIGHEST,
        preferred_element_type=jnp.float32,
    ).reshape(row_count, D)
    return (residual.astype(jnp.float32) + moe_out).astype(jnp.bfloat16)


def solution(mesh):
    n_group, n_expert = mesh.devices.shape
    chip_mesh = jax.sharding.Mesh(
        mesh.devices.reshape(n_group, n_expert // 2, 2), ("group", "x", "core")
    )
    everyone = ("group", "x", "core")
    return jax.shard_map(
        body,
        mesh=chip_mesh,
        in_specs=(
            P(everyone, None),
            P(),
            P(None, HEAD_AXES),
            P(None, HEAD_AXES),
            P(None, HEAD_AXES),
            P(HEAD_AXES),
            P(HEAD_AXES),
            P(HEAD_AXES, None),
            P("group", None, HEAD_AXES),
            P("group", None, HEAD_AXES),
            P("group", None, None),
            P("group", None),
            P("group", None),
            P(),
            P("group", None),
            P(),
            P(everyone, None),
            P(everyone, None),
            P(None, everyone),
            P(None, everyone),
            P(everyone, None),
        ),
        out_specs=P(everyone, None),
        check_vma=False,
    )
```

```python
import math

import jax
import jax.numpy as jnp
from jax import lax
from jax.sharding import PartitionSpec as P

D = 2048
HD = 128
EXPERTS = 64
TOP = 8
PAGE = 128
REQ = 8
SPAN = 64
MAXP = 12


EPSILON = 1e-05
MASKED = -1e30
HEAD_AXES = ("x", "core")


def from_partner(value, axis, bit):
    mask = 2**bit
    pairs = [(source, source ^ mask) for source in range(lax.axis_size(axis))]
    return lax.ppermute(value, axis, pairs)


def rms_norm(values, norm_gain):
    return (
        values * lax.rsqrt(jnp.mean(values * values, axis=-1, keepdims=True) + EPSILON) * norm_gain
    )


def rotate(values, position):
    half_width = values.shape[-1] // 2
    inverse_freq = 10000.0 ** (-2.0 * jnp.arange(half_width, dtype=jnp.float32) / values.shape[-1])
    angles = position[:, None] * inverse_freq[None, :]
    cosine = jnp.cos(angles)[:, None, :]
    sine_part = jnp.sin(angles)[:, None, :]
    first_part = values[..., :half_width]
    second = values[..., half_width:]
    return jnp.concatenate(
        [first_part * cosine - second * sine_part, second * cosine + first_part * sine_part],
        axis=-1,
    )


def masked_scores(queries, key_rows, allowed):
    scores = jnp.einsum(
        "chd,lhd->hcl", queries, key_rows, preferred_element_type=jnp.float32
    ) / math.sqrt(queries.shape[-1])
    return jnp.where(allowed[None], scores, MASKED)


def attend(queries, key_rows, value_rows, allowed):
    scores = masked_scores(queries, key_rows, allowed)
    row_max = jnp.max(scores, axis=-1, keepdims=True)
    raised = jnp.where(allowed[None], jnp.exp(scores - row_max), 0.0)
    weights = (raised / jnp.sum(raised, axis=-1, keepdims=True)).astype(jnp.bfloat16)
    return jnp.einsum("hcl,lhd->chd", weights, value_rows, preferred_element_type=jnp.float32)


def body(
    tokens,
    attention_gain,
    query_weight,
    key_weight,
    value_weight,
    query_gain,
    key_gain,
    out_weight,
    key_pages,
    value_pages,
    page_table,
    far_table,
    cached_lengths,
    far_lengths,
    visible_from,
    feedforward_gain,
    routes,
    route_weights,
    gate_weight,
    up_weight,
    down_weight,
):
    n_group = lax.axis_size("group")
    n_expert = lax.axis_size(HEAD_AXES)
    group_id = lax.axis_index("group")
    as_float = tokens.astype(jnp.float32)
    normed = rms_norm(as_float, attention_gain).astype(jnp.bfloat16)
    row_block = lax.all_gather(normed, HEAD_AXES, axis=0, tiled=True)
    swap = [(0, 1), (1, 0)]
    gate_full = jnp.concatenate([gate_weight, lax.ppermute(gate_weight, "core", swap)], axis=1)
    up_full = jnp.concatenate([up_weight, lax.ppermute(up_weight, "core", swap)], axis=1)
    down_full = jnp.concatenate([down_weight, lax.ppermute(down_weight, "core", swap)], axis=0)
    joined = jnp.concatenate(
        [
            jnp.dot(row_block, query_weight, preferred_element_type=jnp.float32),
            jnp.dot(row_block, key_weight, preferred_element_type=jnp.float32),
            jnp.dot(row_block, value_weight, preferred_element_type=jnp.float32),
        ],
        axis=1,
    )
    local_width = query_weight.shape[1]
    heads_here = local_width // HD
    query_raw = joined[:, :local_width]
    key_raw = joined[:, local_width : 2 * local_width]
    new_values = (
        joined[:, 2 * local_width :].astype(jnp.bfloat16).reshape(REQ, SPAN, heads_here, HD)
    )
    query_sums, key_sums = lax.psum(
        (jnp.sum(query_raw * query_raw, axis=1), jnp.sum(key_raw * key_raw, axis=1)), HEAD_AXES
    )
    full_width = local_width * n_expert
    query_normed = query_raw * lax.rsqrt(query_sums[:, None] / full_width + EPSILON) * query_gain
    key_normed = key_raw * lax.rsqrt(key_sums[:, None] / full_width + EPSILON) * key_gain
    lengths = cached_lengths[0]
    starts = visible_from[0]
    first_flag = (jnp.arange(REQ, dtype=jnp.int32) == 0).astype(jnp.int32)
    offsets = lengths + far_lengths[group_id] * first_flag
    position = (
        (offsets[:, None] + jnp.arange(SPAN, dtype=jnp.int32)[None, :])
        .reshape(-1)
        .astype(jnp.float32)
    )
    queries = (
        rotate(query_normed.reshape(-1, heads_here, HD), position)
        .astype(jnp.bfloat16)
        .reshape(REQ, SPAN, heads_here, HD)
    )
    new_keys = (
        rotate(key_normed.reshape(-1, heads_here, HD), position)
        .astype(jnp.bfloat16)
        .reshape(REQ, SPAN, heads_here, HD)
    )
    cache_slots = MAXP * PAGE
    pool_size = key_pages.shape[0]
    page_pick = (
        page_table[0][:, :, None] == jnp.arange(pool_size, dtype=jnp.int32)[None, None, :]
    ).astype(jnp.bfloat16)
    own_keys = jnp.einsum(
        "rpq,qsc->rpsc", page_pick, key_pages, preferred_element_type=jnp.float32
    ).astype(jnp.bfloat16)
    own_values = jnp.einsum(
        "rpq,qsc->rpsc", page_pick, value_pages, preferred_element_type=jnp.float32
    ).astype(jnp.bfloat16)
    own_values, out_weight = lax.optimization_barrier((own_values, out_weight))
    full_out_weight = lax.all_gather(out_weight, HEAD_AXES, axis=0, tiled=True)
    far_stack = jnp.stack([key_pages[far_table[0]], value_pages[far_table[0]]])
    received = from_partner(far_stack, "group", 0).reshape(2, cache_slots, local_width)
    cache_pos = jnp.arange(cache_slots, dtype=jnp.int32)
    own_visible = (
        (cache_pos[None, :] < lengths[:, None]) & (cache_pos[None, :] >= starts[:, None])
    ).reshape(REQ, 1, MAXP, PAGE)
    far_visible = cache_pos < far_lengths[group_id]
    causal = jnp.arange(SPAN)[:, None] >= jnp.arange(SPAN)[None, :]
    is_first = (jnp.arange(REQ) == 0)[:, None, None]
    new_keys = new_keys.reshape(REQ, SPAN, local_width)
    new_values = new_values.reshape(REQ, SPAN, local_width)
    queries = queries.reshape(REQ, SPAN, local_width)
    scale = math.sqrt(HD)
    head_outs = []
    for head in range(heads_here):
        cols = slice(head * HD, (head + 1) * HD)
        q = queries[:, :, cols]
        s_own = jnp.einsum("rcd,rpsd->rcps", q, own_keys[..., cols], preferred_element_type=jnp.float32) / scale
        s_new = jnp.einsum("rcd,rjd->rcj", q, new_keys[:, :, cols], preferred_element_type=jnp.float32) / scale
        s_far = jnp.einsum("cd,ld->cl", q[0], received[0][:, cols], preferred_element_type=jnp.float32) / scale
        s_own = jnp.where(own_visible, s_own, MASKED)
        s_new = jnp.where(causal[None], s_new, MASKED)
        s_far = jnp.where(far_visible[None, :], s_far, MASKED)
        far_max = jnp.max(s_far, axis=-1, keepdims=True)
        row_max = jnp.maximum(
            jnp.max(s_own, axis=(2, 3))[..., None], jnp.max(s_new, axis=-1, keepdims=True)
        )
        row_max = jnp.where(is_first, jnp.maximum(row_max, far_max[None]), row_max)
        p_own = jnp.where(own_visible, jnp.exp(s_own - row_max[..., None]), 0.0)
        p_new = jnp.where(causal[None], jnp.exp(s_new - row_max), 0.0)
        p_far = jnp.where(far_visible[None, :], jnp.exp(s_far - row_max[0]), 0.0)
        total = jnp.sum(p_own, axis=(2, 3))[..., None] + jnp.sum(p_new, axis=-1, keepdims=True)
        total = jnp.where(is_first, total + jnp.sum(p_far, axis=-1, keepdims=True)[None], total)
        w_own = (p_own / total[..., None]).astype(jnp.bfloat16)
        w_new = (p_new / total).astype(jnp.bfloat16)
        w_far = (p_far / total[0]).astype(jnp.bfloat16)
        ctx = jnp.einsum("rcps,rpsd->rcd", w_own, own_values[..., cols], preferred_element_type=jnp.float32)
        ctx = ctx + jnp.einsum("rcj,rjd->rcd", w_new, new_values[:, :, cols], preferred_element_type=jnp.float32)
        far_ctx = jnp.einsum("cl,ld->cd", w_far, received[1][:, cols], preferred_element_type=jnp.float32)
        ctx = ctx + jnp.where(is_first, far_ctx[None], 0.0)
        head_outs.append(ctx.astype(jnp.bfloat16))
    context = jnp.concatenate(head_outs, axis=-1)
    token_context = lax.all_to_all(
        context, HEAD_AXES, split_axis=0, concat_axis=2, tiled=True
    ).reshape(SPAN, -1)
    attended = jnp.dot(token_context, full_out_weight, preferred_element_type=jnp.float32)
    residual = (as_float + attended).astype(jnp.bfloat16)
    moe_in = rms_norm(residual.astype(jnp.float32), feedforward_gain).astype(jnp.bfloat16)
    row_count = tokens.shape[0]
    n_chip = lax.axis_size(("group", "x"))
    capacity = row_count * TOP * 3 // (2 * EXPERTS)
    slots = EXPERTS * capacity
    flat_routes = routes.reshape(-1)
    onehot = (flat_routes[:, None] == jnp.arange(EXPERTS, dtype=jnp.int32)[None, :]).astype(
        jnp.int32
    )
    earlier = jnp.cumsum(onehot, axis=0) - onehot
    slot_index = jnp.sum(earlier * onehot, axis=1)
    position_of = (flat_routes * capacity + slot_index).reshape(row_count, TOP)
    slot_ids = jnp.arange(slots, dtype=jnp.int32).reshape(EXPERTS, capacity)
    picks = position_of[None, None, :, :] == slot_ids[:, :, None, None]
    lanes = 128
    bands = D // lanes
    token_ids = jnp.arange(row_count, dtype=jnp.int32)[None, None, :, None]
    slot_token = jnp.sum(jnp.where(picks, token_ids, 0), axis=(2, 3)) + jnp.where(
        jnp.any(picks, axis=(2, 3)), 0, row_count
    )
    padded_in = jnp.concatenate([moe_in, jnp.zeros((1, D), moe_in.dtype)], axis=0)
    buffer = padded_in.reshape(row_count + 1, bands, lanes)[slot_token]

    def exchange(blocks):
        flat = blocks.reshape(n_chip, capacity * bands, lanes)
        moved = lax.all_to_all(flat, ("group", "x"), split_axis=0, concat_axis=0, tiled=True)
        return moved.reshape(n_chip, capacity, bands, lanes)

    incoming = exchange(buffer)
    gate_act = jnp.einsum("esjl,jlf->esf", incoming, gate_full.reshape(bands, lanes, -1), preferred_element_type=jnp.float32)
    up_act = jnp.einsum("esjl,jlf->esf", incoming, up_full.reshape(bands, lanes, -1), preferred_element_type=jnp.float32)
    hidden = (jax.nn.silu(gate_act) * up_act).astype(jnp.bfloat16)
    expert_rows = jnp.einsum(
        "esf,fjl->esjl", hidden, down_full.reshape(-1, bands, lanes), preferred_element_type=jnp.float32
    ).astype(jnp.bfloat16)
    returned = exchange(expert_rows)
    picked = returned.reshape(slots, bands, lanes)[position_of]
    moe_out = jnp.sum(
        route_weights[:, :, None, None] * picked.astype(jnp.float32), axis=1
    ).reshape(row_count, D)
    return (residual.astype(jnp.float32) + moe_out).astype(jnp.bfloat16)


def solution(mesh):
    n_group, n_expert = mesh.devices.shape
    chip_mesh = jax.sharding.Mesh(
        mesh.devices.reshape(n_group, n_expert // 2, 2), ("group", "x", "core")
    )
    everyone = ("group", "x", "core")
    return jax.shard_map(
        body,
        mesh=chip_mesh,
        in_specs=(
            P(everyone, None),
            P(),
            P(None, HEAD_AXES),
            P(None, HEAD_AXES),
            P(None, HEAD_AXES),
            P(HEAD_AXES),
            P(HEAD_AXES),
            P(HEAD_AXES, None),
            P("group", None, HEAD_AXES),
            P("group", None, HEAD_AXES),
            P("group", None, None),
            P("group", None),
            P("group", None),
            P(),
            P("group", None),
            P(),
            P(everyone, None),
            P(everyone, None),
            P(None, everyone),
            P(None, everyone),
            P(everyone, None),
        ),
        out_specs=P(everyone, None),
        check_vma=False,
    )
```

```python
import math

import jax
import jax.numpy as jnp
from jax import lax
from jax.sharding import PartitionSpec as P

D = 2048
HD = 128
EXPERTS = 64
TOP = 8
PAGE = 128
REQ = 8
SPAN = 64
MAXP = 12


EPSILON = 1e-05
MASKED = -1e30
HEAD_AXES = ("x", "core")


def from_partner(value, axis, bit):
    mask = 2**bit
    pairs = [(source, source ^ mask) for source in range(lax.axis_size(axis))]
    return lax.ppermute(value, axis, pairs)


def rms_norm(values, norm_gain):
    return (
        values * lax.rsqrt(jnp.mean(values * values, axis=-1, keepdims=True) + EPSILON) * norm_gain
    )


def rotate(values, position):
    half_width = values.shape[-1] // 2
    inverse_freq = 10000.0 ** (-2.0 * jnp.arange(half_width, dtype=jnp.float32) / values.shape[-1])
    angles = position[:, None] * inverse_freq[None, :]
    cosine = jnp.cos(angles)[:, None, :]
    sine_part = jnp.sin(angles)[:, None, :]
    first_part = values[..., :half_width]
    second = values[..., half_width:]
    return jnp.concatenate(
        [first_part * cosine - second * sine_part, second * cosine + first_part * sine_part],
        axis=-1,
    )


def masked_scores(queries, key_rows, allowed):
    scores = jnp.einsum(
        "chd,lhd->hcl", queries, key_rows, preferred_element_type=jnp.float32
    ) / math.sqrt(queries.shape[-1])
    return jnp.where(allowed[None], scores, MASKED)


def attend(queries, key_rows, value_rows, allowed):
    scores = masked_scores(queries, key_rows, allowed)
    row_max = jnp.max(scores, axis=-1, keepdims=True)
    raised = jnp.where(allowed[None], jnp.exp(scores - row_max), 0.0)
    weights = (raised / jnp.sum(raised, axis=-1, keepdims=True)).astype(jnp.bfloat16)
    return jnp.einsum("hcl,lhd->chd", weights, value_rows, preferred_element_type=jnp.float32)


def body(
    tokens,
    attention_gain,
    query_weight,
    key_weight,
    value_weight,
    query_gain,
    key_gain,
    out_weight,
    key_pages,
    value_pages,
    page_table,
    far_table,
    cached_lengths,
    far_lengths,
    visible_from,
    feedforward_gain,
    routes,
    route_weights,
    gate_weight,
    up_weight,
    down_weight,
):
    n_group = lax.axis_size("group")
    n_expert = lax.axis_size(HEAD_AXES)
    group_id = lax.axis_index("group")
    as_float = tokens.astype(jnp.float32)
    normed = rms_norm(as_float, attention_gain).astype(jnp.bfloat16)
    row_block = lax.all_gather(normed, HEAD_AXES, axis=0, tiled=True)
    swap = [(0, 1), (1, 0)]
    gate_full = jnp.concatenate([gate_weight, lax.ppermute(gate_weight, "core", swap)], axis=1)
    up_full = jnp.concatenate([up_weight, lax.ppermute(up_weight, "core", swap)], axis=1)
    down_full = jnp.concatenate([down_weight, lax.ppermute(down_weight, "core", swap)], axis=0)
    joined = jnp.concatenate(
        [
            jnp.dot(row_block, query_weight, preferred_element_type=jnp.float32),
            jnp.dot(row_block, key_weight, preferred_element_type=jnp.float32),
            jnp.dot(row_block, value_weight, preferred_element_type=jnp.float32),
        ],
        axis=1,
    )
    local_width = query_weight.shape[1]
    heads_here = local_width // HD
    query_raw = joined[:, :local_width]
    key_raw = joined[:, local_width : 2 * local_width]
    new_values = (
        joined[:, 2 * local_width :].astype(jnp.bfloat16).reshape(REQ, SPAN, heads_here, HD)
    )
    query_sums, key_sums = lax.psum(
        (jnp.sum(query_raw * query_raw, axis=1), jnp.sum(key_raw * key_raw, axis=1)), HEAD_AXES
    )
    full_width = local_width * n_expert
    query_normed = query_raw * lax.rsqrt(query_sums[:, None] / full_width + EPSILON) * query_gain
    key_normed = key_raw * lax.rsqrt(key_sums[:, None] / full_width + EPSILON) * key_gain
    lengths = cached_lengths[0]
    starts = visible_from[0]
    first_flag = (jnp.arange(REQ, dtype=jnp.int32) == 0).astype(jnp.int32)
    offsets = lengths + far_lengths[group_id] * first_flag
    position = (
        (offsets[:, None] + jnp.arange(SPAN, dtype=jnp.int32)[None, :])
        .reshape(-1)
        .astype(jnp.float32)
    )
    queries = (
        rotate(query_normed.reshape(-1, heads_here, HD), position)
        .astype(jnp.bfloat16)
        .reshape(REQ, SPAN, heads_here, HD)
    )
    new_keys = (
        rotate(key_normed.reshape(-1, heads_here, HD), position)
        .astype(jnp.bfloat16)
        .reshape(REQ, SPAN, heads_here, HD)
    )
    cache_slots = MAXP * PAGE
    pool_size = key_pages.shape[0]
    page_pick = (
        page_table[0][:, :, None] == jnp.arange(pool_size, dtype=jnp.int32)[None, None, :]
    ).astype(jnp.bfloat16)
    own_keys = jnp.einsum(
        "rpq,qsc->rpsc", page_pick, key_pages, preferred_element_type=jnp.float32
    ).astype(jnp.bfloat16).reshape(REQ, cache_slots, local_width)
    own_values = jnp.einsum(
        "rpq,qsc->rpsc", page_pick, value_pages, preferred_element_type=jnp.float32
    ).astype(jnp.bfloat16).reshape(REQ, cache_slots, local_width)
    own_values, out_weight = lax.optimization_barrier((own_values, out_weight))
    full_out_weight = lax.all_gather(out_weight, HEAD_AXES, axis=0, tiled=True)
    far_stack = jnp.stack([key_pages[far_table[0]], value_pages[far_table[0]]])
    received = from_partner(far_stack, "group", 0).reshape(2, cache_slots, local_width)
    cache_pos = jnp.arange(cache_slots, dtype=jnp.int32)
    own_visible = (cache_pos[None, :] < lengths[:, None]) & (cache_pos[None, :] >= starts[:, None])
    far_visible = cache_pos < far_lengths[group_id]
    causal = jnp.arange(SPAN)[:, None] >= jnp.arange(SPAN)[None, :]
    is_first = (jnp.arange(REQ) == 0)[:, None, None]
    new_keys = new_keys.reshape(REQ, SPAN, local_width)
    new_values = new_values.reshape(REQ, SPAN, local_width)
    queries = queries.reshape(REQ, SPAN, local_width)
    scale = math.sqrt(HD)
    head_outs = []
    for head in range(heads_here):
        cols = slice(head * HD, (head + 1) * HD)
        q = queries[:, :, cols]
        s_own = jnp.einsum("rcd,rld->rcl", q, own_keys[:, :, cols], preferred_element_type=jnp.float32) / scale
        s_new = jnp.einsum("rcd,rjd->rcj", q, new_keys[:, :, cols], preferred_element_type=jnp.float32) / scale
        s_far = jnp.einsum("cd,ld->cl", q[0], received[0][:, cols], preferred_element_type=jnp.float32) / scale
        s_own = jnp.where(own_visible[:, None, :], s_own, MASKED)
        s_new = jnp.where(causal[None], s_new, MASKED)
        s_far = jnp.where(far_visible[None, :], s_far, MASKED)
        far_max = jnp.max(s_far, axis=-1, keepdims=True)
        row_max = jnp.maximum(
            jnp.max(s_own, axis=-1, keepdims=True), jnp.max(s_new, axis=-1, keepdims=True)
        )
        row_max = jnp.where(is_first, jnp.maximum(row_max, far_max[None]), row_max)
        p_own = jnp.where(own_visible[:, None, :], jnp.exp(s_own - row_max), 0.0)
        p_new = jnp.where(causal[None], jnp.exp(s_new - row_max), 0.0)
        p_far = jnp.where(far_visible[None, :], jnp.exp(s_far - row_max[0]), 0.0)
        total = jnp.sum(p_own, axis=-1, keepdims=True) + jnp.sum(p_new, axis=-1, keepdims=True)
        total = jnp.where(is_first, total + jnp.sum(p_far, axis=-1, keepdims=True)[None], total)
        w_own = (p_own / total).astype(jnp.bfloat16)
        w_new = (p_new / total).astype(jnp.bfloat16)
        w_far = (p_far / total[0]).astype(jnp.bfloat16)
        ctx = jnp.einsum("rcl,rld->rcd", w_own, own_values[:, :, cols], preferred_element_type=jnp.float32)
        ctx = ctx + jnp.einsum("rcj,rjd->rcd", w_new, new_values[:, :, cols], preferred_element_type=jnp.float32)
        far_ctx = jnp.einsum("cl,ld->cd", w_far, received[1][:, cols], preferred_element_type=jnp.float32)
        ctx = ctx + jnp.where(is_first, far_ctx[None], 0.0)
        head_outs.append(ctx.astype(jnp.bfloat16))
    context = jnp.concatenate(head_outs, axis=-1)
    token_context = lax.all_to_all(
        context, HEAD_AXES, split_axis=0, concat_axis=2, tiled=True
    ).reshape(SPAN, -1)
    attended = jnp.dot(token_context, full_out_weight, preferred_element_type=jnp.float32)
    residual = (as_float + attended).astype(jnp.bfloat16)
    moe_in = rms_norm(residual.astype(jnp.float32), feedforward_gain).astype(jnp.bfloat16)
    row_count = tokens.shape[0]
    n_chip = lax.axis_size(("group", "x"))
    capacity = row_count * TOP * 3 // (2 * EXPERTS)
    slots = EXPERTS * capacity
    flat_routes = routes.reshape(-1)
    onehot = (flat_routes[:, None] == jnp.arange(EXPERTS, dtype=jnp.int32)[None, :]).astype(
        jnp.int32
    )
    earlier = jnp.cumsum(onehot, axis=0) - onehot
    slot_index = jnp.sum(earlier * onehot, axis=1)
    position_of = (flat_routes * capacity + slot_index).reshape(row_count, TOP)
    slot_ids = jnp.arange(slots, dtype=jnp.int32).reshape(EXPERTS, capacity)
    picks = position_of[None, None, :, :] == slot_ids[:, :, None, None]
    lanes = 128
    bands = D // lanes
    token_ids = jnp.arange(row_count, dtype=jnp.int32)[None, None, :, None]
    slot_token = jnp.sum(jnp.where(picks, token_ids, 0), axis=(2, 3)) + jnp.where(
        jnp.any(picks, axis=(2, 3)), 0, row_count
    )
    padded_in = jnp.concatenate([moe_in, jnp.zeros((1, D), moe_in.dtype)], axis=0)
    buffer = padded_in.reshape(row_count + 1, bands, lanes)[slot_token]

    def exchange(blocks):
        flat = blocks.reshape(n_chip, capacity * bands, lanes)
        moved = lax.all_to_all(flat, ("group", "x"), split_axis=0, concat_axis=0, tiled=True)
        return moved.reshape(n_chip, capacity, bands, lanes)

    incoming = exchange(buffer)
    gate_act = jnp.einsum("esjl,jlf->esf", incoming, gate_full.reshape(bands, lanes, -1), preferred_element_type=jnp.float32)
    up_act = jnp.einsum("esjl,jlf->esf", incoming, up_full.reshape(bands, lanes, -1), preferred_element_type=jnp.float32)
    hidden = (jax.nn.silu(gate_act) * up_act).astype(jnp.bfloat16)
    expert_rows = jnp.einsum(
        "esf,fjl->esjl", hidden, down_full.reshape(-1, bands, lanes), preferred_element_type=jnp.float32
    ).astype(jnp.bfloat16)
    returned = exchange(expert_rows)
    picked = returned.reshape(slots, bands, lanes)[position_of]
    moe_out = jnp.sum(
        route_weights[:, :, None, None] * picked.astype(jnp.float32), axis=1
    ).reshape(row_count, D)
    return (residual.astype(jnp.float32) + moe_out).astype(jnp.bfloat16)


def solution(mesh):
    n_group, n_expert = mesh.devices.shape
    chip_mesh = jax.sharding.Mesh(
        mesh.devices.reshape(n_group, n_expert // 2, 2), ("group", "x", "core")
    )
    everyone = ("group", "x", "core")
    return jax.shard_map(
        body,
        mesh=chip_mesh,
        in_specs=(
            P(everyone, None),
            P(),
            P(None, HEAD_AXES),
            P(None, HEAD_AXES),
            P(None, HEAD_AXES),
            P(HEAD_AXES),
            P(HEAD_AXES),
            P(HEAD_AXES, None),
            P("group", None, HEAD_AXES),
            P("group", None, HEAD_AXES),
            P("group", None, None),
            P("group", None),
            P("group", None),
            P(),
            P("group", None),
            P(),
            P(everyone, None),
            P(everyone, None),
            P(None, everyone),
            P(None, everyone),
            P(everyone, None),
        ),
        out_specs=P(everyone, None),
        check_vma=False,
    )
```

```python
import math

import jax
import jax.numpy as jnp
from jax import lax
from jax.sharding import PartitionSpec as P

D = 2048
HD = 128
EXPERTS = 64
TOP = 8
PAGE = 128
REQ = 8
SPAN = 64
MAXP = 12


EPSILON = 1e-05
MASKED = -1e30
HEAD_AXES = ("x", "core")


def from_partner(value, axis, bit):
    mask = 2**bit
    pairs = [(source, source ^ mask) for source in range(lax.axis_size(axis))]
    return lax.ppermute(value, axis, pairs)


def rms_norm(values, norm_gain):
    return (
        values * lax.rsqrt(jnp.mean(values * values, axis=-1, keepdims=True) + EPSILON) * norm_gain
    )


def rotate(values, position):
    half_width = values.shape[-1] // 2
    inverse_freq = 10000.0 ** (-2.0 * jnp.arange(half_width, dtype=jnp.float32) / values.shape[-1])
    angles = position[:, None] * inverse_freq[None, :]
    cosine = jnp.cos(angles)[:, None, :]
    sine_part = jnp.sin(angles)[:, None, :]
    first_part = values[..., :half_width]
    second = values[..., half_width:]
    return jnp.concatenate(
        [first_part * cosine - second * sine_part, second * cosine + first_part * sine_part],
        axis=-1,
    )


def masked_scores(queries, key_rows, allowed):
    scores = jnp.einsum(
        "chd,lhd->hcl", queries, key_rows, preferred_element_type=jnp.float32
    ) / math.sqrt(queries.shape[-1])
    return jnp.where(allowed[None], scores, MASKED)


def attend(queries, key_rows, value_rows, allowed):
    scores = masked_scores(queries, key_rows, allowed)
    row_max = jnp.max(scores, axis=-1, keepdims=True)
    raised = jnp.where(allowed[None], jnp.exp(scores - row_max), 0.0)
    weights = (raised / jnp.sum(raised, axis=-1, keepdims=True)).astype(jnp.bfloat16)
    return jnp.einsum("hcl,lhd->chd", weights, value_rows, preferred_element_type=jnp.float32)


def body(
    tokens,
    attention_gain,
    query_weight,
    key_weight,
    value_weight,
    query_gain,
    key_gain,
    out_weight,
    key_pages,
    value_pages,
    page_table,
    far_table,
    cached_lengths,
    far_lengths,
    visible_from,
    feedforward_gain,
    routes,
    route_weights,
    gate_weight,
    up_weight,
    down_weight,
):
    n_group = lax.axis_size("group")
    n_expert = lax.axis_size(HEAD_AXES)
    group_id = lax.axis_index("group")
    as_float = tokens.astype(jnp.float32)
    normed = rms_norm(as_float, attention_gain).astype(jnp.bfloat16)
    row_block = lax.all_gather(normed, HEAD_AXES, axis=0, tiled=True)
    swap = [(0, 1), (1, 0)]
    gate_full = jnp.concatenate([gate_weight, lax.ppermute(gate_weight, "core", swap)], axis=1)
    up_full = jnp.concatenate([up_weight, lax.ppermute(up_weight, "core", swap)], axis=1)
    down_full = jnp.concatenate([down_weight, lax.ppermute(down_weight, "core", swap)], axis=0)
    joined = jnp.concatenate(
        [
            jnp.dot(row_block, query_weight, preferred_element_type=jnp.float32),
            jnp.dot(row_block, key_weight, preferred_element_type=jnp.float32),
            jnp.dot(row_block, value_weight, preferred_element_type=jnp.float32),
        ],
        axis=1,
    )
    local_width = query_weight.shape[1]
    heads_here = local_width // HD
    query_raw = joined[:, :local_width]
    key_raw = joined[:, local_width : 2 * local_width]
    new_values = (
        joined[:, 2 * local_width :].astype(jnp.bfloat16).reshape(REQ, SPAN, heads_here, HD)
    )
    query_sums, key_sums = lax.psum(
        (jnp.sum(query_raw * query_raw, axis=1), jnp.sum(key_raw * key_raw, axis=1)), HEAD_AXES
    )
    full_width = local_width * n_expert
    query_normed = query_raw * lax.rsqrt(query_sums[:, None] / full_width + EPSILON) * query_gain
    key_normed = key_raw * lax.rsqrt(key_sums[:, None] / full_width + EPSILON) * key_gain
    lengths = cached_lengths[0]
    starts = visible_from[0]
    first_flag = (jnp.arange(REQ, dtype=jnp.int32) == 0).astype(jnp.int32)
    offsets = lengths + far_lengths[group_id] * first_flag
    position = (
        (offsets[:, None] + jnp.arange(SPAN, dtype=jnp.int32)[None, :])
        .reshape(-1)
        .astype(jnp.float32)
    )
    queries = (
        rotate(query_normed.reshape(-1, heads_here, HD), position)
        .astype(jnp.bfloat16)
        .reshape(REQ, SPAN, heads_here, HD)
    )
    new_keys = (
        rotate(key_normed.reshape(-1, heads_here, HD), position)
        .astype(jnp.bfloat16)
        .reshape(REQ, SPAN, heads_here, HD)
    )
    cache_slots = MAXP * PAGE
    pool_size = key_pages.shape[0]
    page_pick = (
        page_table[0][:, :, None] == jnp.arange(pool_size, dtype=jnp.int32)[None, None, :]
    ).astype(jnp.bfloat16)
    own_keys = jnp.einsum(
        "rpq,qsc->rpsc", page_pick, key_pages, preferred_element_type=jnp.float32
    ).astype(jnp.bfloat16).reshape(REQ, cache_slots, local_width)
    own_values = jnp.einsum(
        "rpq,qsc->rpsc", page_pick, value_pages, preferred_element_type=jnp.float32
    ).astype(jnp.bfloat16).reshape(REQ, cache_slots, local_width)
    own_values, out_weight = lax.optimization_barrier((own_values, out_weight))
    full_out_weight = lax.all_gather(out_weight, HEAD_AXES, axis=0, tiled=True)
    far_stack = jnp.stack([key_pages[far_table[0]], value_pages[far_table[0]]])
    received = from_partner(far_stack, "group", 0).reshape(2, cache_slots, local_width)
    cache_pos = jnp.arange(cache_slots, dtype=jnp.int32)
    own_visible = (cache_pos[None, :] < lengths[:, None]) & (cache_pos[None, :] >= starts[:, None])
    far_visible = cache_pos < far_lengths[group_id]
    causal = jnp.arange(SPAN)[:, None] >= jnp.arange(SPAN)[None, :]
    is_first = (jnp.arange(REQ) == 0)[:, None, None]
    new_keys = new_keys.reshape(REQ, SPAN, local_width)
    new_values = new_values.reshape(REQ, SPAN, local_width)
    queries = queries.reshape(REQ, SPAN, local_width)
    scale = math.sqrt(HD)
    head_outs = []
    for head in range(heads_here):
        cols = slice(head * HD, (head + 1) * HD)
        q = queries[:, :, cols]
        s_own = jnp.einsum("rcd,rld->rcl", q, own_keys[:, :, cols], preferred_element_type=jnp.float32) / scale
        s_new = jnp.einsum("rcd,rjd->rcj", q, new_keys[:, :, cols], preferred_element_type=jnp.float32) / scale
        s_far = jnp.einsum("cd,ld->cl", q[0], received[0][:, cols], preferred_element_type=jnp.float32) / scale
        s_own = jnp.where(own_visible[:, None, :], s_own, MASKED)
        s_new = jnp.where(causal[None], s_new, MASKED)
        s_far = jnp.where(far_visible[None, :], s_far, MASKED)
        far_max = jnp.max(s_far, axis=-1, keepdims=True)
        row_max = jnp.maximum(
            jnp.max(s_own, axis=-1, keepdims=True), jnp.max(s_new, axis=-1, keepdims=True)
        )
        row_max = jnp.where(is_first, jnp.maximum(row_max, far_max[None]), row_max)
        p_own = jnp.where(own_visible[:, None, :], jnp.exp(s_own - row_max), 0.0)
        p_new = jnp.where(causal[None], jnp.exp(s_new - row_max), 0.0)
        p_far = jnp.where(far_visible[None, :], jnp.exp(s_far - row_max[0]), 0.0)
        total = jnp.sum(p_own, axis=-1, keepdims=True) + jnp.sum(p_new, axis=-1, keepdims=True)
        total = jnp.where(is_first, total + jnp.sum(p_far, axis=-1, keepdims=True)[None], total)
        w_own = (p_own / total).astype(jnp.bfloat16)
        w_new = (p_new / total).astype(jnp.bfloat16)
        w_far = (p_far / total[0]).astype(jnp.bfloat16)
        ctx = jnp.einsum("rcl,rld->rcd", w_own, own_values[:, :, cols], preferred_element_type=jnp.float32)
        ctx = ctx + jnp.einsum("rcj,rjd->rcd", w_new, new_values[:, :, cols], preferred_element_type=jnp.float32)
        far_ctx = jnp.einsum("cl,ld->cd", w_far, received[1][:, cols], preferred_element_type=jnp.float32)
        ctx = ctx + jnp.where(is_first, far_ctx[None], 0.0)
        head_outs.append(ctx.astype(jnp.bfloat16))
    context = jnp.concatenate(head_outs, axis=-1)
    token_context = lax.all_to_all(
        context, HEAD_AXES, split_axis=0, concat_axis=2, tiled=True
    ).reshape(SPAN, -1)
    attended = jnp.dot(token_context, full_out_weight, preferred_element_type=jnp.float32)
    residual = (as_float + attended).astype(jnp.bfloat16)
    moe_in = rms_norm(residual.astype(jnp.float32), feedforward_gain).astype(jnp.bfloat16)
    row_count = tokens.shape[0]
    n_chip = lax.axis_size(("group", "x"))
    capacity = row_count * TOP * 3 // (2 * EXPERTS)
    slots = EXPERTS * capacity
    flat_routes = routes.reshape(-1)
    onehot = (flat_routes[:, None] == jnp.arange(EXPERTS, dtype=jnp.int32)[None, :]).astype(
        jnp.int32
    )
    earlier = jnp.cumsum(onehot, axis=0) - onehot
    slot_index = jnp.sum(earlier * onehot, axis=1)
    position_of = (flat_routes * capacity + slot_index).reshape(row_count, TOP)
    slot_ids = jnp.arange(slots, dtype=jnp.int32).reshape(EXPERTS, capacity)
    picks = position_of[None, None, :, :] == slot_ids[:, :, None, None]
    lanes = 128
    bands = D // lanes
    token_ids = jnp.arange(row_count, dtype=jnp.int32)[None, None, :]
    taken = jnp.any(picks, axis=3)
    slot_token = jnp.sum(jnp.where(taken, token_ids, 0), axis=2) + jnp.where(
        jnp.any(taken, axis=2), 0, row_count
    )
    padded_in = jnp.concatenate([moe_in, jnp.zeros((1, D), moe_in.dtype)], axis=0)
    buffer = padded_in.reshape(row_count + 1, bands, lanes)[slot_token]

    def exchange(blocks):
        flat = blocks.reshape(n_chip, capacity * bands, lanes)
        moved = lax.all_to_all(flat, ("group", "x"), split_axis=0, concat_axis=0, tiled=True)
        return moved.reshape(n_chip, capacity, bands, lanes)

    incoming = exchange(buffer)
    gate_act = jnp.einsum("esjl,jlf->esf", incoming, gate_full.reshape(bands, lanes, -1), preferred_element_type=jnp.float32)
    up_act = jnp.einsum("esjl,jlf->esf", incoming, up_full.reshape(bands, lanes, -1), preferred_element_type=jnp.float32)
    hidden = (jax.nn.silu(gate_act) * up_act).astype(jnp.bfloat16)
    expert_rows = jnp.einsum(
        "esf,fjl->esjl", hidden, down_full.reshape(-1, bands, lanes), preferred_element_type=jnp.float32
    ).astype(jnp.bfloat16)
    returned = exchange(expert_rows)
    picked = returned.reshape(slots, bands, lanes)[position_of]
    moe_out = jnp.sum(
        route_weights[:, :, None, None] * picked.astype(jnp.float32), axis=1
    ).reshape(row_count, D)
    return (residual.astype(jnp.float32) + moe_out).astype(jnp.bfloat16)


def solution(mesh):
    n_group, n_expert = mesh.devices.shape
    chip_mesh = jax.sharding.Mesh(
        mesh.devices.reshape(n_group, n_expert // 2, 2), ("group", "x", "core")
    )
    everyone = ("group", "x", "core")
    return jax.shard_map(
        body,
        mesh=chip_mesh,
        in_specs=(
            P(everyone, None),
            P(),
            P(None, HEAD_AXES),
            P(None, HEAD_AXES),
            P(None, HEAD_AXES),
            P(HEAD_AXES),
            P(HEAD_AXES),
            P(HEAD_AXES, None),
            P("group", None, HEAD_AXES),
            P("group", None, HEAD_AXES),
            P("group", None, None),
            P("group", None),
            P("group", None),
            P(),
            P("group", None),
            P(),
            P(everyone, None),
            P(everyone, None),
            P(None, everyone),
            P(None, everyone),
            P(everyone, None),
        ),
        out_specs=P(everyone, None),
        check_vma=False,
    )
```

```python
import math

import jax
import jax.numpy as jnp
from jax import lax
from jax.sharding import PartitionSpec as P

D = 2048
HD = 128
EXPERTS = 64
TOP = 8
PAGE = 128
REQ = 8
SPAN = 64
MAXP = 12


EPSILON = 1e-05
MASKED = -1e30
HEAD_AXES = ("x", "core")


def from_partner(value, axis, bit):
    mask = 2**bit
    pairs = [(source, source ^ mask) for source in range(lax.axis_size(axis))]
    return lax.ppermute(value, axis, pairs)


def rms_norm(values, norm_gain):
    return (
        values * lax.rsqrt(jnp.mean(values * values, axis=-1, keepdims=True) + EPSILON) * norm_gain
    )


def rotate(values, position):
    half_width = values.shape[-1] // 2
    inverse_freq = 10000.0 ** (-2.0 * jnp.arange(half_width, dtype=jnp.float32) / values.shape[-1])
    angles = position[:, None] * inverse_freq[None, :]
    cosine = jnp.cos(angles)[:, None, :]
    sine_part = jnp.sin(angles)[:, None, :]
    first_part = values[..., :half_width]
    second = values[..., half_width:]
    return jnp.concatenate(
        [first_part * cosine - second * sine_part, second * cosine + first_part * sine_part],
        axis=-1,
    )


def masked_scores(queries, key_rows, allowed):
    scores = jnp.einsum(
        "chd,lhd->hcl", queries, key_rows, preferred_element_type=jnp.float32
    ) / math.sqrt(queries.shape[-1])
    return jnp.where(allowed[None], scores, MASKED)


def attend(queries, key_rows, value_rows, allowed):
    scores = masked_scores(queries, key_rows, allowed)
    row_max = jnp.max(scores, axis=-1, keepdims=True)
    raised = jnp.where(allowed[None], jnp.exp(scores - row_max), 0.0)
    weights = (raised / jnp.sum(raised, axis=-1, keepdims=True)).astype(jnp.bfloat16)
    return jnp.einsum("hcl,lhd->chd", weights, value_rows, preferred_element_type=jnp.float32)


def body(
    tokens,
    attention_gain,
    query_weight,
    key_weight,
    value_weight,
    query_gain,
    key_gain,
    out_weight,
    key_pages,
    value_pages,
    page_table,
    far_table,
    cached_lengths,
    far_lengths,
    visible_from,
    feedforward_gain,
    routes,
    route_weights,
    gate_weight,
    up_weight,
    down_weight,
):
    n_group = lax.axis_size("group")
    n_expert = lax.axis_size(HEAD_AXES)
    group_id = lax.axis_index("group")
    as_float = tokens.astype(jnp.float32)
    normed = rms_norm(as_float, attention_gain).astype(jnp.bfloat16)
    row_block = lax.all_gather(normed, HEAD_AXES, axis=0, tiled=True)
    swap = [(0, 1), (1, 0)]
    gate_full = jnp.concatenate([gate_weight, lax.ppermute(gate_weight, "core", swap)], axis=1)
    up_full = jnp.concatenate([up_weight, lax.ppermute(up_weight, "core", swap)], axis=1)
    down_full = jnp.concatenate([down_weight, lax.ppermute(down_weight, "core", swap)], axis=0)
    joined = jnp.concatenate(
        [
            jnp.dot(row_block, query_weight, preferred_element_type=jnp.float32),
            jnp.dot(row_block, key_weight, preferred_element_type=jnp.float32),
            jnp.dot(row_block, value_weight, preferred_element_type=jnp.float32),
        ],
        axis=1,
    )
    local_width = query_weight.shape[1]
    heads_here = local_width // HD
    query_raw = joined[:, :local_width]
    key_raw = joined[:, local_width : 2 * local_width]
    new_values = (
        joined[:, 2 * local_width :].astype(jnp.bfloat16).reshape(REQ, SPAN, heads_here, HD)
    )
    query_sums, key_sums = lax.psum(
        (jnp.sum(query_raw * query_raw, axis=1), jnp.sum(key_raw * key_raw, axis=1)), HEAD_AXES
    )
    full_width = local_width * n_expert
    query_normed = query_raw * lax.rsqrt(query_sums[:, None] / full_width + EPSILON) * query_gain
    key_normed = key_raw * lax.rsqrt(key_sums[:, None] / full_width + EPSILON) * key_gain
    lengths = cached_lengths[0]
    starts = visible_from[0]
    first_flag = (jnp.arange(REQ, dtype=jnp.int32) == 0).astype(jnp.int32)
    offsets = lengths + far_lengths[group_id] * first_flag
    position = (
        (offsets[:, None] + jnp.arange(SPAN, dtype=jnp.int32)[None, :])
        .reshape(-1)
        .astype(jnp.float32)
    )
    queries = (
        rotate(query_normed.reshape(-1, heads_here, HD), position)
        .astype(jnp.bfloat16)
        .reshape(REQ, SPAN, heads_here, HD)
    )
    new_keys = (
        rotate(key_normed.reshape(-1, heads_here, HD), position)
        .astype(jnp.bfloat16)
        .reshape(REQ, SPAN, heads_here, HD)
    )
    cache_slots = MAXP * PAGE
    pool_size = key_pages.shape[0]
    page_pick = (
        page_table[0][:, :, None] == jnp.arange(pool_size, dtype=jnp.int32)[None, None, :]
    ).astype(jnp.bfloat16)
    own_keys = jnp.einsum(
        "rpq,qsc->rpsc", page_pick, key_pages, preferred_element_type=jnp.float32
    ).astype(jnp.bfloat16).reshape(REQ, cache_slots, local_width)
    own_values = jnp.einsum(
        "rpq,qsc->rpsc", page_pick, value_pages, preferred_element_type=jnp.float32
    ).astype(jnp.bfloat16).reshape(REQ, cache_slots, local_width)
    own_values, out_weight = lax.optimization_barrier((own_values, out_weight))
    full_out_weight = lax.all_gather(out_weight, HEAD_AXES, axis=0, tiled=True)
    far_stack = jnp.stack([key_pages[far_table[0]], value_pages[far_table[0]]])
    received = from_partner(far_stack, "group", 0).reshape(2, cache_slots, local_width)
    cache_pos = jnp.arange(cache_slots, dtype=jnp.int32)
    own_visible = (cache_pos[None, :] < lengths[:, None]) & (cache_pos[None, :] >= starts[:, None])
    far_visible = cache_pos < far_lengths[group_id]
    causal = jnp.arange(SPAN)[:, None] >= jnp.arange(SPAN)[None, :]
    is_first = (jnp.arange(REQ) == 0)[:, None, None]
    new_keys = new_keys.reshape(REQ, SPAN, local_width)
    new_values = new_values.reshape(REQ, SPAN, local_width)
    queries = queries.reshape(REQ, SPAN, local_width)
    scale = math.sqrt(HD)
    head_outs = []
    for head in range(heads_here):
        cols = slice(head * HD, (head + 1) * HD)
        q = queries[:, :, cols]
        s_own = jnp.einsum("rcd,rld->rcl", q, own_keys[:, :, cols], preferred_element_type=jnp.float32) / scale
        s_new = jnp.einsum("rcd,rjd->rcj", q, new_keys[:, :, cols], preferred_element_type=jnp.float32) / scale
        s_far = jnp.einsum("cd,ld->cl", q[0], received[0][:, cols], preferred_element_type=jnp.float32) / scale
        s_own = jnp.where(own_visible[:, None, :], s_own, MASKED)
        s_new = jnp.where(causal[None], s_new, MASKED)
        s_far = jnp.where(far_visible[None, :], s_far, MASKED)
        far_max = jnp.max(s_far, axis=-1, keepdims=True)
        row_max = jnp.maximum(
            jnp.max(s_own, axis=-1, keepdims=True), jnp.max(s_new, axis=-1, keepdims=True)
        )
        row_max = jnp.where(is_first, jnp.maximum(row_max, far_max[None]), row_max)
        p_own = jnp.where(own_visible[:, None, :], jnp.exp(s_own - row_max), 0.0)
        p_new = jnp.where(causal[None], jnp.exp(s_new - row_max), 0.0)
        p_far = jnp.where(far_visible[None, :], jnp.exp(s_far - row_max[0]), 0.0)
        total = jnp.sum(p_own, axis=-1, keepdims=True) + jnp.sum(p_new, axis=-1, keepdims=True)
        total = jnp.where(is_first, total + jnp.sum(p_far, axis=-1, keepdims=True)[None], total)
        w_own = (p_own / total).astype(jnp.bfloat16)
        w_new = (p_new / total).astype(jnp.bfloat16)
        w_far = (p_far / total[0]).astype(jnp.bfloat16)
        ctx = jnp.einsum("rcl,rld->rcd", w_own, own_values[:, :, cols], preferred_element_type=jnp.float32)
        ctx = ctx + jnp.einsum("rcj,rjd->rcd", w_new, new_values[:, :, cols], preferred_element_type=jnp.float32)
        far_ctx = jnp.einsum("cl,ld->cd", w_far, received[1][:, cols], preferred_element_type=jnp.float32)
        ctx = ctx + jnp.where(is_first, far_ctx[None], 0.0)
        head_outs.append(ctx.astype(jnp.bfloat16))
    context = jnp.concatenate(head_outs, axis=-1)
    token_context = lax.all_to_all(
        context, HEAD_AXES, split_axis=0, concat_axis=2, tiled=True
    ).reshape(SPAN, -1)
    attended = jnp.dot(token_context, full_out_weight, preferred_element_type=jnp.float32)
    residual = (as_float + attended).astype(jnp.bfloat16)
    moe_in = rms_norm(residual.astype(jnp.float32), feedforward_gain).astype(jnp.bfloat16)
    row_count = tokens.shape[0]
    n_chip = lax.axis_size(("group", "x"))
    capacity = row_count * TOP * 3 // (2 * EXPERTS)
    slots = EXPERTS * capacity
    flat_routes = routes.reshape(-1)
    onehot = (flat_routes[:, None] == jnp.arange(EXPERTS, dtype=jnp.int32)[None, :]).astype(
        jnp.int32
    )
    earlier = jnp.cumsum(onehot, axis=0) - onehot
    slot_index = jnp.sum(earlier * onehot, axis=1)
    position_of = (flat_routes * capacity + slot_index).reshape(row_count, TOP)
    lanes = 128
    bands = D // lanes
    hits = (
        position_of.reshape(-1)[:, None] == jnp.arange(slots, dtype=jnp.int32)[None, :]
    ).astype(jnp.bfloat16)
    owner_plus_one = (jnp.arange(row_count * TOP, dtype=jnp.int32) // TOP + 1).astype(jnp.bfloat16)
    owner = jnp.dot(owner_plus_one[None, :], hits, preferred_element_type=jnp.float32)[0]
    slot_token = jnp.where(owner > 0, owner - 1, row_count).astype(jnp.int32).reshape(
        EXPERTS, capacity
    )
    padded_in = jnp.concatenate([moe_in, jnp.zeros((1, D), moe_in.dtype)], axis=0)
    buffer = padded_in.reshape(row_count + 1, bands, lanes)[slot_token]

    def exchange(blocks):
        flat = blocks.reshape(n_chip, capacity * bands, lanes)
        moved = lax.all_to_all(flat, ("group", "x"), split_axis=0, concat_axis=0, tiled=True)
        return moved.reshape(n_chip, capacity, bands, lanes)

    incoming = exchange(buffer)
    gate_act = jnp.einsum("esjl,jlf->esf", incoming, gate_full.reshape(bands, lanes, -1), preferred_element_type=jnp.float32)
    up_act = jnp.einsum("esjl,jlf->esf", incoming, up_full.reshape(bands, lanes, -1), preferred_element_type=jnp.float32)
    hidden = (jax.nn.silu(gate_act) * up_act).astype(jnp.bfloat16)
    expert_rows = jnp.einsum(
        "esf,fjl->esjl", hidden, down_full.reshape(-1, bands, lanes), preferred_element_type=jnp.float32
    ).astype(jnp.bfloat16)
    returned = exchange(expert_rows)
    picked = returned.reshape(slots, bands, lanes)[position_of]
    moe_out = jnp.sum(
        route_weights[:, :, None, None] * picked.astype(jnp.float32), axis=1
    ).reshape(row_count, D)
    return (residual.astype(jnp.float32) + moe_out).astype(jnp.bfloat16)


def solution(mesh):
    n_group, n_expert = mesh.devices.shape
    chip_mesh = jax.sharding.Mesh(
        mesh.devices.reshape(n_group, n_expert // 2, 2), ("group", "x", "core")
    )
    everyone = ("group", "x", "core")
    return jax.shard_map(
        body,
        mesh=chip_mesh,
        in_specs=(
            P(everyone, None),
            P(),
            P(None, HEAD_AXES),
            P(None, HEAD_AXES),
            P(None, HEAD_AXES),
            P(HEAD_AXES),
            P(HEAD_AXES),
            P(HEAD_AXES, None),
            P("group", None, HEAD_AXES),
            P("group", None, HEAD_AXES),
            P("group", None, None),
            P("group", None),
            P("group", None),
            P(),
            P("group", None),
            P(),
            P(everyone, None),
            P(everyone, None),
            P(None, everyone),
            P(None, everyone),
            P(everyone, None),
        ),
        out_specs=P(everyone, None),
        check_vma=False,
    )
```

```python
import math

import jax
import jax.numpy as jnp
from jax import lax
from jax.sharding import PartitionSpec as P

D = 2048
HD = 128
EXPERTS = 64
TOP = 8
PAGE = 128
REQ = 8
SPAN = 64
MAXP = 12


EPSILON = 1e-05
MASKED = -1e30
HEAD_AXES = ("x", "core")


def from_partner(value, axis, bit):
    mask = 2**bit
    pairs = [(source, source ^ mask) for source in range(lax.axis_size(axis))]
    return lax.ppermute(value, axis, pairs)


def rms_norm(values, norm_gain):
    return (
        values * lax.rsqrt(jnp.mean(values * values, axis=-1, keepdims=True) + EPSILON) * norm_gain
    )


def rotate(values, position):
    half_width = values.shape[-1] // 2
    inverse_freq = 10000.0 ** (-2.0 * jnp.arange(half_width, dtype=jnp.float32) / values.shape[-1])
    angles = position[:, None] * inverse_freq[None, :]
    cosine = jnp.cos(angles)[:, None, :]
    sine_part = jnp.sin(angles)[:, None, :]
    first_part = values[..., :half_width]
    second = values[..., half_width:]
    return jnp.concatenate(
        [first_part * cosine - second * sine_part, second * cosine + first_part * sine_part],
        axis=-1,
    )


def masked_scores(queries, key_rows, allowed):
    scores = jnp.einsum(
        "chd,lhd->hcl", queries, key_rows, preferred_element_type=jnp.float32
    ) / math.sqrt(queries.shape[-1])
    return jnp.where(allowed[None], scores, MASKED)


def attend(queries, key_rows, value_rows, allowed):
    scores = masked_scores(queries, key_rows, allowed)
    row_max = jnp.max(scores, axis=-1, keepdims=True)
    raised = jnp.where(allowed[None], jnp.exp(scores - row_max), 0.0)
    weights = (raised / jnp.sum(raised, axis=-1, keepdims=True)).astype(jnp.bfloat16)
    return jnp.einsum("hcl,lhd->chd", weights, value_rows, preferred_element_type=jnp.float32)


def body(
    tokens,
    attention_gain,
    query_weight,
    key_weight,
    value_weight,
    query_gain,
    key_gain,
    out_weight,
    key_pages,
    value_pages,
    page_table,
    far_table,
    cached_lengths,
    far_lengths,
    visible_from,
    feedforward_gain,
    routes,
    route_weights,
    gate_weight,
    up_weight,
    down_weight,
):
    n_group = lax.axis_size("group")
    n_expert = lax.axis_size(HEAD_AXES)
    group_id = lax.axis_index("group")
    as_float = tokens.astype(jnp.float32)
    normed = rms_norm(as_float, attention_gain).astype(jnp.bfloat16)
    row_block = lax.all_gather(normed, HEAD_AXES, axis=0, tiled=True)
    swap = [(0, 1), (1, 0)]
    gate_full = jnp.concatenate([gate_weight, lax.ppermute(gate_weight, "core", swap)], axis=1)
    up_full = jnp.concatenate([up_weight, lax.ppermute(up_weight, "core", swap)], axis=1)
    down_full = jnp.concatenate([down_weight, lax.ppermute(down_weight, "core", swap)], axis=0)
    joined = jnp.concatenate(
        [
            jnp.dot(row_block, query_weight, preferred_element_type=jnp.float32),
            jnp.dot(row_block, key_weight, preferred_element_type=jnp.float32),
            jnp.dot(row_block, value_weight, preferred_element_type=jnp.float32),
        ],
        axis=1,
    )
    local_width = query_weight.shape[1]
    heads_here = local_width // HD
    query_raw = joined[:, :local_width]
    key_raw = joined[:, local_width : 2 * local_width]
    new_values = (
        joined[:, 2 * local_width :].astype(jnp.bfloat16).reshape(REQ, SPAN, heads_here, HD)
    )
    query_sums, key_sums = lax.psum(
        (jnp.sum(query_raw * query_raw, axis=1), jnp.sum(key_raw * key_raw, axis=1)), HEAD_AXES
    )
    full_width = local_width * n_expert
    query_normed = query_raw * lax.rsqrt(query_sums[:, None] / full_width + EPSILON) * query_gain
    key_normed = key_raw * lax.rsqrt(key_sums[:, None] / full_width + EPSILON) * key_gain
    lengths = cached_lengths[0]
    starts = visible_from[0]
    first_flag = (jnp.arange(REQ, dtype=jnp.int32) == 0).astype(jnp.int32)
    offsets = lengths + far_lengths[group_id] * first_flag
    position = (
        (offsets[:, None] + jnp.arange(SPAN, dtype=jnp.int32)[None, :])
        .reshape(-1)
        .astype(jnp.float32)
    )
    queries = (
        rotate(query_normed.reshape(-1, heads_here, HD), position)
        .astype(jnp.bfloat16)
        .reshape(REQ, SPAN, heads_here, HD)
    )
    new_keys = (
        rotate(key_normed.reshape(-1, heads_here, HD), position)
        .astype(jnp.bfloat16)
        .reshape(REQ, SPAN, heads_here, HD)
    )
    cache_slots = MAXP * PAGE
    pool_size = key_pages.shape[0]
    page_pick = (
        page_table[0][:, :, None] == jnp.arange(pool_size, dtype=jnp.int32)[None, None, :]
    ).astype(jnp.bfloat16)
    own_keys = jnp.einsum(
        "rpq,qsc->rpsc", page_pick, key_pages, preferred_element_type=jnp.float32
    ).astype(jnp.bfloat16).reshape(REQ, cache_slots, local_width)
    own_values = jnp.einsum(
        "rpq,qsc->rpsc", page_pick, value_pages, preferred_element_type=jnp.float32
    ).astype(jnp.bfloat16).reshape(REQ, cache_slots, local_width)
    own_values, out_weight = lax.optimization_barrier((own_values, out_weight))
    full_out_weight = lax.all_gather(out_weight, HEAD_AXES, axis=0, tiled=True)
    far_keys = key_pages[far_table[0]].reshape(cache_slots, local_width)
    far_values = value_pages[far_table[0]].reshape(cache_slots, local_width)
    cache_pos = jnp.arange(cache_slots, dtype=jnp.int32)
    own_visible = (cache_pos[None, :] < lengths[:, None]) & (cache_pos[None, :] >= starts[:, None])
    causal = jnp.arange(SPAN)[:, None] >= jnp.arange(SPAN)[None, :]
    is_first = (jnp.arange(REQ) == 0)[:, None, None]
    new_keys = new_keys.reshape(REQ, SPAN, local_width)
    new_values = new_values.reshape(REQ, SPAN, local_width)
    queries = queries.reshape(REQ, SPAN, local_width)
    scale = math.sqrt(HD)
    guest_queries = from_partner(queries[0], "group", 0)
    guest_visible = cache_pos < far_lengths[group_id ^ 1]
    guest_ctx = []
    guest_stats = []
    for head in range(heads_here):
        cols = slice(head * HD, (head + 1) * HD)
        s_guest = jnp.einsum(
            "cd,ld->cl", guest_queries[:, cols], far_keys[:, cols], preferred_element_type=jnp.float32
        ) / scale
        s_guest = jnp.where(guest_visible[None, :], s_guest, MASKED)
        guest_max = jnp.max(s_guest, axis=-1, keepdims=True)
        p_guest = jnp.where(guest_visible[None, :], jnp.exp(s_guest - guest_max), 0.0)
        guest_sum = jnp.sum(p_guest, axis=-1, keepdims=True)
        guest_ctx.append(
            jnp.einsum(
                "cl,ld->cd", p_guest.astype(jnp.bfloat16), far_values[:, cols], preferred_element_type=jnp.float32
            )
        )
        guest_stats.append(jnp.concatenate([guest_max, guest_sum], axis=-1))
    far_ctx_all = from_partner(jnp.concatenate(guest_ctx, axis=-1), "group", 0)
    far_stats = from_partner(jnp.stack(guest_stats, axis=1), "group", 0)
    head_outs = []
    for head in range(heads_here):
        cols = slice(head * HD, (head + 1) * HD)
        q = queries[:, :, cols]
        s_own = jnp.einsum("rcd,rld->rcl", q, own_keys[:, :, cols], preferred_element_type=jnp.float32) / scale
        s_new = jnp.einsum("rcd,rjd->rcj", q, new_keys[:, :, cols], preferred_element_type=jnp.float32) / scale
        s_own = jnp.where(own_visible[:, None, :], s_own, MASKED)
        s_new = jnp.where(causal[None], s_new, MASKED)
        far_max = far_stats[:, head, 0:1]
        far_sum = far_stats[:, head, 1:2]
        row_max = jnp.maximum(
            jnp.max(s_own, axis=-1, keepdims=True), jnp.max(s_new, axis=-1, keepdims=True)
        )
        row_max = jnp.where(is_first, jnp.maximum(row_max, far_max[None]), row_max)
        p_own = jnp.where(own_visible[:, None, :], jnp.exp(s_own - row_max), 0.0)
        p_new = jnp.where(causal[None], jnp.exp(s_new - row_max), 0.0)
        far_scale = jnp.exp(far_max - row_max[0])
        total = jnp.sum(p_own, axis=-1, keepdims=True) + jnp.sum(p_new, axis=-1, keepdims=True)
        total = jnp.where(is_first, total + (far_sum * far_scale)[None], total)
        w_own = (p_own / total).astype(jnp.bfloat16)
        w_new = (p_new / total).astype(jnp.bfloat16)
        ctx = jnp.einsum("rcl,rld->rcd", w_own, own_values[:, :, cols], preferred_element_type=jnp.float32)
        ctx = ctx + jnp.einsum("rcj,rjd->rcd", w_new, new_values[:, :, cols], preferred_element_type=jnp.float32)
        far_part = far_ctx_all[:, cols] * (far_scale / total[0])
        ctx = ctx + jnp.where(is_first, far_part[None], 0.0)
        head_outs.append(ctx.astype(jnp.bfloat16))
    context = jnp.concatenate(head_outs, axis=-1)
    token_context = lax.all_to_all(
        context, HEAD_AXES, split_axis=0, concat_axis=2, tiled=True
    ).reshape(SPAN, -1)
    attended = jnp.dot(token_context, full_out_weight, preferred_element_type=jnp.float32)
    residual = (as_float + attended).astype(jnp.bfloat16)
    moe_in = rms_norm(residual.astype(jnp.float32), feedforward_gain).astype(jnp.bfloat16)
    row_count = tokens.shape[0]
    n_chip = lax.axis_size(("group", "x"))
    capacity = row_count * TOP * 3 // (2 * EXPERTS)
    slots = EXPERTS * capacity
    flat_routes = routes.reshape(-1)
    onehot = (flat_routes[:, None] == jnp.arange(EXPERTS, dtype=jnp.int32)[None, :]).astype(
        jnp.int32
    )
    earlier = jnp.cumsum(onehot, axis=0) - onehot
    slot_index = jnp.sum(earlier * onehot, axis=1)
    position_of = (flat_routes * capacity + slot_index).reshape(row_count, TOP)
    lanes = 128
    bands = D // lanes
    hits = (
        position_of.reshape(-1)[:, None] == jnp.arange(slots, dtype=jnp.int32)[None, :]
    ).astype(jnp.bfloat16)
    owner_plus_one = (jnp.arange(row_count * TOP, dtype=jnp.int32) // TOP + 1).astype(jnp.bfloat16)
    owner = jnp.dot(owner_plus_one[None, :], hits, preferred_element_type=jnp.float32)[0]
    slot_token = jnp.where(owner > 0, owner - 1, row_count).astype(jnp.int32).reshape(
        EXPERTS, capacity
    )
    padded_in = jnp.concatenate([moe_in, jnp.zeros((1, D), moe_in.dtype)], axis=0)
    buffer = padded_in.reshape(row_count + 1, bands, lanes)[slot_token]

    def exchange(blocks):
        flat = blocks.reshape(n_chip, capacity * bands, lanes)
        moved = lax.all_to_all(flat, ("group", "x"), split_axis=0, concat_axis=0, tiled=True)
        return moved.reshape(n_chip, capacity, bands, lanes)

    incoming = exchange(buffer)
    gate_act = jnp.einsum("esjl,jlf->esf", incoming, gate_full.reshape(bands, lanes, -1), preferred_element_type=jnp.float32)
    up_act = jnp.einsum("esjl,jlf->esf", incoming, up_full.reshape(bands, lanes, -1), preferred_element_type=jnp.float32)
    hidden = (jax.nn.silu(gate_act) * up_act).astype(jnp.bfloat16)
    expert_rows = jnp.einsum(
        "esf,fjl->esjl", hidden, down_full.reshape(-1, bands, lanes), preferred_element_type=jnp.float32
    ).astype(jnp.bfloat16)
    returned = exchange(expert_rows)
    picked = returned.reshape(slots, bands, lanes)[position_of]
    moe_out = jnp.sum(
        route_weights[:, :, None, None] * picked.astype(jnp.float32), axis=1
    ).reshape(row_count, D)
    return (residual.astype(jnp.float32) + moe_out).astype(jnp.bfloat16)


def solution(mesh):
    n_group, n_expert = mesh.devices.shape
    chip_mesh = jax.sharding.Mesh(
        mesh.devices.reshape(n_group, n_expert // 2, 2), ("group", "x", "core")
    )
    everyone = ("group", "x", "core")
    return jax.shard_map(
        body,
        mesh=chip_mesh,
        in_specs=(
            P(everyone, None),
            P(),
            P(None, HEAD_AXES),
            P(None, HEAD_AXES),
            P(None, HEAD_AXES),
            P(HEAD_AXES),
            P(HEAD_AXES),
            P(HEAD_AXES, None),
            P("group", None, HEAD_AXES),
            P("group", None, HEAD_AXES),
            P("group", None, None),
            P("group", None),
            P("group", None),
            P(),
            P("group", None),
            P(),
            P(everyone, None),
            P(everyone, None),
            P(None, everyone),
            P(None, everyone),
            P(everyone, None),
        ),
        out_specs=P(everyone, None),
        check_vma=False,
    )
```

```python
import math

import jax
import jax.numpy as jnp
from jax import lax
from jax.sharding import PartitionSpec as P

D = 2048
HD = 128
EXPERTS = 64
TOP = 8
PAGE = 128
REQ = 8
SPAN = 64
MAXP = 12


EPSILON = 1e-05
MASKED = -1e30
HEAD_AXES = ("x", "core")


def from_partner(value, axis, bit):
    mask = 2**bit
    pairs = [(source, source ^ mask) for source in range(lax.axis_size(axis))]
    return lax.ppermute(value, axis, pairs)


def rms_norm(values, norm_gain):
    return (
        values * lax.rsqrt(jnp.mean(values * values, axis=-1, keepdims=True) + EPSILON) * norm_gain
    )


def rotate(values, position):
    half_width = values.shape[-1] // 2
    inverse_freq = 10000.0 ** (-2.0 * jnp.arange(half_width, dtype=jnp.float32) / values.shape[-1])
    angles = position[:, None] * inverse_freq[None, :]
    cosine = jnp.cos(angles)[:, None, :]
    sine_part = jnp.sin(angles)[:, None, :]
    first_part = values[..., :half_width]
    second = values[..., half_width:]
    return jnp.concatenate(
        [first_part * cosine - second * sine_part, second * cosine + first_part * sine_part],
        axis=-1,
    )


def masked_scores(queries, key_rows, allowed):
    scores = jnp.einsum(
        "chd,lhd->hcl", queries, key_rows, preferred_element_type=jnp.float32
    ) / math.sqrt(queries.shape[-1])
    return jnp.where(allowed[None], scores, MASKED)


def attend(queries, key_rows, value_rows, allowed):
    scores = masked_scores(queries, key_rows, allowed)
    row_max = jnp.max(scores, axis=-1, keepdims=True)
    raised = jnp.where(allowed[None], jnp.exp(scores - row_max), 0.0)
    weights = (raised / jnp.sum(raised, axis=-1, keepdims=True)).astype(jnp.bfloat16)
    return jnp.einsum("hcl,lhd->chd", weights, value_rows, preferred_element_type=jnp.float32)


def body(
    tokens,
    attention_gain,
    query_weight,
    key_weight,
    value_weight,
    query_gain,
    key_gain,
    out_weight,
    key_pages,
    value_pages,
    page_table,
    far_table,
    cached_lengths,
    far_lengths,
    visible_from,
    feedforward_gain,
    routes,
    route_weights,
    gate_weight,
    up_weight,
    down_weight,
):
    n_group = lax.axis_size("group")
    n_expert = lax.axis_size(HEAD_AXES)
    group_id = lax.axis_index("group")
    as_float = tokens.astype(jnp.float32)
    token_block = lax.all_gather(tokens, HEAD_AXES, axis=0, tiled=True)
    row_block = rms_norm(token_block.astype(jnp.float32), attention_gain).astype(jnp.bfloat16)
    swap = [(0, 1), (1, 0)]
    gate_full = jnp.concatenate([gate_weight, lax.ppermute(gate_weight, "core", swap)], axis=1)
    up_full = jnp.concatenate([up_weight, lax.ppermute(up_weight, "core", swap)], axis=1)
    down_full = jnp.concatenate([down_weight, lax.ppermute(down_weight, "core", swap)], axis=0)
    joined = jnp.concatenate(
        [
            jnp.dot(row_block, query_weight, preferred_element_type=jnp.float32),
            jnp.dot(row_block, key_weight, preferred_element_type=jnp.float32),
            jnp.dot(row_block, value_weight, preferred_element_type=jnp.float32),
        ],
        axis=1,
    )
    local_width = query_weight.shape[1]
    heads_here = local_width // HD
    query_raw = joined[:, :local_width]
    key_raw = joined[:, local_width : 2 * local_width]
    new_values = (
        joined[:, 2 * local_width :].astype(jnp.bfloat16).reshape(REQ, SPAN, heads_here, HD)
    )
    query_sums, key_sums = lax.psum(
        lax.psum(
            (jnp.sum(query_raw * query_raw, axis=1), jnp.sum(key_raw * key_raw, axis=1)), "core"
        ),
        "x",
    )
    full_width = local_width * n_expert
    query_normed = query_raw * lax.rsqrt(query_sums[:, None] / full_width + EPSILON) * query_gain
    key_normed = key_raw * lax.rsqrt(key_sums[:, None] / full_width + EPSILON) * key_gain
    lengths = cached_lengths[0]
    starts = visible_from[0]
    first_flag = (jnp.arange(REQ, dtype=jnp.int32) == 0).astype(jnp.int32)
    offsets = lengths + far_lengths[group_id] * first_flag
    position = (
        (offsets[:, None] + jnp.arange(SPAN, dtype=jnp.int32)[None, :])
        .reshape(-1)
        .astype(jnp.float32)
    )
    queries = (
        rotate(query_normed.reshape(-1, heads_here, HD), position)
        .astype(jnp.bfloat16)
        .reshape(REQ, SPAN, heads_here, HD)
    )
    new_keys = (
        rotate(key_normed.reshape(-1, heads_here, HD), position)
        .astype(jnp.bfloat16)
        .reshape(REQ, SPAN, heads_here, HD)
    )
    cache_slots = MAXP * PAGE
    pool_size = key_pages.shape[0]
    page_pick = (
        page_table[0][:, :, None] == jnp.arange(pool_size, dtype=jnp.int32)[None, None, :]
    ).astype(jnp.bfloat16)
    own_keys = jnp.einsum(
        "rpq,qsc->rpsc", page_pick, key_pages, preferred_element_type=jnp.float32
    ).astype(jnp.bfloat16).reshape(REQ, cache_slots, local_width)
    own_values = jnp.einsum(
        "rpq,qsc->rpsc", page_pick, value_pages, preferred_element_type=jnp.float32
    ).astype(jnp.bfloat16).reshape(REQ, cache_slots, local_width)
    own_values, out_weight = lax.optimization_barrier((own_values, out_weight))
    full_out_weight = lax.all_gather(out_weight, HEAD_AXES, axis=0, tiled=True)
    far_keys = key_pages[far_table[0]].reshape(cache_slots, local_width)
    far_values = value_pages[far_table[0]].reshape(cache_slots, local_width)
    cache_pos = jnp.arange(cache_slots, dtype=jnp.int32)
    own_visible = (cache_pos[None, :] < lengths[:, None]) & (cache_pos[None, :] >= starts[:, None])
    causal = jnp.arange(SPAN)[:, None] >= jnp.arange(SPAN)[None, :]
    is_first = (jnp.arange(REQ) == 0)[:, None, None]
    new_keys = new_keys.reshape(REQ, SPAN, local_width)
    new_values = new_values.reshape(REQ, SPAN, local_width)
    queries = queries.reshape(REQ, SPAN, local_width)
    scale = math.sqrt(HD)
    guest_queries = from_partner(queries[0], "group", 0)
    guest_visible = cache_pos < far_lengths[group_id ^ 1]
    guest_ctx = []
    guest_stats = []
    for head in range(heads_here):
        cols = slice(head * HD, (head + 1) * HD)
        s_guest = jnp.einsum(
            "cd,ld->cl", guest_queries[:, cols], far_keys[:, cols], preferred_element_type=jnp.float32
        ) / scale
        s_guest = jnp.where(guest_visible[None, :], s_guest, MASKED)
        guest_max = jnp.max(s_guest, axis=-1, keepdims=True)
        p_guest = jnp.where(guest_visible[None, :], jnp.exp(s_guest - guest_max), 0.0)
        guest_sum = jnp.sum(p_guest, axis=-1, keepdims=True)
        guest_ctx.append(
            jnp.einsum(
                "cl,ld->cd", p_guest.astype(jnp.bfloat16), far_values[:, cols], preferred_element_type=jnp.float32
            )
        )
        guest_stats.append(jnp.concatenate([guest_max, guest_sum], axis=-1))
    far_ctx_all = from_partner(jnp.concatenate(guest_ctx, axis=-1), "group", 0)
    far_stats = from_partner(jnp.stack(guest_stats, axis=1), "group", 0)
    head_outs = []
    for head in range(heads_here):
        cols = slice(head * HD, (head + 1) * HD)
        q = queries[:, :, cols]
        s_own = jnp.einsum("rcd,rld->rcl", q, own_keys[:, :, cols], preferred_element_type=jnp.float32) / scale
        s_new = jnp.einsum("rcd,rjd->rcj", q, new_keys[:, :, cols], preferred_element_type=jnp.float32) / scale
        s_own = jnp.where(own_visible[:, None, :], s_own, MASKED)
        s_new = jnp.where(causal[None], s_new, MASKED)
        far_max = far_stats[:, head, 0:1]
        far_sum = far_stats[:, head, 1:2]
        row_max = jnp.maximum(
            jnp.max(s_own, axis=-1, keepdims=True), jnp.max(s_new, axis=-1, keepdims=True)
        )
        row_max = jnp.where(is_first, jnp.maximum(row_max, far_max[None]), row_max)
        p_own = jnp.where(own_visible[:, None, :], jnp.exp(s_own - row_max), 0.0)
        p_new = jnp.where(causal[None], jnp.exp(s_new - row_max), 0.0)
        far_scale = jnp.exp(far_max - row_max[0])
        total = jnp.sum(p_own, axis=-1, keepdims=True) + jnp.sum(p_new, axis=-1, keepdims=True)
        total = jnp.where(is_first, total + (far_sum * far_scale)[None], total)
        w_own = (p_own / total).astype(jnp.bfloat16)
        w_new = (p_new / total).astype(jnp.bfloat16)
        ctx = jnp.einsum("rcl,rld->rcd", w_own, own_values[:, :, cols], preferred_element_type=jnp.float32)
        ctx = ctx + jnp.einsum("rcj,rjd->rcd", w_new, new_values[:, :, cols], preferred_element_type=jnp.float32)
        far_part = far_ctx_all[:, cols] * (far_scale / total[0])
        ctx = ctx + jnp.where(is_first, far_part[None], 0.0)
        head_outs.append(ctx.astype(jnp.bfloat16))
    context = jnp.concatenate(head_outs, axis=-1)
    token_context = lax.all_to_all(
        context, HEAD_AXES, split_axis=0, concat_axis=2, tiled=True
    ).reshape(SPAN, -1)
    attended = jnp.dot(token_context, full_out_weight, preferred_element_type=jnp.float32)
    residual = (as_float + attended).astype(jnp.bfloat16)
    moe_in = rms_norm(residual.astype(jnp.float32), feedforward_gain).astype(jnp.bfloat16)
    row_count = tokens.shape[0]
    n_chip = lax.axis_size(("group", "x"))
    capacity = row_count * TOP * 3 // (2 * EXPERTS)
    slots = EXPERTS * capacity
    flat_routes = routes.reshape(-1)
    onehot = (flat_routes[:, None] == jnp.arange(EXPERTS, dtype=jnp.int32)[None, :]).astype(
        jnp.int32
    )
    earlier = jnp.cumsum(onehot, axis=0) - onehot
    slot_index = jnp.sum(earlier * onehot, axis=1)
    position_of = (flat_routes * capacity + slot_index).reshape(row_count, TOP)
    lanes = 128
    bands = D // lanes
    hits = (
        position_of.reshape(-1)[:, None] == jnp.arange(slots, dtype=jnp.int32)[None, :]
    ).astype(jnp.bfloat16)
    owner_plus_one = (jnp.arange(row_count * TOP, dtype=jnp.int32) // TOP + 1).astype(jnp.bfloat16)
    owner = jnp.dot(owner_plus_one[None, :], hits, preferred_element_type=jnp.float32)[0]
    slot_token = jnp.where(owner > 0, owner - 1, row_count).astype(jnp.int32).reshape(
        EXPERTS, capacity
    )
    padded_in = jnp.concatenate([moe_in, jnp.zeros((1, D), moe_in.dtype)], axis=0)
    buffer = padded_in.reshape(row_count + 1, bands, lanes)[slot_token]

    def exchange(blocks):
        flat = blocks.reshape(n_chip, capacity * bands, lanes)
        moved = lax.all_to_all(flat, ("group", "x"), split_axis=0, concat_axis=0, tiled=True)
        return moved.reshape(n_chip, capacity, bands, lanes)

    incoming = exchange(buffer)
    gate_act = jnp.einsum("esjl,jlf->esf", incoming, gate_full.reshape(bands, lanes, -1), preferred_element_type=jnp.float32)
    up_act = jnp.einsum("esjl,jlf->esf", incoming, up_full.reshape(bands, lanes, -1), preferred_element_type=jnp.float32)
    hidden = (jax.nn.silu(gate_act) * up_act).astype(jnp.bfloat16)
    expert_rows = jnp.einsum(
        "esf,fjl->esjl", hidden, down_full.reshape(-1, bands, lanes), preferred_element_type=jnp.float32
    ).astype(jnp.bfloat16)
    returned = exchange(expert_rows)
    picked = returned.reshape(slots, bands, lanes)[position_of]
    moe_out = jnp.sum(
        route_weights[:, :, None, None] * picked.astype(jnp.float32), axis=1
    ).reshape(row_count, D)
    return (residual.astype(jnp.float32) + moe_out).astype(jnp.bfloat16)


def solution(mesh):
    n_group, n_expert = mesh.devices.shape
    chip_mesh = jax.sharding.Mesh(
        mesh.devices.reshape(n_group, n_expert // 2, 2), ("group", "x", "core")
    )
    everyone = ("group", "x", "core")
    return jax.shard_map(
        body,
        mesh=chip_mesh,
        in_specs=(
            P(everyone, None),
            P(),
            P(None, HEAD_AXES),
            P(None, HEAD_AXES),
            P(None, HEAD_AXES),
            P(HEAD_AXES),
            P(HEAD_AXES),
            P(HEAD_AXES, None),
            P("group", None, HEAD_AXES),
            P("group", None, HEAD_AXES),
            P("group", None, None),
            P("group", None),
            P("group", None),
            P(),
            P("group", None),
            P(),
            P(everyone, None),
            P(everyone, None),
            P(None, everyone),
            P(None, everyone),
            P(everyone, None),
        ),
        out_specs=P(everyone, None),
        check_vma=False,
    )
```

```python
import math

import jax
import jax.numpy as jnp
from jax import lax
from jax.sharding import PartitionSpec as P

D = 2048
HD = 128
EXPERTS = 64
TOP = 8
PAGE = 128
REQ = 8
SPAN = 64
MAXP = 12


EPSILON = 1e-05
MASKED = -1e30
HEAD_AXES = ("x", "core")


def from_partner(value, axis, bit):
    mask = 2**bit
    pairs = [(source, source ^ mask) for source in range(lax.axis_size(axis))]
    return lax.ppermute(value, axis, pairs)


def rms_norm(values, norm_gain):
    return (
        values * lax.rsqrt(jnp.mean(values * values, axis=-1, keepdims=True) + EPSILON) * norm_gain
    )


def rotate(values, position):
    half_width = values.shape[-1] // 2
    inverse_freq = 10000.0 ** (-2.0 * jnp.arange(half_width, dtype=jnp.float32) / values.shape[-1])
    angles = position[:, None] * inverse_freq[None, :]
    cosine = jnp.cos(angles)[:, None, :]
    sine_part = jnp.sin(angles)[:, None, :]
    first_part = values[..., :half_width]
    second = values[..., half_width:]
    return jnp.concatenate(
        [first_part * cosine - second * sine_part, second * cosine + first_part * sine_part],
        axis=-1,
    )


def masked_scores(queries, key_rows, allowed):
    scores = jnp.einsum(
        "chd,lhd->hcl", queries, key_rows, preferred_element_type=jnp.float32
    ) / math.sqrt(queries.shape[-1])
    return jnp.where(allowed[None], scores, MASKED)


def attend(queries, key_rows, value_rows, allowed):
    scores = masked_scores(queries, key_rows, allowed)
    row_max = jnp.max(scores, axis=-1, keepdims=True)
    raised = jnp.where(allowed[None], jnp.exp(scores - row_max), 0.0)
    weights = (raised / jnp.sum(raised, axis=-1, keepdims=True)).astype(jnp.bfloat16)
    return jnp.einsum("hcl,lhd->chd", weights, value_rows, preferred_element_type=jnp.float32)


def body(
    tokens,
    attention_gain,
    query_weight,
    key_weight,
    value_weight,
    query_gain,
    key_gain,
    out_weight,
    key_pages,
    value_pages,
    page_table,
    far_table,
    cached_lengths,
    far_lengths,
    visible_from,
    feedforward_gain,
    routes,
    route_weights,
    gate_weight,
    up_weight,
    down_weight,
):
    n_group = lax.axis_size("group")
    n_expert = lax.axis_size(HEAD_AXES)
    group_id = lax.axis_index("group")
    as_float = tokens.astype(jnp.float32)
    token_copies = jnp.broadcast_to(tokens[None], (n_expert,) + tokens.shape)
    token_block = lax.all_to_all(
        token_copies, HEAD_AXES, split_axis=0, concat_axis=0, tiled=True
    ).reshape(-1, D)
    row_block = rms_norm(token_block.astype(jnp.float32), attention_gain).astype(jnp.bfloat16)
    swap = [(0, 1), (1, 0)]
    gate_full = jnp.concatenate([gate_weight, lax.ppermute(gate_weight, "core", swap)], axis=1)
    up_full = jnp.concatenate([up_weight, lax.ppermute(up_weight, "core", swap)], axis=1)
    down_full = jnp.concatenate([down_weight, lax.ppermute(down_weight, "core", swap)], axis=0)
    joined = jnp.concatenate(
        [
            jnp.dot(row_block, query_weight, preferred_element_type=jnp.float32),
            jnp.dot(row_block, key_weight, preferred_element_type=jnp.float32),
            jnp.dot(row_block, value_weight, preferred_element_type=jnp.float32),
        ],
        axis=1,
    )
    local_width = query_weight.shape[1]
    heads_here = local_width // HD
    query_raw = joined[:, :local_width]
    key_raw = joined[:, local_width : 2 * local_width]
    new_values = (
        joined[:, 2 * local_width :].astype(jnp.bfloat16).reshape(REQ, SPAN, heads_here, HD)
    )
    query_sums, key_sums = lax.psum(
        lax.psum(
            (jnp.sum(query_raw * query_raw, axis=1), jnp.sum(key_raw * key_raw, axis=1)), "core"
        ),
        "x",
    )
    full_width = local_width * n_expert
    query_normed = query_raw * lax.rsqrt(query_sums[:, None] / full_width + EPSILON) * query_gain
    key_normed = key_raw * lax.rsqrt(key_sums[:, None] / full_width + EPSILON) * key_gain
    lengths = cached_lengths[0]
    starts = visible_from[0]
    first_flag = (jnp.arange(REQ, dtype=jnp.int32) == 0).astype(jnp.int32)
    offsets = lengths + far_lengths[group_id] * first_flag
    position = (
        (offsets[:, None] + jnp.arange(SPAN, dtype=jnp.int32)[None, :])
        .reshape(-1)
        .astype(jnp.float32)
    )
    queries = (
        rotate(query_normed.reshape(-1, heads_here, HD), position)
        .astype(jnp.bfloat16)
        .reshape(REQ, SPAN, heads_here, HD)
    )
    new_keys = (
        rotate(key_normed.reshape(-1, heads_here, HD), position)
        .astype(jnp.bfloat16)
        .reshape(REQ, SPAN, heads_here, HD)
    )
    cache_slots = MAXP * PAGE
    pool_size = key_pages.shape[0]
    page_pick = (
        page_table[0][:, :, None] == jnp.arange(pool_size, dtype=jnp.int32)[None, None, :]
    ).astype(jnp.bfloat16)
    own_keys = jnp.einsum(
        "rpq,qsc->rpsc", page_pick, key_pages, preferred_element_type=jnp.float32
    ).astype(jnp.bfloat16).reshape(REQ, cache_slots, local_width)
    own_values = jnp.einsum(
        "rpq,qsc->rpsc", page_pick, value_pages, preferred_element_type=jnp.float32
    ).astype(jnp.bfloat16).reshape(REQ, cache_slots, local_width)
    own_values, out_weight = lax.optimization_barrier((own_values, out_weight))
    full_out_weight = lax.all_gather(out_weight, HEAD_AXES, axis=0, tiled=True)
    far_keys = key_pages[far_table[0]].reshape(cache_slots, local_width)
    far_values = value_pages[far_table[0]].reshape(cache_slots, local_width)
    cache_pos = jnp.arange(cache_slots, dtype=jnp.int32)
    own_visible = (cache_pos[None, :] < lengths[:, None]) & (cache_pos[None, :] >= starts[:, None])
    causal = jnp.arange(SPAN)[:, None] >= jnp.arange(SPAN)[None, :]
    is_first = (jnp.arange(REQ) == 0)[:, None, None]
    new_keys = new_keys.reshape(REQ, SPAN, local_width)
    new_values = new_values.reshape(REQ, SPAN, local_width)
    queries = queries.reshape(REQ, SPAN, local_width)
    scale = math.sqrt(HD)
    guest_queries = from_partner(queries[0], "group", 0)
    guest_visible = cache_pos < far_lengths[group_id ^ 1]
    guest_ctx = []
    guest_stats = []
    for head in range(heads_here):
        cols = slice(head * HD, (head + 1) * HD)
        s_guest = jnp.einsum(
            "cd,ld->cl", guest_queries[:, cols], far_keys[:, cols], preferred_element_type=jnp.float32
        ) / scale
        s_guest = jnp.where(guest_visible[None, :], s_guest, MASKED)
        guest_max = jnp.max(s_guest, axis=-1, keepdims=True)
        p_guest = jnp.where(guest_visible[None, :], jnp.exp(s_guest - guest_max), 0.0)
        guest_sum = jnp.sum(p_guest, axis=-1, keepdims=True)
        guest_ctx.append(
            jnp.einsum(
                "cl,ld->cd", p_guest.astype(jnp.bfloat16), far_values[:, cols], preferred_element_type=jnp.float32
            )
        )
        guest_stats.append(jnp.concatenate([guest_max, guest_sum], axis=-1))
    far_ctx_all = from_partner(jnp.concatenate(guest_ctx, axis=-1), "group", 0)
    far_stats = from_partner(jnp.stack(guest_stats, axis=1), "group", 0)
    head_outs = []
    for head in range(heads_here):
        cols = slice(head * HD, (head + 1) * HD)
        q = queries[:, :, cols]
        s_own = jnp.einsum("rcd,rld->rcl", q, own_keys[:, :, cols], preferred_element_type=jnp.float32) / scale
        s_new = jnp.einsum("rcd,rjd->rcj", q, new_keys[:, :, cols], preferred_element_type=jnp.float32) / scale
        s_own = jnp.where(own_visible[:, None, :], s_own, MASKED)
        s_new = jnp.where(causal[None], s_new, MASKED)
        far_max = far_stats[:, head, 0:1]
        far_sum = far_stats[:, head, 1:2]
        row_max = jnp.maximum(
            jnp.max(s_own, axis=-1, keepdims=True), jnp.max(s_new, axis=-1, keepdims=True)
        )
        row_max = jnp.where(is_first, jnp.maximum(row_max, far_max[None]), row_max)
        p_own = jnp.where(own_visible[:, None, :], jnp.exp(s_own - row_max), 0.0)
        p_new = jnp.where(causal[None], jnp.exp(s_new - row_max), 0.0)
        far_scale = jnp.exp(far_max - row_max[0])
        total = jnp.sum(p_own, axis=-1, keepdims=True) + jnp.sum(p_new, axis=-1, keepdims=True)
        total = jnp.where(is_first, total + (far_sum * far_scale)[None], total)
        w_own = (p_own / total).astype(jnp.bfloat16)
        w_new = (p_new / total).astype(jnp.bfloat16)
        ctx = jnp.einsum("rcl,rld->rcd", w_own, own_values[:, :, cols], preferred_element_type=jnp.float32)
        ctx = ctx + jnp.einsum("rcj,rjd->rcd", w_new, new_values[:, :, cols], preferred_element_type=jnp.float32)
        far_part = far_ctx_all[:, cols] * (far_scale / total[0])
        ctx = ctx + jnp.where(is_first, far_part[None], 0.0)
        head_outs.append(ctx.astype(jnp.bfloat16))
    context = jnp.concatenate(head_outs, axis=-1)
    token_context = lax.all_to_all(
        context, HEAD_AXES, split_axis=0, concat_axis=2, tiled=True
    ).reshape(SPAN, -1)
    attended = jnp.dot(token_context, full_out_weight, preferred_element_type=jnp.float32)
    residual = (as_float + attended).astype(jnp.bfloat16)
    moe_in = rms_norm(residual.astype(jnp.float32), feedforward_gain).astype(jnp.bfloat16)
    row_count = tokens.shape[0]
    n_chip = lax.axis_size(("group", "x"))
    capacity = row_count * TOP * 3 // (2 * EXPERTS)
    slots = EXPERTS * capacity
    flat_routes = routes.reshape(-1)
    onehot = (flat_routes[:, None] == jnp.arange(EXPERTS, dtype=jnp.int32)[None, :]).astype(
        jnp.int32
    )
    earlier = jnp.cumsum(onehot, axis=0) - onehot
    slot_index = jnp.sum(earlier * onehot, axis=1)
    position_of = (flat_routes * capacity + slot_index).reshape(row_count, TOP)
    lanes = 128
    bands = D // lanes
    hits = (
        position_of.reshape(-1)[:, None] == jnp.arange(slots, dtype=jnp.int32)[None, :]
    ).astype(jnp.bfloat16)
    owner_plus_one = (jnp.arange(row_count * TOP, dtype=jnp.int32) // TOP + 1).astype(jnp.bfloat16)
    owner = jnp.dot(owner_plus_one[None, :], hits, preferred_element_type=jnp.float32)[0]
    slot_token = jnp.where(owner > 0, owner - 1, row_count).astype(jnp.int32).reshape(
        EXPERTS, capacity
    )
    padded_in = jnp.concatenate([moe_in, jnp.zeros((1, D), moe_in.dtype)], axis=0)
    buffer = padded_in.reshape(row_count + 1, bands, lanes)[slot_token]

    def exchange(blocks):
        flat = blocks.reshape(n_chip, capacity * bands, lanes)
        moved = lax.all_to_all(flat, ("group", "x"), split_axis=0, concat_axis=0, tiled=True)
        return moved.reshape(n_chip, capacity, bands, lanes)

    incoming = exchange(buffer)
    gate_act = jnp.einsum("esjl,jlf->esf", incoming, gate_full.reshape(bands, lanes, -1), preferred_element_type=jnp.float32)
    up_act = jnp.einsum("esjl,jlf->esf", incoming, up_full.reshape(bands, lanes, -1), preferred_element_type=jnp.float32)
    hidden = (jax.nn.silu(gate_act) * up_act).astype(jnp.bfloat16)
    expert_rows = jnp.einsum(
        "esf,fjl->esjl", hidden, down_full.reshape(-1, bands, lanes), preferred_element_type=jnp.float32
    ).astype(jnp.bfloat16)
    returned = exchange(expert_rows)
    picked = returned.reshape(slots, bands, lanes)[position_of]
    moe_out = jnp.sum(
        route_weights[:, :, None, None] * picked.astype(jnp.float32), axis=1
    ).reshape(row_count, D)
    return (residual.astype(jnp.float32) + moe_out).astype(jnp.bfloat16)


def solution(mesh):
    n_group, n_expert = mesh.devices.shape
    chip_mesh = jax.sharding.Mesh(
        mesh.devices.reshape(n_group, n_expert // 2, 2), ("group", "x", "core")
    )
    everyone = ("group", "x", "core")
    return jax.shard_map(
        body,
        mesh=chip_mesh,
        in_specs=(
            P(everyone, None),
            P(),
            P(None, HEAD_AXES),
            P(None, HEAD_AXES),
            P(None, HEAD_AXES),
            P(HEAD_AXES),
            P(HEAD_AXES),
            P(HEAD_AXES, None),
            P("group", None, HEAD_AXES),
            P("group", None, HEAD_AXES),
            P("group", None, None),
            P("group", None),
            P("group", None),
            P(),
            P("group", None),
            P(),
            P(everyone, None),
            P(everyone, None),
            P(None, everyone),
            P(None, everyone),
            P(everyone, None),
        ),
        out_specs=P(everyone, None),
        check_vma=False,
    )
```

```python
import math

import jax
import jax.numpy as jnp
from jax import lax
from jax.sharding import PartitionSpec as P

D = 2048
HD = 128
EXPERTS = 64
TOP = 8
PAGE = 128
REQ = 8
SPAN = 64
MAXP = 12


EPSILON = 1e-05
MASKED = -1e30
HEAD_AXES = ("x", "core")


def from_partner(value, axis, bit):
    mask = 2**bit
    pairs = [(source, source ^ mask) for source in range(lax.axis_size(axis))]
    return lax.ppermute(value, axis, pairs)


def rms_norm(values, norm_gain):
    return (
        values * lax.rsqrt(jnp.mean(values * values, axis=-1, keepdims=True) + EPSILON) * norm_gain
    )


def rotate(values, position):
    half_width = values.shape[-1] // 2
    inverse_freq = 10000.0 ** (-2.0 * jnp.arange(half_width, dtype=jnp.float32) / values.shape[-1])
    angles = position[:, None] * inverse_freq[None, :]
    cosine = jnp.cos(angles)[:, None, :]
    sine_part = jnp.sin(angles)[:, None, :]
    first_part = values[..., :half_width]
    second = values[..., half_width:]
    return jnp.concatenate(
        [first_part * cosine - second * sine_part, second * cosine + first_part * sine_part],
        axis=-1,
    )


def masked_scores(queries, key_rows, allowed):
    scores = jnp.einsum(
        "chd,lhd->hcl", queries, key_rows, preferred_element_type=jnp.float32
    ) / math.sqrt(queries.shape[-1])
    return jnp.where(allowed[None], scores, MASKED)


def attend(queries, key_rows, value_rows, allowed):
    scores = masked_scores(queries, key_rows, allowed)
    row_max = jnp.max(scores, axis=-1, keepdims=True)
    raised = jnp.where(allowed[None], jnp.exp(scores - row_max), 0.0)
    weights = (raised / jnp.sum(raised, axis=-1, keepdims=True)).astype(jnp.bfloat16)
    return jnp.einsum("hcl,lhd->chd", weights, value_rows, preferred_element_type=jnp.float32)


def body(
    tokens,
    attention_gain,
    query_weight,
    key_weight,
    value_weight,
    query_gain,
    key_gain,
    out_weight,
    key_pages,
    value_pages,
    page_table,
    far_table,
    cached_lengths,
    far_lengths,
    visible_from,
    feedforward_gain,
    routes,
    route_weights,
    gate_weight,
    up_weight,
    down_weight,
):
    n_group = lax.axis_size("group")
    n_expert = lax.axis_size(HEAD_AXES)
    group_id = lax.axis_index("group")
    as_float = tokens.astype(jnp.float32)
    token_block = lax.all_gather(tokens, HEAD_AXES, axis=0, tiled=True)
    row_block = rms_norm(token_block.astype(jnp.float32), attention_gain).astype(jnp.bfloat16)
    swap = [(0, 1), (1, 0)]
    gate_full = jnp.concatenate([gate_weight, lax.ppermute(gate_weight, "core", swap)], axis=1)
    up_full = jnp.concatenate([up_weight, lax.ppermute(up_weight, "core", swap)], axis=1)
    down_full = jnp.concatenate([down_weight, lax.ppermute(down_weight, "core", swap)], axis=0)
    joined = jnp.concatenate(
        [
            jnp.dot(row_block, query_weight, preferred_element_type=jnp.float32),
            jnp.dot(row_block, key_weight, preferred_element_type=jnp.float32),
            jnp.dot(row_block, value_weight, preferred_element_type=jnp.float32),
        ],
        axis=1,
    )
    local_width = query_weight.shape[1]
    heads_here = local_width // HD
    query_raw = joined[:, :local_width]
    key_raw = joined[:, local_width : 2 * local_width]
    new_values = (
        joined[:, 2 * local_width :].astype(jnp.bfloat16).reshape(REQ, SPAN, heads_here, HD)
    )
    query_sums, key_sums = lax.psum(
        lax.psum(
            (jnp.sum(query_raw * query_raw, axis=1), jnp.sum(key_raw * key_raw, axis=1)), "core"
        ),
        "x",
    )
    full_width = local_width * n_expert
    query_normed = query_raw * lax.rsqrt(query_sums[:, None] / full_width + EPSILON) * query_gain
    key_normed = key_raw * lax.rsqrt(key_sums[:, None] / full_width + EPSILON) * key_gain
    lengths = cached_lengths[0]
    starts = visible_from[0]
    first_flag = (jnp.arange(REQ, dtype=jnp.int32) == 0).astype(jnp.int32)
    offsets = lengths + far_lengths[group_id] * first_flag
    position = (
        (offsets[:, None] + jnp.arange(SPAN, dtype=jnp.int32)[None, :])
        .reshape(-1)
        .astype(jnp.float32)
    )
    queries = (
        rotate(query_normed.reshape(-1, heads_here, HD), position)
        .astype(jnp.bfloat16)
        .reshape(REQ, SPAN, heads_here, HD)
    )
    new_keys = (
        rotate(key_normed.reshape(-1, heads_here, HD), position)
        .astype(jnp.bfloat16)
        .reshape(REQ, SPAN, heads_here, HD)
    )
    cache_slots = MAXP * PAGE
    pool_size = key_pages.shape[0]
    page_pick = (
        page_table[0][:, :, None] == jnp.arange(pool_size, dtype=jnp.int32)[None, None, :]
    ).astype(jnp.bfloat16)
    own_keys = jnp.einsum(
        "rpq,qsc->rpsc", page_pick, key_pages, preferred_element_type=jnp.float32
    ).astype(jnp.bfloat16)
    own_values = jnp.einsum(
        "rpq,qsc->rpsc", page_pick, value_pages, preferred_element_type=jnp.float32
    ).astype(jnp.bfloat16)
    own_values, out_weight = lax.optimization_barrier((own_values, out_weight))
    full_out_weight = lax.all_gather(out_weight, HEAD_AXES, axis=0, tiled=True)
    far_keys = key_pages[far_table[0]].reshape(cache_slots, local_width)
    far_values = value_pages[far_table[0]].reshape(cache_slots, local_width)
    cache_pos = jnp.arange(cache_slots, dtype=jnp.int32)
    own_visible = (
        (cache_pos[None, :] < lengths[:, None]) & (cache_pos[None, :] >= starts[:, None])
    ).reshape(REQ, 1, MAXP, PAGE)
    causal = jnp.arange(SPAN)[:, None] >= jnp.arange(SPAN)[None, :]
    is_first = (jnp.arange(REQ) == 0)[:, None, None]
    new_keys = new_keys.reshape(REQ, SPAN, local_width)
    new_values = new_values.reshape(REQ, SPAN, local_width)
    queries = queries.reshape(REQ, SPAN, local_width)
    scale = math.sqrt(HD)
    guest_queries = from_partner(queries[0], "group", 0)
    guest_visible = cache_pos < far_lengths[group_id ^ 1]
    guest_ctx = []
    guest_stats = []
    for head in range(heads_here):
        cols = slice(head * HD, (head + 1) * HD)
        s_guest = jnp.einsum(
            "cd,ld->cl", guest_queries[:, cols], far_keys[:, cols], preferred_element_type=jnp.float32
        ) / scale
        s_guest = jnp.where(guest_visible[None, :], s_guest, MASKED)
        guest_max = jnp.max(s_guest, axis=-1, keepdims=True)
        p_guest = jnp.where(guest_visible[None, :], jnp.exp(s_guest - guest_max), 0.0)
        guest_sum = jnp.sum(p_guest, axis=-1, keepdims=True)
        guest_ctx.append(
            jnp.einsum(
                "cl,ld->cd", p_guest.astype(jnp.bfloat16), far_values[:, cols], preferred_element_type=jnp.float32
            )
        )
        guest_stats.append(jnp.concatenate([guest_max, guest_sum], axis=-1))
    far_ctx_all = from_partner(jnp.concatenate(guest_ctx, axis=-1), "group", 0)
    far_stats = from_partner(jnp.stack(guest_stats, axis=1), "group", 0)
    head_outs = []
    for head in range(heads_here):
        cols = slice(head * HD, (head + 1) * HD)
        q = queries[:, :, cols]
        s_own = jnp.einsum("rcd,rpsd->rcps", q, own_keys[..., cols], preferred_element_type=jnp.float32) / scale
        s_new = jnp.einsum("rcd,rjd->rcj", q, new_keys[:, :, cols], preferred_element_type=jnp.float32) / scale
        s_own = jnp.where(own_visible, s_own, MASKED)
        s_new = jnp.where(causal[None], s_new, MASKED)
        far_max = far_stats[:, head, 0:1]
        far_sum = far_stats[:, head, 1:2]
        row_max = jnp.maximum(
            jnp.max(s_own, axis=(2, 3))[..., None], jnp.max(s_new, axis=-1, keepdims=True)
        )
        row_max = jnp.where(is_first, jnp.maximum(row_max, far_max[None]), row_max)
        p_own = jnp.where(own_visible, jnp.exp(s_own - row_max[..., None]), 0.0)
        p_new = jnp.where(causal[None], jnp.exp(s_new - row_max), 0.0)
        far_scale = jnp.exp(far_max - row_max[0])
        total = jnp.sum(p_own, axis=(2, 3))[..., None] + jnp.sum(p_new, axis=-1, keepdims=True)
        total = jnp.where(is_first, total + (far_sum * far_scale)[None], total)
        w_own = (p_own / total[..., None]).astype(jnp.bfloat16)
        w_new = (p_new / total).astype(jnp.bfloat16)
        ctx = jnp.einsum("rcps,rpsd->rcd", w_own, own_values[..., cols], preferred_element_type=jnp.float32)
        ctx = ctx + jnp.einsum("rcj,rjd->rcd", w_new, new_values[:, :, cols], preferred_element_type=jnp.float32)
        far_part = far_ctx_all[:, cols] * (far_scale / total[0])
        ctx = ctx + jnp.where(is_first, far_part[None], 0.0)
        head_outs.append(ctx.astype(jnp.bfloat16))
    context = jnp.concatenate(head_outs, axis=-1)
    token_context = lax.all_to_all(
        context, HEAD_AXES, split_axis=0, concat_axis=2, tiled=True
    ).reshape(SPAN, -1)
    attended = jnp.dot(token_context, full_out_weight, preferred_element_type=jnp.float32)
    residual = (as_float + attended).astype(jnp.bfloat16)
    moe_in = rms_norm(residual.astype(jnp.float32), feedforward_gain).astype(jnp.bfloat16)
    row_count = tokens.shape[0]
    n_chip = lax.axis_size(("group", "x"))
    capacity = row_count * TOP * 3 // (2 * EXPERTS)
    slots = EXPERTS * capacity
    flat_routes = routes.reshape(-1)
    onehot = (flat_routes[:, None] == jnp.arange(EXPERTS, dtype=jnp.int32)[None, :]).astype(
        jnp.int32
    )
    earlier = jnp.cumsum(onehot, axis=0) - onehot
    slot_index = jnp.sum(earlier * onehot, axis=1)
    position_of = (flat_routes * capacity + slot_index).reshape(row_count, TOP)
    lanes = 128
    bands = D // lanes
    hits = (
        position_of.reshape(-1)[:, None] == jnp.arange(slots, dtype=jnp.int32)[None, :]
    ).astype(jnp.bfloat16)
    owner_plus_one = (jnp.arange(row_count * TOP, dtype=jnp.int32) // TOP + 1).astype(jnp.bfloat16)
    owner = jnp.dot(owner_plus_one[None, :], hits, preferred_element_type=jnp.float32)[0]
    slot_token = jnp.where(owner > 0, owner - 1, row_count).astype(jnp.int32).reshape(
        EXPERTS, capacity
    )
    padded_in = jnp.concatenate([moe_in, jnp.zeros((1, D), moe_in.dtype)], axis=0)
    buffer = padded_in.reshape(row_count + 1, bands, lanes)[slot_token]

    def exchange(blocks):
        flat = blocks.reshape(n_chip, capacity * bands, lanes)
        moved = lax.all_to_all(flat, ("group", "x"), split_axis=0, concat_axis=0, tiled=True)
        return moved.reshape(n_chip, capacity, bands, lanes)

    incoming = exchange(buffer)
    gate_act = jnp.einsum("esjl,jlf->esf", incoming, gate_full.reshape(bands, lanes, -1), preferred_element_type=jnp.float32)
    up_act = jnp.einsum("esjl,jlf->esf", incoming, up_full.reshape(bands, lanes, -1), preferred_element_type=jnp.float32)
    hidden = (jax.nn.silu(gate_act) * up_act).astype(jnp.bfloat16)
    expert_rows = jnp.einsum(
        "esf,fjl->esjl", hidden, down_full.reshape(-1, bands, lanes), preferred_element_type=jnp.float32
    ).astype(jnp.bfloat16)
    returned = exchange(expert_rows)
    picked = returned.reshape(slots, bands, lanes)[position_of]
    moe_out = jnp.sum(
        route_weights[:, :, None, None] * picked.astype(jnp.float32), axis=1
    ).reshape(row_count, D)
    return (residual.astype(jnp.float32) + moe_out).astype(jnp.bfloat16)


def solution(mesh):
    n_group, n_expert = mesh.devices.shape
    chip_mesh = jax.sharding.Mesh(
        mesh.devices.reshape(n_group, n_expert // 2, 2), ("group", "x", "core")
    )
    everyone = ("group", "x", "core")
    return jax.shard_map(
        body,
        mesh=chip_mesh,
        in_specs=(
            P(everyone, None),
            P(),
            P(None, HEAD_AXES),
            P(None, HEAD_AXES),
            P(None, HEAD_AXES),
            P(HEAD_AXES),
            P(HEAD_AXES),
            P(HEAD_AXES, None),
            P("group", None, HEAD_AXES),
            P("group", None, HEAD_AXES),
            P("group", None, None),
            P("group", None),
            P("group", None),
            P(),
            P("group", None),
            P(),
            P(everyone, None),
            P(everyone, None),
            P(None, everyone),
            P(None, everyone),
            P(everyone, None),
        ),
        out_specs=P(everyone, None),
        check_vma=False,
    )
```

```python
import math

import jax
import jax.numpy as jnp
from jax import lax
from jax.sharding import PartitionSpec as P

D = 2048
HD = 128
EXPERTS = 64
TOP = 8
PAGE = 128
REQ = 8
SPAN = 64
MAXP = 12


EPSILON = 1e-05
MASKED = -1e30
HEAD_AXES = ("x", "core")


def from_partner(value, axis, bit):
    mask = 2**bit
    pairs = [(source, source ^ mask) for source in range(lax.axis_size(axis))]
    return lax.ppermute(value, axis, pairs)


def rms_norm(values, norm_gain):
    return (
        values * lax.rsqrt(jnp.mean(values * values, axis=-1, keepdims=True) + EPSILON) * norm_gain
    )


def rotate(values, position):
    half_width = values.shape[-1] // 2
    inverse_freq = 10000.0 ** (-2.0 * jnp.arange(half_width, dtype=jnp.float32) / values.shape[-1])
    angles = position[:, None] * inverse_freq[None, :]
    cosine = jnp.cos(angles)[:, None, :]
    sine_part = jnp.sin(angles)[:, None, :]
    first_part = values[..., :half_width]
    second = values[..., half_width:]
    return jnp.concatenate(
        [first_part * cosine - second * sine_part, second * cosine + first_part * sine_part],
        axis=-1,
    )


def masked_scores(queries, key_rows, allowed):
    scores = jnp.einsum(
        "chd,lhd->hcl", queries, key_rows, preferred_element_type=jnp.float32
    ) / math.sqrt(queries.shape[-1])
    return jnp.where(allowed[None], scores, MASKED)


def attend(queries, key_rows, value_rows, allowed):
    scores = masked_scores(queries, key_rows, allowed)
    row_max = jnp.max(scores, axis=-1, keepdims=True)
    raised = jnp.where(allowed[None], jnp.exp(scores - row_max), 0.0)
    weights = (raised / jnp.sum(raised, axis=-1, keepdims=True)).astype(jnp.bfloat16)
    return jnp.einsum("hcl,lhd->chd", weights, value_rows, preferred_element_type=jnp.float32)


def body(
    tokens,
    attention_gain,
    query_weight,
    key_weight,
    value_weight,
    query_gain,
    key_gain,
    out_weight,
    key_pages,
    value_pages,
    page_table,
    far_table,
    cached_lengths,
    far_lengths,
    visible_from,
    feedforward_gain,
    routes,
    route_weights,
    gate_weight,
    up_weight,
    down_weight,
):
    n_group = lax.axis_size("group")
    n_expert = lax.axis_size(HEAD_AXES)
    group_id = lax.axis_index("group")
    as_float = tokens.astype(jnp.float32)
    token_block = lax.all_gather(tokens, HEAD_AXES, axis=0, tiled=True)
    row_block = rms_norm(token_block.astype(jnp.float32), attention_gain).astype(jnp.bfloat16)
    swap = [(0, 1), (1, 0)]
    gate_other = lax.ppermute(gate_weight, "core", swap)
    up_other = lax.ppermute(up_weight, "core", swap)
    down_other = lax.ppermute(down_weight, "core", swap)
    joined = jnp.concatenate(
        [
            jnp.dot(row_block, query_weight, preferred_element_type=jnp.float32),
            jnp.dot(row_block, key_weight, preferred_element_type=jnp.float32),
            jnp.dot(row_block, value_weight, preferred_element_type=jnp.float32),
        ],
        axis=1,
    )
    local_width = query_weight.shape[1]
    heads_here = local_width // HD
    query_raw = joined[:, :local_width]
    key_raw = joined[:, local_width : 2 * local_width]
    new_values = (
        joined[:, 2 * local_width :].astype(jnp.bfloat16).reshape(REQ, SPAN, heads_here, HD)
    )
    query_sums, key_sums = lax.psum(
        lax.psum(
            (jnp.sum(query_raw * query_raw, axis=1), jnp.sum(key_raw * key_raw, axis=1)), "core"
        ),
        "x",
    )
    full_width = local_width * n_expert
    query_normed = query_raw * lax.rsqrt(query_sums[:, None] / full_width + EPSILON) * query_gain
    key_normed = key_raw * lax.rsqrt(key_sums[:, None] / full_width + EPSILON) * key_gain
    lengths = cached_lengths[0]
    starts = visible_from[0]
    first_flag = (jnp.arange(REQ, dtype=jnp.int32) == 0).astype(jnp.int32)
    offsets = lengths + far_lengths[group_id] * first_flag
    position = (
        (offsets[:, None] + jnp.arange(SPAN, dtype=jnp.int32)[None, :])
        .reshape(-1)
        .astype(jnp.float32)
    )
    queries = (
        rotate(query_normed.reshape(-1, heads_here, HD), position)
        .astype(jnp.bfloat16)
        .reshape(REQ, SPAN, heads_here, HD)
    )
    new_keys = (
        rotate(key_normed.reshape(-1, heads_here, HD), position)
        .astype(jnp.bfloat16)
        .reshape(REQ, SPAN, heads_here, HD)
    )
    cache_slots = MAXP * PAGE
    pool_size = key_pages.shape[0]
    page_pick = (
        page_table[0][:, :, None] == jnp.arange(pool_size, dtype=jnp.int32)[None, None, :]
    ).astype(jnp.bfloat16)
    own_keys = jnp.einsum(
        "rpq,qsc->rpsc", page_pick, key_pages, preferred_element_type=jnp.float32
    ).astype(jnp.bfloat16).reshape(REQ, cache_slots, local_width)
    own_values = jnp.einsum(
        "rpq,qsc->rpsc", page_pick, value_pages, preferred_element_type=jnp.float32
    ).astype(jnp.bfloat16).reshape(REQ, cache_slots, local_width)
    own_values, out_weight = lax.optimization_barrier((own_values, out_weight))
    full_out_weight = lax.all_gather(out_weight, HEAD_AXES, axis=0, tiled=True)
    far_keys = key_pages[far_table[0]].reshape(cache_slots, local_width)
    far_values = value_pages[far_table[0]].reshape(cache_slots, local_width)
    cache_pos = jnp.arange(cache_slots, dtype=jnp.int32)
    own_visible = (cache_pos[None, :] < lengths[:, None]) & (cache_pos[None, :] >= starts[:, None])
    causal = jnp.arange(SPAN)[:, None] >= jnp.arange(SPAN)[None, :]
    is_first = (jnp.arange(REQ) == 0)[:, None, None]
    new_keys = new_keys.reshape(REQ, SPAN, local_width)
    new_values = new_values.reshape(REQ, SPAN, local_width)
    queries = queries.reshape(REQ, SPAN, local_width)
    scale = math.sqrt(HD)
    guest_queries = from_partner(queries[0], "group", 0)
    guest_visible = cache_pos < far_lengths[group_id ^ 1]
    guest_ctx = []
    guest_stats = []
    for head in range(heads_here):
        cols = slice(head * HD, (head + 1) * HD)
        s_guest = jnp.einsum(
            "cd,ld->cl", guest_queries[:, cols], far_keys[:, cols], preferred_element_type=jnp.float32
        ) / scale
        s_guest = jnp.where(guest_visible[None, :], s_guest, MASKED)
        guest_max = jnp.max(s_guest, axis=-1, keepdims=True)
        p_guest = jnp.where(guest_visible[None, :], jnp.exp(s_guest - guest_max), 0.0)
        guest_sum = jnp.sum(p_guest, axis=-1, keepdims=True)
        guest_ctx.append(
            jnp.einsum(
                "cl,ld->cd", p_guest.astype(jnp.bfloat16), far_values[:, cols], preferred_element_type=jnp.float32
            )
        )
        guest_stats.append(jnp.concatenate([guest_max, guest_sum], axis=-1))
    far_ctx_all = from_partner(jnp.concatenate(guest_ctx, axis=-1), "group", 0)
    far_stats = from_partner(jnp.stack(guest_stats, axis=1), "group", 0)
    head_outs = []
    for head in range(heads_here):
        cols = slice(head * HD, (head + 1) * HD)
        q = queries[:, :, cols]
        s_own = jnp.einsum("rcd,rld->rcl", q, own_keys[:, :, cols], preferred_element_type=jnp.float32) / scale
        s_new = jnp.einsum("rcd,rjd->rcj", q, new_keys[:, :, cols], preferred_element_type=jnp.float32) / scale
        s_own = jnp.where(own_visible[:, None, :], s_own, MASKED)
        s_new = jnp.where(causal[None], s_new, MASKED)
        far_max = far_stats[:, head, 0:1]
        far_sum = far_stats[:, head, 1:2]
        row_max = jnp.maximum(
            jnp.max(s_own, axis=-1, keepdims=True), jnp.max(s_new, axis=-1, keepdims=True)
        )
        row_max = jnp.where(is_first, jnp.maximum(row_max, far_max[None]), row_max)
        p_own = jnp.where(own_visible[:, None, :], jnp.exp(s_own - row_max), 0.0)
        p_new = jnp.where(causal[None], jnp.exp(s_new - row_max), 0.0)
        far_scale = jnp.exp(far_max - row_max[0])
        total = jnp.sum(p_own, axis=-1, keepdims=True) + jnp.sum(p_new, axis=-1, keepdims=True)
        total = jnp.where(is_first, total + (far_sum * far_scale)[None], total)
        w_own = (p_own / total).astype(jnp.bfloat16)
        w_new = (p_new / total).astype(jnp.bfloat16)
        ctx = jnp.einsum("rcl,rld->rcd", w_own, own_values[:, :, cols], preferred_element_type=jnp.float32)
        ctx = ctx + jnp.einsum("rcj,rjd->rcd", w_new, new_values[:, :, cols], preferred_element_type=jnp.float32)
        far_part = far_ctx_all[:, cols] * (far_scale / total[0])
        ctx = ctx + jnp.where(is_first, far_part[None], 0.0)
        head_outs.append(ctx.astype(jnp.bfloat16))
    context = jnp.concatenate(head_outs, axis=-1)
    token_context = lax.all_to_all(
        context, HEAD_AXES, split_axis=0, concat_axis=2, tiled=True
    ).reshape(SPAN, -1)
    attended = jnp.dot(token_context, full_out_weight, preferred_element_type=jnp.float32)
    residual = (as_float + attended).astype(jnp.bfloat16)
    moe_in = rms_norm(residual.astype(jnp.float32), feedforward_gain).astype(jnp.bfloat16)
    row_count = tokens.shape[0]
    n_chip = lax.axis_size(("group", "x"))
    capacity = row_count * TOP * 3 // (2 * EXPERTS)
    slots = EXPERTS * capacity
    flat_routes = routes.reshape(-1)
    onehot = (flat_routes[:, None] == jnp.arange(EXPERTS, dtype=jnp.int32)[None, :]).astype(
        jnp.int32
    )
    earlier = jnp.cumsum(onehot, axis=0) - onehot
    slot_index = jnp.sum(earlier * onehot, axis=1)
    position_of = (flat_routes * capacity + slot_index).reshape(row_count, TOP)
    lanes = 128
    bands = D // lanes
    hits = (
        position_of.reshape(-1)[:, None] == jnp.arange(slots, dtype=jnp.int32)[None, :]
    ).astype(jnp.bfloat16)
    owner_plus_one = (jnp.arange(row_count * TOP, dtype=jnp.int32) // TOP + 1).astype(jnp.bfloat16)
    owner = jnp.dot(owner_plus_one[None, :], hits, preferred_element_type=jnp.float32)[0]
    slot_token = jnp.where(owner > 0, owner - 1, row_count).astype(jnp.int32).reshape(
        EXPERTS, capacity
    )
    padded_in = jnp.concatenate([moe_in, jnp.zeros((1, D), moe_in.dtype)], axis=0)
    buffer = padded_in.reshape(row_count + 1, bands, lanes)[slot_token]

    def exchange(blocks):
        flat = blocks.reshape(n_chip, capacity * bands, lanes)
        moved = lax.all_to_all(flat, ("group", "x"), split_axis=0, concat_axis=0, tiled=True)
        return moved.reshape(n_chip, capacity, bands, lanes)

    incoming = exchange(buffer)

    def expert_half(gate_part, up_part, down_part):
        gate_act = jnp.einsum(
            "esjl,jlf->esf", incoming, gate_part.reshape(bands, lanes, -1), preferred_element_type=jnp.float32
        )
        up_act = jnp.einsum(
            "esjl,jlf->esf", incoming, up_part.reshape(bands, lanes, -1), preferred_element_type=jnp.float32
        )
        hidden = (jax.nn.silu(gate_act) * up_act).astype(jnp.bfloat16)
        return jnp.einsum(
            "esf,fjl->esjl", hidden, down_part.reshape(-1, bands, lanes), preferred_element_type=jnp.float32
        )

    expert_rows = (
        expert_half(gate_weight, up_weight, down_weight)
        + expert_half(gate_other, up_other, down_other)
    ).astype(jnp.bfloat16)
    returned = exchange(expert_rows)
    picked = returned.reshape(slots, bands, lanes)[position_of]
    moe_out = jnp.sum(
        route_weights[:, :, None, None] * picked.astype(jnp.float32), axis=1
    ).reshape(row_count, D)
    return (residual.astype(jnp.float32) + moe_out).astype(jnp.bfloat16)


def solution(mesh):
    n_group, n_expert = mesh.devices.shape
    chip_mesh = jax.sharding.Mesh(
        mesh.devices.reshape(n_group, n_expert // 2, 2), ("group", "x", "core")
    )
    everyone = ("group", "x", "core")
    return jax.shard_map(
        body,
        mesh=chip_mesh,
        in_specs=(
            P(everyone, None),
            P(),
            P(None, HEAD_AXES),
            P(None, HEAD_AXES),
            P(None, HEAD_AXES),
            P(HEAD_AXES),
            P(HEAD_AXES),
            P(HEAD_AXES, None),
            P("group", None, HEAD_AXES),
            P("group", None, HEAD_AXES),
            P("group", None, None),
            P("group", None),
            P("group", None),
            P(),
            P("group", None),
            P(),
            P(everyone, None),
            P(everyone, None),
            P(None, everyone),
            P(None, everyone),
            P(everyone, None),
        ),
        out_specs=P(everyone, None),
        check_vma=False,
    )
```

```python
import math

import jax
import jax.numpy as jnp
from jax import lax
from jax.sharding import PartitionSpec as P

D = 2048
HD = 128
EXPERTS = 64
TOP = 8
PAGE = 128
REQ = 8
SPAN = 64
MAXP = 12


EPSILON = 1e-05
MASKED = -1e30
HEAD_AXES = ("x", "core")


def from_partner(value, axis, bit):
    mask = 2**bit
    pairs = [(source, source ^ mask) for source in range(lax.axis_size(axis))]
    return lax.ppermute(value, axis, pairs)


def rms_norm(values, norm_gain):
    return (
        values * lax.rsqrt(jnp.mean(values * values, axis=-1, keepdims=True) + EPSILON) * norm_gain
    )


def rotate(values, position):
    half_width = values.shape[-1] // 2
    inverse_freq = 10000.0 ** (-2.0 * jnp.arange(half_width, dtype=jnp.float32) / values.shape[-1])
    angles = position[:, None] * inverse_freq[None, :]
    cosine = jnp.cos(angles)[:, None, :]
    sine_part = jnp.sin(angles)[:, None, :]
    first_part = values[..., :half_width]
    second = values[..., half_width:]
    return jnp.concatenate(
        [first_part * cosine - second * sine_part, second * cosine + first_part * sine_part],
        axis=-1,
    )


def masked_scores(queries, key_rows, allowed):
    scores = jnp.einsum(
        "chd,lhd->hcl", queries, key_rows, preferred_element_type=jnp.float32
    ) / math.sqrt(queries.shape[-1])
    return jnp.where(allowed[None], scores, MASKED)


def attend(queries, key_rows, value_rows, allowed):
    scores = masked_scores(queries, key_rows, allowed)
    row_max = jnp.max(scores, axis=-1, keepdims=True)
    raised = jnp.where(allowed[None], jnp.exp(scores - row_max), 0.0)
    weights = (raised / jnp.sum(raised, axis=-1, keepdims=True)).astype(jnp.bfloat16)
    return jnp.einsum("hcl,lhd->chd", weights, value_rows, preferred_element_type=jnp.float32)


def body(
    tokens,
    attention_gain,
    query_weight,
    key_weight,
    value_weight,
    query_gain,
    key_gain,
    out_weight,
    key_pages,
    value_pages,
    page_table,
    far_table,
    cached_lengths,
    far_lengths,
    visible_from,
    feedforward_gain,
    routes,
    route_weights,
    gate_weight,
    up_weight,
    down_weight,
):
    n_group = lax.axis_size("group")
    n_expert = lax.axis_size(HEAD_AXES)
    group_id = lax.axis_index("group")
    as_float = tokens.astype(jnp.float32)
    token_block = lax.all_gather(tokens, HEAD_AXES, axis=0, tiled=True)
    row_block = rms_norm(token_block.astype(jnp.float32), attention_gain).astype(jnp.bfloat16)
    swap = [(0, 1), (1, 0)]
    gate_full = jnp.concatenate([gate_weight, lax.ppermute(gate_weight, "core", swap)], axis=1)
    up_full = jnp.concatenate([up_weight, lax.ppermute(up_weight, "core", swap)], axis=1)
    down_full = jnp.concatenate([down_weight, lax.ppermute(down_weight, "core", swap)], axis=0)
    joined = jnp.concatenate(
        [
            jnp.dot(row_block, query_weight, preferred_element_type=jnp.float32),
            jnp.dot(row_block, key_weight, preferred_element_type=jnp.float32),
            jnp.dot(row_block, value_weight, preferred_element_type=jnp.float32),
        ],
        axis=1,
    )
    local_width = query_weight.shape[1]
    heads_here = local_width // HD
    query_raw = joined[:, :local_width]
    key_raw = joined[:, local_width : 2 * local_width]
    new_values = (
        joined[:, 2 * local_width :].astype(jnp.bfloat16).reshape(REQ, SPAN, heads_here, HD)
    )
    query_sums, key_sums = lax.psum(
        lax.psum(
            (jnp.sum(query_raw * query_raw, axis=1), jnp.sum(key_raw * key_raw, axis=1)), "core"
        ),
        "x",
    )
    full_width = local_width * n_expert
    query_normed = query_raw * lax.rsqrt(query_sums[:, None] / full_width + EPSILON) * query_gain
    key_normed = key_raw * lax.rsqrt(key_sums[:, None] / full_width + EPSILON) * key_gain
    lengths = cached_lengths[0]
    starts = visible_from[0]
    first_flag = (jnp.arange(REQ, dtype=jnp.int32) == 0).astype(jnp.int32)
    offsets = lengths + far_lengths[group_id] * first_flag
    position = (
        (offsets[:, None] + jnp.arange(SPAN, dtype=jnp.int32)[None, :])
        .reshape(-1)
        .astype(jnp.float32)
    )
    queries = (
        rotate(query_normed.reshape(-1, heads_here, HD), position)
        .astype(jnp.bfloat16)
        .reshape(REQ, SPAN, heads_here, HD)
    )
    new_keys = (
        rotate(key_normed.reshape(-1, heads_here, HD), position)
        .astype(jnp.bfloat16)
        .reshape(REQ, SPAN, heads_here, HD)
    )
    cache_slots = MAXP * PAGE
    pool_size = key_pages.shape[0]
    page_pick = (
        page_table[0][:, :, None] == jnp.arange(pool_size, dtype=jnp.int32)[None, None, :]
    ).astype(jnp.bfloat16)
    own_keys = jnp.einsum(
        "rpq,qsc->rpsc", page_pick, key_pages, preferred_element_type=jnp.float32
    ).astype(jnp.bfloat16).reshape(REQ, cache_slots, local_width)
    own_values = jnp.einsum(
        "rpq,qsc->rpsc", page_pick, value_pages, preferred_element_type=jnp.float32
    ).astype(jnp.bfloat16).reshape(REQ, cache_slots, local_width)
    own_values, out_weight = lax.optimization_barrier((own_values, out_weight))
    full_out_weight = lax.all_gather(out_weight, HEAD_AXES, axis=0, tiled=True)
    far_keys = key_pages[far_table[0]].reshape(cache_slots, local_width)
    far_values = value_pages[far_table[0]].reshape(cache_slots, local_width)
    cache_pos = jnp.arange(cache_slots, dtype=jnp.int32)
    own_visible = (cache_pos[None, :] < lengths[:, None]) & (cache_pos[None, :] >= starts[:, None])
    causal = jnp.arange(SPAN)[:, None] >= jnp.arange(SPAN)[None, :]
    is_first = (jnp.arange(REQ) == 0)[:, None, None]
    new_keys = new_keys.reshape(REQ, SPAN, local_width)
    new_values = new_values.reshape(REQ, SPAN, local_width)
    queries = queries.reshape(REQ, SPAN, local_width)
    scale = math.sqrt(HD)
    guest_queries = from_partner(queries[0], "group", 0)
    guest_visible = cache_pos < far_lengths[group_id ^ 1]
    guest_ctx = []
    guest_stats = []
    for head in range(heads_here):
        cols = slice(head * HD, (head + 1) * HD)
        s_guest = jnp.einsum(
            "cd,ld->cl", guest_queries[:, cols], far_keys[:, cols], preferred_element_type=jnp.float32
        ) / scale
        s_guest = jnp.where(guest_visible[None, :], s_guest, MASKED)
        guest_max = jnp.max(s_guest, axis=-1, keepdims=True)
        p_guest = jnp.where(guest_visible[None, :], jnp.exp(s_guest - guest_max), 0.0)
        guest_sum = jnp.sum(p_guest, axis=-1, keepdims=True)
        guest_ctx.append(
            jnp.einsum(
                "cl,ld->cd", p_guest.astype(jnp.bfloat16), far_values[:, cols], preferred_element_type=jnp.float32
            )
        )
        guest_stats.append(jnp.concatenate([guest_max, guest_sum], axis=-1))
    far_ctx_all = from_partner(jnp.concatenate(guest_ctx, axis=-1), "group", 0)
    far_stats = from_partner(jnp.stack(guest_stats, axis=1), "group", 0)
    head_outs = []
    for head in range(heads_here):
        cols = slice(head * HD, (head + 1) * HD)
        q = queries[:, :, cols]
        s_own = jnp.einsum("rcd,rld->rcl", q, own_keys[:, :, cols], preferred_element_type=jnp.float32) / scale
        s_new = jnp.einsum("rcd,rjd->rcj", q, new_keys[:, :, cols], preferred_element_type=jnp.float32) / scale
        s_own = jnp.where(own_visible[:, None, :], s_own, MASKED)
        s_new = jnp.where(causal[None], s_new, MASKED)
        far_max = far_stats[:, head, 0:1]
        far_sum = far_stats[:, head, 1:2]
        row_max = jnp.maximum(
            jnp.max(s_own, axis=-1, keepdims=True), jnp.max(s_new, axis=-1, keepdims=True)
        )
        row_max = jnp.where(is_first, jnp.maximum(row_max, far_max[None]), row_max)
        p_own = jnp.where(own_visible[:, None, :], jnp.exp(s_own - row_max), 0.0)
        p_new = jnp.where(causal[None], jnp.exp(s_new - row_max), 0.0)
        far_scale = jnp.exp(far_max - row_max[0])
        total = jnp.sum(p_own, axis=-1, keepdims=True) + jnp.sum(p_new, axis=-1, keepdims=True)
        total = jnp.where(is_first, total + (far_sum * far_scale)[None], total)
        w_own = (p_own / total).astype(jnp.bfloat16)
        w_new = (p_new / total).astype(jnp.bfloat16)
        ctx = jnp.einsum("rcl,rld->rcd", w_own, own_values[:, :, cols], preferred_element_type=jnp.float32)
        ctx = ctx + jnp.einsum("rcj,rjd->rcd", w_new, new_values[:, :, cols], preferred_element_type=jnp.float32)
        far_part = far_ctx_all[:, cols] * (far_scale / total[0])
        ctx = ctx + jnp.where(is_first, far_part[None], 0.0)
        head_outs.append(ctx.astype(jnp.bfloat16))
    context = jnp.concatenate(head_outs, axis=-1)
    core = lax.axis_index("core")
    by_chip = lax.all_to_all(
        context.reshape(lax.axis_size("x"), 2, SPAN, local_width), "x", split_axis=0, concat_axis=0, tiled=True
    )
    mine = lax.dynamic_index_in_dim(by_chip, core, axis=1, keepdims=False)
    for_partner = lax.dynamic_index_in_dim(by_chip, 1 - core, axis=1, keepdims=False)
    theirs = lax.ppermute(for_partner, "core", [(0, 1), (1, 0)])
    first_core = jnp.where(core == 0, mine, theirs)
    second_core = jnp.where(core == 0, theirs, mine)
    token_context = (
        jnp.stack([first_core, second_core], axis=1)
        .transpose(2, 0, 1, 3)
        .reshape(SPAN, -1)
    )
    attended = jnp.dot(token_context, full_out_weight, preferred_element_type=jnp.float32)
    residual = (as_float + attended).astype(jnp.bfloat16)
    moe_in = rms_norm(residual.astype(jnp.float32), feedforward_gain).astype(jnp.bfloat16)
    row_count = tokens.shape[0]
    n_chip = lax.axis_size(("group", "x"))
    capacity = row_count * TOP * 3 // (2 * EXPERTS)
    slots = EXPERTS * capacity
    flat_routes = routes.reshape(-1)
    onehot = (flat_routes[:, None] == jnp.arange(EXPERTS, dtype=jnp.int32)[None, :]).astype(
        jnp.int32
    )
    earlier = jnp.cumsum(onehot, axis=0) - onehot
    slot_index = jnp.sum(earlier * onehot, axis=1)
    position_of = (flat_routes * capacity + slot_index).reshape(row_count, TOP)
    lanes = 128
    bands = D // lanes
    hits = (
        position_of.reshape(-1)[:, None] == jnp.arange(slots, dtype=jnp.int32)[None, :]
    ).astype(jnp.bfloat16)
    owner_plus_one = (jnp.arange(row_count * TOP, dtype=jnp.int32) // TOP + 1).astype(jnp.bfloat16)
    owner = jnp.dot(owner_plus_one[None, :], hits, preferred_element_type=jnp.float32)[0]
    slot_token = jnp.where(owner > 0, owner - 1, row_count).astype(jnp.int32).reshape(
        EXPERTS, capacity
    )
    padded_in = jnp.concatenate([moe_in, jnp.zeros((1, D), moe_in.dtype)], axis=0)
    buffer = padded_in.reshape(row_count + 1, bands, lanes)[slot_token]

    def exchange(blocks):
        flat = blocks.reshape(n_chip, capacity * bands, lanes)
        moved = lax.all_to_all(flat, ("group", "x"), split_axis=0, concat_axis=0, tiled=True)
        return moved.reshape(n_chip, capacity, bands, lanes)

    incoming = exchange(buffer)
    gate_act = jnp.einsum("esjl,jlf->esf", incoming, gate_full.reshape(bands, lanes, -1), preferred_element_type=jnp.float32)
    up_act = jnp.einsum("esjl,jlf->esf", incoming, up_full.reshape(bands, lanes, -1), preferred_element_type=jnp.float32)
    hidden = (jax.nn.silu(gate_act) * up_act).astype(jnp.bfloat16)
    expert_rows = jnp.einsum(
        "esf,fjl->esjl", hidden, down_full.reshape(-1, bands, lanes), preferred_element_type=jnp.float32
    ).astype(jnp.bfloat16)
    returned = exchange(expert_rows)
    picked = returned.reshape(slots, bands, lanes)[position_of]
    moe_out = jnp.sum(
        route_weights[:, :, None, None] * picked.astype(jnp.float32), axis=1
    ).reshape(row_count, D)
    return (residual.astype(jnp.float32) + moe_out).astype(jnp.bfloat16)


def solution(mesh):
    n_group, n_expert = mesh.devices.shape
    chip_mesh = jax.sharding.Mesh(
        mesh.devices.reshape(n_group, n_expert // 2, 2), ("group", "x", "core")
    )
    everyone = ("group", "x", "core")
    return jax.shard_map(
        body,
        mesh=chip_mesh,
        in_specs=(
            P(everyone, None),
            P(),
            P(None, HEAD_AXES),
            P(None, HEAD_AXES),
            P(None, HEAD_AXES),
            P(HEAD_AXES),
            P(HEAD_AXES),
            P(HEAD_AXES, None),
            P("group", None, HEAD_AXES),
            P("group", None, HEAD_AXES),
            P("group", None, None),
            P("group", None),
            P("group", None),
            P(),
            P("group", None),
            P(),
            P(everyone, None),
            P(everyone, None),
            P(None, everyone),
            P(None, everyone),
            P(everyone, None),
        ),
        out_specs=P(everyone, None),
        check_vma=False,
    )
```

```python
import math

import jax
import jax.numpy as jnp
from jax import lax
from jax.sharding import PartitionSpec as P

D = 2048
HD = 128
EXPERTS = 64
TOP = 8
PAGE = 128
REQ = 8
SPAN = 64
MAXP = 12


EPSILON = 1e-05
MASKED = -1e30
HEAD_AXES = ("x", "core")


def from_partner(value, axis, bit):
    mask = 2**bit
    pairs = [(source, source ^ mask) for source in range(lax.axis_size(axis))]
    return lax.ppermute(value, axis, pairs)


def rms_norm(values, norm_gain):
    return (
        values * lax.rsqrt(jnp.mean(values * values, axis=-1, keepdims=True) + EPSILON) * norm_gain
    )


def rotate(values, position):
    half_width = values.shape[-1] // 2
    inverse_freq = 10000.0 ** (-2.0 * jnp.arange(half_width, dtype=jnp.float32) / values.shape[-1])
    angles = position[:, None] * inverse_freq[None, :]
    cosine = jnp.cos(angles)[:, None, :]
    sine_part = jnp.sin(angles)[:, None, :]
    first_part = values[..., :half_width]
    second = values[..., half_width:]
    return jnp.concatenate(
        [first_part * cosine - second * sine_part, second * cosine + first_part * sine_part],
        axis=-1,
    )


def masked_scores(queries, key_rows, allowed):
    scores = jnp.einsum(
        "chd,lhd->hcl", queries, key_rows, preferred_element_type=jnp.float32
    ) / math.sqrt(queries.shape[-1])
    return jnp.where(allowed[None], scores, MASKED)


def attend(queries, key_rows, value_rows, allowed):
    scores = masked_scores(queries, key_rows, allowed)
    row_max = jnp.max(scores, axis=-1, keepdims=True)
    raised = jnp.where(allowed[None], jnp.exp(scores - row_max), 0.0)
    weights = (raised / jnp.sum(raised, axis=-1, keepdims=True)).astype(jnp.bfloat16)
    return jnp.einsum("hcl,lhd->chd", weights, value_rows, preferred_element_type=jnp.float32)


def body(
    tokens,
    attention_gain,
    query_weight,
    key_weight,
    value_weight,
    query_gain,
    key_gain,
    out_weight,
    key_pages,
    value_pages,
    page_table,
    far_table,
    cached_lengths,
    far_lengths,
    visible_from,
    feedforward_gain,
    routes,
    route_weights,
    gate_weight,
    up_weight,
    down_weight,
):
    n_group = lax.axis_size("group")
    n_expert = lax.axis_size(HEAD_AXES)
    group_id = lax.axis_index("group")
    as_float = tokens.astype(jnp.float32)
    token_block = lax.all_gather(tokens, HEAD_AXES, axis=0, tiled=True)
    row_block = rms_norm(token_block.astype(jnp.float32), attention_gain).astype(jnp.bfloat16)
    swap = [(0, 1), (1, 0)]
    gate_full = jnp.concatenate([gate_weight, lax.ppermute(gate_weight, "core", swap)], axis=1)
    up_full = jnp.concatenate([up_weight, lax.ppermute(up_weight, "core", swap)], axis=1)
    down_full = jnp.concatenate([down_weight, lax.ppermute(down_weight, "core", swap)], axis=0)
    joined = jnp.concatenate(
        [
            jnp.dot(row_block, query_weight, preferred_element_type=jnp.float32),
            jnp.dot(row_block, key_weight, preferred_element_type=jnp.float32),
            jnp.dot(row_block, value_weight, preferred_element_type=jnp.float32),
        ],
        axis=1,
    )
    local_width = query_weight.shape[1]
    heads_here = local_width // HD
    query_raw = joined[:, :local_width]
    key_raw = joined[:, local_width : 2 * local_width]
    new_values = (
        joined[:, 2 * local_width :].astype(jnp.bfloat16).reshape(REQ, SPAN, heads_here, HD)
    )
    query_sums, key_sums = lax.psum(
        lax.psum(
            (jnp.sum(query_raw * query_raw, axis=1), jnp.sum(key_raw * key_raw, axis=1)), "core"
        ),
        "x",
    )
    full_width = local_width * n_expert
    query_normed = query_raw * lax.rsqrt(query_sums[:, None] / full_width + EPSILON) * query_gain
    key_normed = key_raw * lax.rsqrt(key_sums[:, None] / full_width + EPSILON) * key_gain
    lengths = cached_lengths[0]
    starts = visible_from[0]
    first_flag = (jnp.arange(REQ, dtype=jnp.int32) == 0).astype(jnp.int32)
    offsets = lengths + far_lengths[group_id] * first_flag
    position = (
        (offsets[:, None] + jnp.arange(SPAN, dtype=jnp.int32)[None, :])
        .reshape(-1)
        .astype(jnp.float32)
    )
    queries = (
        rotate(query_normed.reshape(-1, heads_here, HD), position)
        .astype(jnp.bfloat16)
        .reshape(REQ, SPAN, heads_here, HD)
    )
    new_keys = (
        rotate(key_normed.reshape(-1, heads_here, HD), position)
        .astype(jnp.bfloat16)
        .reshape(REQ, SPAN, heads_here, HD)
    )
    cache_slots = MAXP * PAGE
    pool_size = key_pages.shape[0]
    page_pick = (
        page_table[0][:, :, None] == jnp.arange(pool_size, dtype=jnp.int32)[None, None, :]
    ).astype(jnp.bfloat16)
    own_keys = jnp.einsum(
        "rpq,qsc->rpsc", page_pick, key_pages, preferred_element_type=jnp.float32
    ).astype(jnp.bfloat16).reshape(REQ, cache_slots, local_width)
    own_values = jnp.einsum(
        "rpq,qsc->rpsc", page_pick, value_pages, preferred_element_type=jnp.float32
    ).astype(jnp.bfloat16).reshape(REQ, cache_slots, local_width)
    full_out_weight = lax.all_gather(out_weight, HEAD_AXES, axis=0, tiled=True)
    far_keys = key_pages[far_table[0]].reshape(cache_slots, local_width)
    far_values = value_pages[far_table[0]].reshape(cache_slots, local_width)
    cache_pos = jnp.arange(cache_slots, dtype=jnp.int32)
    own_visible = (cache_pos[None, :] < lengths[:, None]) & (cache_pos[None, :] >= starts[:, None])
    causal = jnp.arange(SPAN)[:, None] >= jnp.arange(SPAN)[None, :]
    is_first = (jnp.arange(REQ) == 0)[:, None, None]
    new_keys = new_keys.reshape(REQ, SPAN, local_width)
    new_values = new_values.reshape(REQ, SPAN, local_width)
    queries = queries.reshape(REQ, SPAN, local_width)
    scale = math.sqrt(HD)
    guest_queries = from_partner(queries[0], "group", 0)
    guest_visible = cache_pos < far_lengths[group_id ^ 1]
    guest_ctx = []
    guest_stats = []
    for head in range(heads_here):
        cols = slice(head * HD, (head + 1) * HD)
        s_guest = jnp.einsum(
            "cd,ld->cl", guest_queries[:, cols], far_keys[:, cols], preferred_element_type=jnp.float32
        ) / scale
        s_guest = jnp.where(guest_visible[None, :], s_guest, MASKED)
        guest_max = jnp.max(s_guest, axis=-1, keepdims=True)
        p_guest = jnp.where(guest_visible[None, :], jnp.exp(s_guest - guest_max), 0.0)
        guest_sum = jnp.sum(p_guest, axis=-1, keepdims=True)
        guest_ctx.append(
            jnp.einsum(
                "cl,ld->cd", p_guest.astype(jnp.bfloat16), far_values[:, cols], preferred_element_type=jnp.float32
            )
        )
        guest_stats.append(jnp.concatenate([guest_max, guest_sum], axis=-1))
    far_ctx_all = from_partner(jnp.concatenate(guest_ctx, axis=-1), "group", 0)
    far_stats = from_partner(jnp.stack(guest_stats, axis=1), "group", 0)
    head_outs = []
    for head in range(heads_here):
        cols = slice(head * HD, (head + 1) * HD)
        q = queries[:, :, cols]
        s_own = jnp.einsum("rcd,rld->rcl", q, own_keys[:, :, cols], preferred_element_type=jnp.float32) / scale
        s_new = jnp.einsum("rcd,rjd->rcj", q, new_keys[:, :, cols], preferred_element_type=jnp.float32) / scale
        s_own = jnp.where(own_visible[:, None, :], s_own, MASKED)
        s_new = jnp.where(causal[None], s_new, MASKED)
        far_max = far_stats[:, head, 0:1]
        far_sum = far_stats[:, head, 1:2]
        row_max = jnp.maximum(
            jnp.max(s_own, axis=-1, keepdims=True), jnp.max(s_new, axis=-1, keepdims=True)
        )
        row_max = jnp.where(is_first, jnp.maximum(row_max, far_max[None]), row_max)
        p_own = jnp.where(own_visible[:, None, :], jnp.exp(s_own - row_max), 0.0)
        p_new = jnp.where(causal[None], jnp.exp(s_new - row_max), 0.0)
        far_scale = jnp.exp(far_max - row_max[0])
        total = jnp.sum(p_own, axis=-1, keepdims=True) + jnp.sum(p_new, axis=-1, keepdims=True)
        total = jnp.where(is_first, total + (far_sum * far_scale)[None], total)
        w_own = (p_own / total).astype(jnp.bfloat16)
        w_new = (p_new / total).astype(jnp.bfloat16)
        ctx = jnp.einsum("rcl,rld->rcd", w_own, own_values[:, :, cols], preferred_element_type=jnp.float32)
        ctx = ctx + jnp.einsum("rcj,rjd->rcd", w_new, new_values[:, :, cols], preferred_element_type=jnp.float32)
        far_part = far_ctx_all[:, cols] * (far_scale / total[0])
        ctx = ctx + jnp.where(is_first, far_part[None], 0.0)
        head_outs.append(ctx.astype(jnp.bfloat16))
    context = jnp.concatenate(head_outs, axis=-1)
    token_context = lax.all_to_all(
        context, HEAD_AXES, split_axis=0, concat_axis=2, tiled=True
    ).reshape(SPAN, -1)
    attended = jnp.dot(token_context, full_out_weight, preferred_element_type=jnp.float32)
    residual = (as_float + attended).astype(jnp.bfloat16)
    moe_in = rms_norm(residual.astype(jnp.float32), feedforward_gain).astype(jnp.bfloat16)
    row_count = tokens.shape[0]
    n_chip = lax.axis_size(("group", "x"))
    capacity = row_count * TOP * 3 // (2 * EXPERTS)
    slots = EXPERTS * capacity
    flat_routes = routes.reshape(-1)
    onehot = (flat_routes[:, None] == jnp.arange(EXPERTS, dtype=jnp.int32)[None, :]).astype(
        jnp.int32
    )
    earlier = jnp.cumsum(onehot, axis=0) - onehot
    slot_index = jnp.sum(earlier * onehot, axis=1)
    position_of = (flat_routes * capacity + slot_index).reshape(row_count, TOP)
    lanes = 128
    bands = D // lanes
    hits = (
        position_of.reshape(-1)[:, None] == jnp.arange(slots, dtype=jnp.int32)[None, :]
    ).astype(jnp.bfloat16)
    owner_plus_one = (jnp.arange(row_count * TOP, dtype=jnp.int32) // TOP + 1).astype(jnp.bfloat16)
    owner = jnp.dot(owner_plus_one[None, :], hits, preferred_element_type=jnp.float32)[0]
    slot_token = jnp.where(owner > 0, owner - 1, row_count).astype(jnp.int32).reshape(
        EXPERTS, capacity
    )
    padded_in = jnp.concatenate([moe_in, jnp.zeros((1, D), moe_in.dtype)], axis=0)
    buffer = padded_in.reshape(row_count + 1, bands, lanes)[slot_token]

    def exchange(blocks):
        flat = blocks.reshape(n_chip, capacity * bands, lanes)
        moved = lax.all_to_all(flat, ("group", "x"), split_axis=0, concat_axis=0, tiled=True)
        return moved.reshape(n_chip, capacity, bands, lanes)

    incoming = exchange(buffer)
    gate_act = jnp.einsum("esjl,jlf->esf", incoming, gate_full.reshape(bands, lanes, -1), preferred_element_type=jnp.float32)
    up_act = jnp.einsum("esjl,jlf->esf", incoming, up_full.reshape(bands, lanes, -1), preferred_element_type=jnp.float32)
    hidden = (jax.nn.silu(gate_act) * up_act).astype(jnp.bfloat16)
    expert_rows = jnp.einsum(
        "esf,fjl->esjl", hidden, down_full.reshape(-1, bands, lanes), preferred_element_type=jnp.float32
    ).astype(jnp.bfloat16)
    returned = exchange(expert_rows)
    picked = returned.reshape(slots, bands, lanes)[position_of]
    moe_out = jnp.sum(
        route_weights[:, :, None, None] * picked.astype(jnp.float32), axis=1
    ).reshape(row_count, D)
    return (residual.astype(jnp.float32) + moe_out).astype(jnp.bfloat16)


def solution(mesh):
    n_group, n_expert = mesh.devices.shape
    chip_mesh = jax.sharding.Mesh(
        mesh.devices.reshape(n_group, n_expert // 2, 2), ("group", "x", "core")
    )
    everyone = ("group", "x", "core")
    return jax.shard_map(
        body,
        mesh=chip_mesh,
        in_specs=(
            P(everyone, None),
            P(),
            P(None, HEAD_AXES),
            P(None, HEAD_AXES),
            P(None, HEAD_AXES),
            P(HEAD_AXES),
            P(HEAD_AXES),
            P(HEAD_AXES, None),
            P("group", None, HEAD_AXES),
            P("group", None, HEAD_AXES),
            P("group", None, None),
            P("group", None),
            P("group", None),
            P(),
            P("group", None),
            P(),
            P(everyone, None),
            P(everyone, None),
            P(None, everyone),
            P(None, everyone),
            P(everyone, None),
        ),
        out_specs=P(everyone, None),
        check_vma=False,
    )
```
